128 devices in a mesh: req: 8 (over y, core), hid: 16 (over x, z).
Axes of the slice: x: 4, y: 4, z: 4, core: 2. Of those that a mesh axis runs over, the one named last changes fastest.
Arguments:
- tokens: bfloat16 [24576, 1536], P(('req', 'hid')), may hold values from -6 to 6
- segment: int32 [24576], P(('req', 'hid')), may hold values from 0 to 35, as said below
- attn_gain: float32 [1536], replicated, may hold values from 0.1 to 1.9
- w_query: bfloat16 [1536, 1536], replicated, may hold values from -0.2 to 0.2
- w_key: bfloat16 [1536, 512], replicated, may hold values from -0.2 to 0.2
- w_value: bfloat16 [1536, 512], replicated, may hold values from -0.15625 to 0.15625
- q_gain: float32 [64], replicated, may hold values from 0.5 to 6
- k_gain: float32 [64], replicated, may hold values from 0.5 to 6
- w_out: bfloat16 [1536, 1536], replicated, may hold values from -0.15625 to 0.15625
- ffn_gain: float32 [1536], replicated, may hold values from 0.1 to 1.9
- w_gate: bfloat16 [4608, 1536], P(('req', 'hid')), may hold values from -0.15625 to 0.15625
- w_up: bfloat16 [4608, 1536], P(('req', 'hid')), may hold values from -0.15625 to 0.15625
- w_down: bfloat16 [4608, 1536], P(('req', 'hid')), may hold values from -0.09375 to 0.09375
Outputs:
- mixed: bfloat16 [24576, 1536], P(('req', 'hid'))
- kv_cache: bfloat16 [24576, 1024], P(('req', 'hid'))
The draws below stay inside these ranges and needn't reach their ends.
Inputs may be any that keep to these rules, and one draw needn't show every extreme that they name: Segment ids never fall along the tokens and start at 0. A segment never crosses a boundary between aligned blocks of 3072 tokens; the first block is one segment of exactly 3072 tokens, and every later block holds exactly five segments.
All inputs are finite; a program needn't handle non-finite values.
Results may differ from the reference program's by a relative error of at most 0.015.
Values may be sent and summed in bfloat16 or wider, within the bound.
No kernel may reach another device: no remote copies, remote signals or barrier semaphores. Data moves between devices by JAX's collectives and lax.ppermute only.
A program may use at most 128 MiB of HBM per device.

```python
import jax
import jax.numpy as jnp
from jax import lax

D = 1536
H = 24
KVH = 8
HD = 64
FF = 4608
GROUP_TOK = 3072
TOKENS = 24576
N_REQ = 8


def block_starts(block_key, block_pos):
    picks = jax.random.permutation(block_key, GROUP_TOK - 1)[:4].astype(jnp.int32) + 1
    hits = jnp.any(block_pos[:, None] == picks[None, :], axis=1)
    return hits | (block_pos == 0)


def draw_segment(key, part):
    block_count = TOKENS // GROUP_TOK
    block_pos = jnp.arange(GROUP_TOK, dtype=jnp.int32)
    block_keys = jax.random.split(jax.random.fold_in(key, 5), block_count)
    flags = jax.vmap(lambda k: block_starts(k, block_pos))(block_keys)
    first_row = (block_pos == 0)[None, :]
    block_idx = jnp.arange(block_count, dtype=jnp.int32)[:, None]
    flags = jnp.where(block_idx == 0, first_row, flags).reshape(TOKENS)
    return (jnp.cumsum(flags.astype(jnp.int32)) - 1).astype(jnp.int32)


def draw_tokens(key, part):
    noise_key = jax.random.fold_in(jax.random.fold_in(key, 11), 0)
    base = jax.random.normal(noise_key, (TOKENS, D), jnp.float32)
    return jnp.clip(base, -6.0, 6.0).astype(jnp.bfloat16)


def draw_w_query(key, part):
    own = jax.random.normal(jax.random.fold_in(key, 1), (D, H * HD), jnp.float32) * D ** (-0.5)
    return jnp.clip(own, -0.199, 0.199).astype(jnp.bfloat16)


def draw_w_key(key, part):
    own = jax.random.normal(jax.random.fold_in(key, 2), (D, KVH * HD), jnp.float32) * D ** (-0.5)
    return jnp.clip(own, -0.199, 0.199).astype(jnp.bfloat16)


def draw_q_gain(key, part):
    return jnp.exp(jax.random.uniform(jax.random.fold_in(key, 21), (HD,), jnp.float32, -0.693, 0.693))


def draw_k_gain(key, part):
    return jnp.exp(jax.random.uniform(jax.random.fold_in(key, 22), (HD,), jnp.float32, -0.693, 0.693))


def block_scale(own_key, shape, cuts, low, largest):
    level, own = 1.0, jax.random.fold_in(own_key, 6)
    for dim, shards_of in cuts:
        draws = jnp.exp(jax.random.uniform(jax.random.fold_in(own, dim), (shards_of,), jnp.float32, low / len(cuts), largest / len(cuts)))
        level = level * jnp.repeat(draws, shape[dim] // shards_of).reshape([-1 if axis == dim else 1 for axis in range(len(shape))])
    return level


def bell_draw(key, extent, scale, reach, shards=(), held_as=jnp.bfloat16):
    result = jax.random.normal(key, extent, jnp.float32) * scale
    if len(shards) > 0:
        result = block_scale(key, extent, shards, -0.22, 0.18) * result
    return jnp.clip(result, min=-reach, max=reach).astype(held_as)


def setup_inputs(seed: int = 0) -> dict:
    streams_of = jax.random.split(jax.random.key(seed), 14)
    tokens = draw_tokens(jax.random.fold_in(streams_of[13], 71), 0)
    segment = draw_segment(jax.random.fold_in(streams_of[13], 71), 0)
    attn_gain = jnp.clip(1.0 + 0.18 * jax.random.normal(streams_of[2], (D,), jnp.float32), 0.1, 1.9)
    w_query = draw_w_query(jax.random.fold_in(streams_of[13], 71), 0)
    w_key = draw_w_key(jax.random.fold_in(streams_of[13], 71), 0)
    w_value = bell_draw(streams_of[5], (D, KVH * HD), D ** -0.5, 0.15625)
    q_gain = draw_q_gain(jax.random.fold_in(streams_of[13], 71), 0)
    k_gain = draw_k_gain(jax.random.fold_in(streams_of[13], 71), 0)
    w_out = bell_draw(streams_of[8], (H * HD, D), (H * HD) ** -0.5, 0.15625)
    ffn_gain = jnp.clip(1.0 + 0.18 * jax.random.normal(streams_of[9], (D,), jnp.float32), 0.1, 1.9)
    w_gate = bell_draw(streams_of[10], (FF, D), D ** -0.5, 0.15625, ((0, 128),))
    w_up = bell_draw(streams_of[11], (FF, D), D ** -0.5, 0.15625, ((0, 128),))
    w_down = bell_draw(streams_of[12], (FF, D), FF ** -0.5, 0.09375, ((0, 128),))
    return dict(tokens=tokens, segment=segment, attn_gain=attn_gain, w_query=w_query, w_key=w_key, w_value=w_value, q_gain=q_gain, k_gain=k_gain, w_out=w_out, ffn_gain=ffn_gain, w_gate=w_gate, w_up=w_up, w_down=w_down)


EPSILON = 1e-05
ROPE_BASE = 1000000.0
NEG_FILL = -1e+30

def rms_scale(values, gain):
    mean_sq = lax.optimization_barrier(jnp.mean(values * values, axis=-1, keepdims=True))
    return values * lax.rsqrt(mean_sq + EPSILON) * gain

def seg_positions(seg_ids):
    indices = jnp.arange(seg_ids.shape[0], dtype=jnp.int32)
    is_first = jnp.concatenate([jnp.ones((1,), bool), seg_ids[1:] != seg_ids[:-1]])
    seg_begin = lax.cummax(jnp.where(is_first, indices, jnp.zeros_like(indices)), axis=0)
    return indices - seg_begin

def rotate(heads, positions):
    half_dim = heads.shape[-1] // 2
    inv_freq = ROPE_BASE ** (-(jnp.arange(half_dim, dtype=jnp.float32) * 2.0) / (2.0 * half_dim))
    angles = positions.astype(jnp.float32)[:, None] * inv_freq[None, :]
    cos_val = jnp.cos(angles)[:, None, :]
    sin_val = jnp.sin(angles)[:, None, :]
    left = heads[..., :half_dim]
    right = heads[..., half_dim:]
    return jnp.concatenate([left * cos_val - right * sin_val, right * cos_val + left * sin_val], axis=-1)

def attend_group(args):
    queries, key_heads, values, seg_ids = args
    count_rows = seg_ids.shape[0]
    groups = H // KVH
    indices = jnp.arange(count_rows, dtype=jnp.int32)
    allowed = (indices[None, :] <= indices[:, None]) & (seg_ids[None, :] == seg_ids[:, None])
    q_grid = queries.reshape(count_rows, KVH, groups, HD).transpose(1, 2, 0, 3)
    k_grid = key_heads.reshape(count_rows, KVH, HD).transpose(1, 0, 2)
    v_grid = values.reshape(count_rows, KVH, HD).transpose(1, 0, 2)

    def one_head(head_args):
        q_head, k_head, v_head = head_args
        scores = jnp.einsum('gqd,cd->gqc', q_head.astype(jnp.float32), k_head.astype(jnp.float32)) * 0.125
        scores = jnp.where(allowed[None], scores, NEG_FILL)
        peak = lax.optimization_barrier(jnp.max(scores, axis=-1, keepdims=True))
        weights = jnp.where(allowed[None], jnp.exp(scores - peak), 0.0)
        weight_sum = lax.optimization_barrier(jnp.sum(weights, axis=-1, keepdims=True))
        probs = lax.optimization_barrier(weights.astype(jnp.bfloat16)).astype(jnp.float32)
        return jnp.einsum('gqc,cd->gqd', probs, v_head.astype(jnp.float32)) / weight_sum
    out_heads = lax.map(one_head, (q_grid, k_grid, v_grid))
    return out_heads.transpose(2, 0, 1, 3).reshape(count_rows, H * HD).astype(jnp.bfloat16)

def reference(tokens, segment, attn_gain, w_query, w_key, w_value, q_gain, k_gain, w_out, ffn_gain, w_gate, w_up, w_down):
    count_rows = tokens.shape[0]
    positions = seg_positions(segment)
    resid = tokens.astype(jnp.float32)
    normed = rms_scale(resid, attn_gain).astype(jnp.bfloat16)
    q_raw = jnp.dot(normed, w_query, preferred_element_type=jnp.float32).reshape(count_rows, H, HD)
    k_raw = jnp.dot(normed, w_key, preferred_element_type=jnp.float32).reshape(count_rows, KVH, HD)
    queries = rotate(rms_scale(q_raw, q_gain), positions).astype(jnp.bfloat16)
    key_heads = rotate(rms_scale(k_raw, k_gain), positions).astype(jnp.bfloat16).reshape(count_rows, KVH * HD)
    values = jnp.dot(normed, w_value, preferred_element_type=jnp.float32).astype(jnp.bfloat16)
    kv_cache = jnp.concatenate([key_heads, values], axis=1)
    attended = lax.map(attend_group, (queries.reshape(N_REQ, GROUP_TOK, H, HD), key_heads.reshape(N_REQ, GROUP_TOK, KVH * HD), values.reshape(N_REQ, GROUP_TOK, KVH * HD), segment.reshape(N_REQ, GROUP_TOK)))
    attended = attended.reshape(count_rows, H * HD)
    after_attn = (resid + jnp.dot(attended, w_out, preferred_element_type=jnp.float32)).astype(jnp.bfloat16)
    after_f32 = lax.optimization_barrier(after_attn).astype(jnp.float32)
    mlp_in = rms_scale(after_f32, ffn_gain).astype(jnp.bfloat16)

    def mlp_group(rows_in):
        gate_act = jnp.dot(rows_in, w_gate.T, preferred_element_type=jnp.float32)
        up_act = jnp.dot(rows_in, w_up.T, preferred_element_type=jnp.float32)
        hidden = (jax.nn.silu(gate_act) * up_act).astype(jnp.bfloat16)
        return jnp.dot(hidden, w_down, preferred_element_type=jnp.float32)
    mlp_out = lax.map(mlp_group, mlp_in.reshape(N_REQ, GROUP_TOK, D)).reshape(count_rows, D)
    mixed = (after_f32 + mlp_out).astype(jnp.bfloat16)
    return (mixed, kv_cache)
```

```python
import jax
import jax.numpy as jnp
from jax import lax
from jax.sharding import PartitionSpec as P

H = 24
KVH = 8
HD = 64


EPSILON = 1e-05
ROPE_BASE = 1000000.0
NEG_FILL = -1e30
SCORE_SCALE = 0.125


def rms_scale(values, gain):
    mean_sq = jnp.mean(values * values, axis=-1, keepdims=True)
    return values * lax.rsqrt(mean_sq + EPSILON) * gain


def seg_positions(seg_ids):
    indices = jnp.arange(seg_ids.shape[0], dtype=jnp.int32)
    is_first = jnp.concatenate([jnp.ones((1,), bool), seg_ids[1:] != seg_ids[:-1]])
    seg_begin = lax.cummax(jnp.where(is_first, indices, jnp.zeros_like(indices)), axis=0)
    return indices - seg_begin


def rotate(heads, positions):
    half_dim = heads.shape[-1] // 2
    inv_freq = ROPE_BASE ** (-(jnp.arange(half_dim, dtype=jnp.float32) * 2.0) / (2.0 * half_dim))
    angles = positions.astype(jnp.float32)[:, None] * inv_freq[None, :]
    cos_val = jnp.cos(angles)[:, None, :]
    sin_val = jnp.sin(angles)[:, None, :]
    left = heads[..., :half_dim]
    right = heads[..., half_dim:]
    return jnp.concatenate(
        [left * cos_val - right * sin_val, right * cos_val + left * sin_val], axis=-1
    )


def block_length(shard_rows):
    return 4 * shard_rows


def key_block(running, key_blk, val_blk, key_seg, key_idx, q_grid, own_seg, query_idx):
    run_peak, run_total, run_acc = running
    k_grid = key_blk.reshape(-1, KVH, HD).transpose(1, 0, 2)
    v_grid = val_blk.reshape(-1, KVH, HD).transpose(1, 0, 2)
    scores = (
        jnp.einsum("kgqd,kcd->kgqc", q_grid, k_grid, preferred_element_type=jnp.float32)
        * SCORE_SCALE
    )
    allowed = (key_idx[None, :] <= query_idx[:, None]) & (key_seg[None, :] == own_seg[:, None])
    scores = jnp.where(allowed, scores, NEG_FILL)
    new_peak = jnp.maximum(run_peak, jnp.max(scores, axis=-1))
    weights = jnp.where(allowed, jnp.exp(scores - new_peak[..., None]), 0.0)
    factor = jnp.exp(run_peak - new_peak)
    new_total = run_total * factor + jnp.sum(weights, axis=-1)
    product = jnp.einsum(
        "kgqc,kcd->kgqd", weights.astype(jnp.bfloat16), v_grid, preferred_element_type=jnp.float32
    )
    return (new_peak, new_total, run_acc * factor[..., None] + product)


def unit_terms(pieces, gathered):
    gate_part, up_part, down_part = pieces
    contract = (((1,), (1,)), ((), ()))
    gate_act = lax.dot_general(gathered, gate_part, contract, preferred_element_type=jnp.float32)
    up_act = lax.dot_general(gathered, up_part, contract, preferred_element_type=jnp.float32)
    hidden = (jax.nn.silu(gate_act) * up_act).astype(jnp.bfloat16)
    return jnp.dot(hidden, down_part, preferred_element_type=jnp.float32)


def gather_by_shifts(part, axis):
    count = lax.psum(1, axis)
    me = lax.axis_index(axis)
    received = [part]
    for shift in range(1, count):
        pairs = [(src, (src + shift) % count) for src in range(count)]
        received.append(lax.ppermute(part, axis, pairs))
    stacked = jnp.stack(received)
    order = (me - jnp.arange(count, dtype=jnp.int32)) % count
    return jnp.take(stacked, order, axis=0).reshape(-1)


def per_device(
    tokens,
    segment,
    attn_gain,
    w_query,
    w_key,
    w_value,
    q_gain,
    k_gain,
    w_out,
    ffn_gain,
    w_gate,
    w_up,
    w_down,
):
    shard_rows = tokens.shape[0]
    groups = H // KVH
    group_seg = gather_by_shifts(segment, "hid")
    row_base = lax.axis_index("hid") * shard_rows
    positions = lax.dynamic_slice_in_dim(seg_positions(group_seg), row_base, shard_rows)
    own_seg = lax.dynamic_slice_in_dim(group_seg, row_base, shard_rows)
    query_idx = row_base + jnp.arange(shard_rows, dtype=jnp.int32)
    resid = tokens.astype(jnp.float32)
    normed = rms_scale(resid, attn_gain).astype(jnp.bfloat16)
    q_raw = jnp.dot(normed, w_query, preferred_element_type=jnp.float32).reshape(shard_rows, H, HD)
    k_raw = jnp.dot(normed, w_key, preferred_element_type=jnp.float32).reshape(shard_rows, KVH, HD)
    queries = rotate(rms_scale(q_raw, q_gain), positions).astype(jnp.bfloat16)
    key_heads = (
        rotate(rms_scale(k_raw, k_gain), positions)
        .astype(jnp.bfloat16)
        .reshape(shard_rows, KVH * HD)
    )
    values = jnp.dot(normed, w_value, preferred_element_type=jnp.float32).astype(jnp.bfloat16)
    kv_cache = jnp.concatenate([key_heads, values], axis=1)
    q_grid = queries.reshape(shard_rows, KVH, groups, HD).transpose(1, 2, 0, 3)
    start_state = (
        jnp.full((KVH, groups, shard_rows), NEG_FILL, jnp.float32),
        jnp.zeros((KVH, groups, shard_rows), jnp.float32),
        jnp.zeros((KVH, groups, shard_rows, HD), jnp.float32),
    )
    kv_part = lax.all_gather(kv_cache, "hid", axis=0, tiled=True)
    key_part = kv_part[:, : KVH * HD]
    val_part = kv_part[:, KVH * HD :]
    key_count = key_part.shape[0]
    blk_len = block_length(shard_rows)

    def one_block(block_idx, state_in):
        offset = jnp.asarray(block_idx, jnp.int32) * blk_len
        local_off = jnp.asarray(block_idx, jnp.int32) * blk_len
        key_blk = lax.dynamic_slice_in_dim(key_part, local_off, blk_len)
        val_blk = lax.dynamic_slice_in_dim(val_part, local_off, blk_len)
        key_seg = lax.dynamic_slice_in_dim(group_seg, offset, blk_len)
        key_idx = offset + jnp.arange(blk_len, dtype=jnp.int32)
        return key_block(state_in, key_blk, val_blk, key_seg, key_idx, q_grid, own_seg, query_idx)

    run_peak, run_total, run_acc = lax.fori_loop(0, key_count // blk_len, one_block, start_state)
    attended = (
        (run_acc / run_total[..., None])
        .transpose(2, 0, 1, 3)
        .reshape(shard_rows, H * HD)
        .astype(jnp.bfloat16)
    )
    after_attn = (resid + jnp.dot(attended, w_out, preferred_element_type=jnp.float32)).astype(
        jnp.bfloat16
    )
    after_f32 = lax.optimization_barrier(after_attn).astype(jnp.float32)
    mlp_in = rms_scale(after_f32, ffn_gain).astype(jnp.bfloat16)
    gathered = lax.all_gather(mlp_in, "req", axis=0, tiled=True)
    unit_sum = unit_terms(
        (
            lax.all_gather(w_gate, "hid", axis=0, tiled=True),
            lax.all_gather(w_up, "hid", axis=0, tiled=True),
            lax.all_gather(w_down, "hid", axis=0, tiled=True),
        ),
        gathered,
    )
    own_share = lax.psum_scatter(
        unit_sum.astype(jnp.bfloat16), "req", scatter_dimension=0, tiled=True
    ).astype(jnp.float32)
    mixed = (after_f32 + own_share).astype(jnp.bfloat16)
    return (mixed, kv_cache)


def solution(mesh):
    placed = (
        P(("req", "hid"), None),
        P(("req", "hid")),
        P(),
        P(),
        P(),
        P(),
        P(),
        P(),
        P(),
        P(),
        P(("req", "hid"), None),
        P(("req", "hid"), None),
        P(("req", "hid"), None),
    )
    return jax.shard_map(
        per_device,
        mesh=mesh,
        in_specs=placed,
        out_specs=(P(("req", "hid"), None), P(("req", "hid"), None)),
        check_vma=False,
    )
```

```python
import jax
import jax.numpy as jnp
from jax import lax
from jax.sharding import PartitionSpec as P

H = 24
KVH = 8
HD = 64


EPSILON = 1e-05
ROPE_BASE = 1000000.0
NEG_FILL = -1e30
SCORE_SCALE = 0.125


def rms_scale(values, gain):
    mean_sq = jnp.mean(values * values, axis=-1, keepdims=True)
    return values * lax.rsqrt(mean_sq + EPSILON) * gain


def seg_positions(seg_ids):
    indices = jnp.arange(seg_ids.shape[0], dtype=jnp.int32)
    is_first = jnp.concatenate([jnp.ones((1,), bool), seg_ids[1:] != seg_ids[:-1]])
    seg_begin = lax.cummax(jnp.where(is_first, indices, jnp.zeros_like(indices)), axis=0)
    return indices - seg_begin


def rotate(heads, positions):
    half_dim = heads.shape[-1] // 2
    inv_freq = ROPE_BASE ** (-(jnp.arange(half_dim, dtype=jnp.float32) * 2.0) / (2.0 * half_dim))
    angles = positions.astype(jnp.float32)[:, None] * inv_freq[None, :]
    cos_val = jnp.cos(angles)[:, None, :]
    sin_val = jnp.sin(angles)[:, None, :]
    left = heads[..., :half_dim]
    right = heads[..., half_dim:]
    return jnp.concatenate(
        [left * cos_val - right * sin_val, right * cos_val + left * sin_val], axis=-1
    )


def block_length(shard_rows):
    return 4 * shard_rows


def key_block(running, key_blk, val_blk, key_idx, q_grid, seg_start, query_idx):
    run_peak, run_total, run_acc = running
    k_grid = key_blk.reshape(-1, KVH, HD).transpose(1, 0, 2)
    v_grid = val_blk.reshape(-1, KVH, HD).transpose(1, 0, 2)
    scores = (
        jnp.einsum("kgqd,kcd->kgqc", q_grid, k_grid, preferred_element_type=jnp.float32)
        * SCORE_SCALE
    )
    allowed = (key_idx[None, :] <= query_idx[:, None]) & (key_idx[None, :] >= seg_start[:, None])
    scores = jnp.where(allowed, scores, NEG_FILL)
    new_peak = jnp.maximum(run_peak, jnp.max(scores, axis=-1))
    weights = jnp.where(allowed, jnp.exp(scores - new_peak[..., None]), 0.0)
    factor = jnp.exp(run_peak - new_peak)
    new_total = run_total * factor + jnp.sum(weights, axis=-1)
    product = jnp.einsum(
        "kgqc,kcd->kgqd", weights.astype(jnp.bfloat16), v_grid, preferred_element_type=jnp.float32
    )
    return (new_peak, new_total, run_acc * factor[..., None] + product)


def unit_terms(pieces, gathered):
    gate_part, up_part, down_part = pieces
    contract = (((1,), (1,)), ((), ()))
    gate_act = lax.dot_general(gathered, gate_part, contract, preferred_element_type=jnp.float32)
    up_act = lax.dot_general(gathered, up_part, contract, preferred_element_type=jnp.float32)
    hidden = (jax.nn.silu(gate_act) * up_act).astype(jnp.bfloat16)
    return jnp.dot(hidden, down_part, preferred_element_type=jnp.float32)


def join_runs(left, right):
    l_last, l_trail, l_full = left
    r_last, r_trail, r_full = right
    same = (l_last == r_last) & (r_full > 0)
    trail = r_trail + jnp.where(same, l_trail, 0)
    full = jnp.where(same & (l_full > 0), 1, 0)
    return (r_last, trail, full)


def group_positions(seg_ids, axis):
    count = lax.psum(1, axis)
    me = lax.axis_index(axis)
    rows = seg_ids.shape[0]
    last = seg_ids[rows - 1]
    trail = jnp.sum((seg_ids == last).astype(jnp.int32))
    full = (seg_ids[0] == last).astype(jnp.int32)
    summary = jnp.stack([last, trail, full])
    shift = 1
    while shift < count:
        pairs = [(src, src + shift) for src in range(count - shift)]
        got = lax.ppermute(summary, axis, pairs)
        joined = jnp.stack(join_runs((got[0], got[1], got[2]), (summary[0], summary[1], summary[2])))
        summary = jnp.where(me >= shift, joined, summary)
        shift *= 2
    before = lax.ppermute(summary, axis, [(src, src + 1) for src in range(count - 1)])
    local = seg_positions(seg_ids)
    lead = local == jnp.arange(rows, dtype=jnp.int32)
    carry = jnp.where((me > 0) & (before[0] == seg_ids[0]), before[1], 0)
    return local + jnp.where(lead, carry, 0)


def per_device(
    tokens,
    segment,
    attn_gain,
    w_query,
    w_key,
    w_value,
    q_gain,
    k_gain,
    w_out,
    ffn_gain,
    w_gate,
    w_up,
    w_down,
):
    shard_rows = tokens.shape[0]
    groups = H // KVH
    row_base = lax.axis_index("hid") * shard_rows
    positions = group_positions(segment, "hid")
    query_idx = row_base + jnp.arange(shard_rows, dtype=jnp.int32)
    seg_start = query_idx - positions
    resid = tokens.astype(jnp.float32)
    normed = rms_scale(resid, attn_gain).astype(jnp.bfloat16)
    q_raw = jnp.dot(normed, w_query, preferred_element_type=jnp.float32).reshape(shard_rows, H, HD)
    k_raw = jnp.dot(normed, w_key, preferred_element_type=jnp.float32).reshape(shard_rows, KVH, HD)
    queries = rotate(rms_scale(q_raw, q_gain), positions).astype(jnp.bfloat16)
    key_heads = (
        rotate(rms_scale(k_raw, k_gain), positions)
        .astype(jnp.bfloat16)
        .reshape(shard_rows, KVH * HD)
    )
    values = jnp.dot(normed, w_value, preferred_element_type=jnp.float32).astype(jnp.bfloat16)
    kv_cache = jnp.concatenate([key_heads, values], axis=1)
    q_grid = queries.reshape(shard_rows, KVH, groups, HD).transpose(1, 2, 0, 3)
    start_state = (
        jnp.full((KVH, groups, shard_rows), NEG_FILL, jnp.float32),
        jnp.zeros((KVH, groups, shard_rows), jnp.float32),
        jnp.zeros((KVH, groups, shard_rows, HD), jnp.float32),
    )
    hid_count = lax.psum(1, "hid")
    pieces = [kv_cache, w_gate, w_up, w_down]
    sizes = [p.size for p in pieces]
    bundle = lax.all_gather(
        jnp.concatenate([p.reshape(-1) for p in pieces]), "hid", axis=0, tiled=False
    )
    cuts = [sum(sizes[:i]) for i in range(len(sizes) + 1)]
    parts = [
        bundle[:, cuts[i] : cuts[i + 1]].reshape((hid_count * p.shape[0],) + p.shape[1:])
        for i, p in enumerate(pieces)
    ]
    kv_part, gate_rows, up_rows, down_rows = parts
    key_part = kv_part[:, : KVH * HD]
    val_part = kv_part[:, KVH * HD :]
    key_count = key_part.shape[0]
    blk_len = block_length(shard_rows)

    def one_block(block_idx, state_in):
        offset = jnp.asarray(block_idx, jnp.int32) * blk_len
        local_off = jnp.asarray(block_idx, jnp.int32) * blk_len
        key_blk = lax.dynamic_slice_in_dim(key_part, local_off, blk_len)
        val_blk = lax.dynamic_slice_in_dim(val_part, local_off, blk_len)
        key_idx = offset + jnp.arange(blk_len, dtype=jnp.int32)
        return key_block(state_in, key_blk, val_blk, key_idx, q_grid, seg_start, query_idx)

    run_peak, run_total, run_acc = lax.fori_loop(0, key_count // blk_len, one_block, start_state)
    attended = (
        (run_acc / run_total[..., None])
        .transpose(2, 0, 1, 3)
        .reshape(shard_rows, H * HD)
        .astype(jnp.bfloat16)
    )
    after_attn = (resid + jnp.dot(attended, w_out, preferred_element_type=jnp.float32)).astype(
        jnp.bfloat16
    )
    after_f32 = lax.optimization_barrier(after_attn).astype(jnp.float32)
    mlp_in = rms_scale(after_f32, ffn_gain).astype(jnp.bfloat16)
    gathered = lax.all_gather(mlp_in, "req", axis=0, tiled=True)
    unit_sum = unit_terms(
        (gate_rows, up_rows, down_rows),
        gathered,
    )
    own_share = lax.psum_scatter(
        unit_sum.astype(jnp.bfloat16), "req", scatter_dimension=0, tiled=True
    ).astype(jnp.float32)
    mixed = (after_f32 + own_share).astype(jnp.bfloat16)
    return (mixed, kv_cache)


def solution(mesh):
    placed = (
        P(("req", "hid"), None),
        P(("req", "hid")),
        P(),
        P(),
        P(),
        P(),
        P(),
        P(),
        P(),
        P(),
        P(("req", "hid"), None),
        P(("req", "hid"), None),
        P(("req", "hid"), None),
    )
    return jax.shard_map(
        per_device,
        mesh=mesh,
        in_specs=placed,
        out_specs=(P(("req", "hid"), None), P(("req", "hid"), None)),
        check_vma=False,
    )
```

```python
import jax
import jax.numpy as jnp
from jax import lax
from jax.sharding import PartitionSpec as P

H = 24
KVH = 8
HD = 64


EPSILON = 1e-05
ROPE_BASE = 1000000.0
NEG_FILL = -1e30
SCORE_SCALE = 0.125


def rms_scale(values, gain):
    mean_sq = jnp.mean(values * values, axis=-1, keepdims=True)
    return values * lax.rsqrt(mean_sq + EPSILON) * gain


def seg_positions(seg_ids):
    indices = jnp.arange(seg_ids.shape[0], dtype=jnp.int32)
    is_first = jnp.concatenate([jnp.ones((1,), bool), seg_ids[1:] != seg_ids[:-1]])
    seg_begin = lax.cummax(jnp.where(is_first, indices, jnp.zeros_like(indices)), axis=0)
    return indices - seg_begin


def rotate(heads, positions):
    half_dim = heads.shape[-1] // 2
    inv_freq = ROPE_BASE ** (-(jnp.arange(half_dim, dtype=jnp.float32) * 2.0) / (2.0 * half_dim))
    angles = positions.astype(jnp.float32)[:, None] * inv_freq[None, :]
    cos_val = jnp.cos(angles)[:, None, :]
    sin_val = jnp.sin(angles)[:, None, :]
    left = heads[..., :half_dim]
    right = heads[..., half_dim:]
    return jnp.concatenate(
        [left * cos_val - right * sin_val, right * cos_val + left * sin_val], axis=-1
    )


def block_length(shard_rows):
    return 4 * shard_rows


def key_block(running, key_blk, val_blk, key_idx, q_grid, seg_start, query_idx):
    run_peak, run_total, run_acc = running
    k_grid = key_blk.reshape(-1, KVH, HD).transpose(1, 0, 2)
    v_grid = val_blk.reshape(-1, KVH, HD).transpose(1, 0, 2)
    scores = (
        jnp.einsum("kgqd,kcd->kgqc", q_grid, k_grid, preferred_element_type=jnp.float32)
        * SCORE_SCALE
    )
    allowed = (key_idx[None, :] <= query_idx[:, None]) & (key_idx[None, :] >= seg_start[:, None])
    scores = jnp.where(allowed, scores, NEG_FILL)
    new_peak = jnp.maximum(run_peak, jnp.max(scores, axis=-1))
    weights = jnp.where(allowed, jnp.exp(scores - new_peak[..., None]), 0.0)
    factor = jnp.exp(run_peak - new_peak)
    new_total = run_total * factor + jnp.sum(weights, axis=-1)
    product = jnp.einsum(
        "kgqc,kcd->kgqd", weights.astype(jnp.bfloat16), v_grid, preferred_element_type=jnp.float32
    )
    return (new_peak, new_total, run_acc * factor[..., None] + product)


def unit_terms(pieces, gathered):
    gate_part, up_part, down_part = pieces
    contract = (((1,), (1,)), ((), ()))
    gate_act = lax.dot_general(gathered, gate_part, contract, preferred_element_type=jnp.float32)
    up_act = lax.dot_general(gathered, up_part, contract, preferred_element_type=jnp.float32)
    hidden = (jax.nn.silu(gate_act) * up_act).astype(jnp.bfloat16)
    return jnp.dot(hidden, down_part, preferred_element_type=jnp.float32)


def gather_by_shifts(part, axis):
    count = lax.psum(1, axis)
    me = lax.axis_index(axis)
    received = [part]
    for shift in range(1, count):
        pairs = [(src, (src + shift) % count) for src in range(count)]
        received.append(lax.ppermute(part, axis, pairs))
    stacked = jnp.stack(received)
    order = (me - jnp.arange(count, dtype=jnp.int32)) % count
    return jnp.take(stacked, order, axis=0).reshape(-1)


def per_device(
    tokens,
    segment,
    attn_gain,
    w_query,
    w_key,
    w_value,
    q_gain,
    k_gain,
    w_out,
    ffn_gain,
    w_gate,
    w_up,
    w_down,
):
    shard_rows = tokens.shape[0]
    groups = H // KVH
    row_base = lax.axis_index("hid") * shard_rows
    group_seg = gather_by_shifts(segment, "hid")
    positions = lax.dynamic_slice_in_dim(seg_positions(group_seg), row_base, shard_rows)
    query_idx = row_base + jnp.arange(shard_rows, dtype=jnp.int32)
    seg_start = query_idx - positions
    resid = tokens.astype(jnp.float32)
    normed = rms_scale(resid, attn_gain).astype(jnp.bfloat16)
    q_raw = jnp.dot(normed, w_query, preferred_element_type=jnp.float32).reshape(shard_rows, H, HD)
    k_raw = jnp.dot(normed, w_key, preferred_element_type=jnp.float32).reshape(shard_rows, KVH, HD)
    queries = rotate(rms_scale(q_raw, q_gain), positions).astype(jnp.bfloat16)
    key_heads = (
        rotate(rms_scale(k_raw, k_gain), positions)
        .astype(jnp.bfloat16)
        .reshape(shard_rows, KVH * HD)
    )
    values = jnp.dot(normed, w_value, preferred_element_type=jnp.float32).astype(jnp.bfloat16)
    kv_cache = jnp.concatenate([key_heads, values], axis=1)
    q_grid = queries.reshape(shard_rows, KVH, groups, HD).transpose(1, 2, 0, 3)
    start_state = (
        jnp.full((KVH, groups, shard_rows), NEG_FILL, jnp.float32),
        jnp.zeros((KVH, groups, shard_rows), jnp.float32),
        jnp.zeros((KVH, groups, shard_rows, HD), jnp.float32),
    )
    kv_part = lax.all_gather(kv_cache, "hid", axis=0, tiled=True)
    unit_rows = lax.all_gather(
        jnp.concatenate([w_gate, w_up, w_down], axis=1), "hid", axis=0, tiled=True
    )
    width = w_gate.shape[1]
    gate_rows = unit_rows[:, :width]
    up_rows = unit_rows[:, width : 2 * width]
    down_rows = unit_rows[:, 2 * width :]
    key_part = kv_part[:, : KVH * HD]
    val_part = kv_part[:, KVH * HD :]
    key_count = key_part.shape[0]
    blk_len = block_length(shard_rows)

    def one_block(block_idx, state_in):
        offset = jnp.asarray(block_idx, jnp.int32) * blk_len
        local_off = jnp.asarray(block_idx, jnp.int32) * blk_len
        key_blk = lax.dynamic_slice_in_dim(key_part, local_off, blk_len)
        val_blk = lax.dynamic_slice_in_dim(val_part, local_off, blk_len)
        key_idx = offset + jnp.arange(blk_len, dtype=jnp.int32)
        return key_block(state_in, key_blk, val_blk, key_idx, q_grid, seg_start, query_idx)

    run_peak, run_total, run_acc = lax.fori_loop(0, key_count // blk_len, one_block, start_state)
    attended = (
        (run_acc / run_total[..., None])
        .transpose(2, 0, 1, 3)
        .reshape(shard_rows, H * HD)
        .astype(jnp.bfloat16)
    )
    after_attn = (resid + jnp.dot(attended, w_out, preferred_element_type=jnp.float32)).astype(
        jnp.bfloat16
    )
    after_f32 = lax.optimization_barrier(after_attn).astype(jnp.float32)
    mlp_in = rms_scale(after_f32, ffn_gain).astype(jnp.bfloat16)
    gathered = lax.all_gather(mlp_in, "req", axis=0, tiled=True)
    unit_sum = unit_terms(
        (gate_rows, up_rows, down_rows),
        gathered,
    )
    own_share = lax.psum_scatter(
        unit_sum.astype(jnp.bfloat16), "req", scatter_dimension=0, tiled=True
    ).astype(jnp.float32)
    mixed = (after_f32 + own_share).astype(jnp.bfloat16)
    return (mixed, kv_cache)


def solution(mesh):
    placed = (
        P(("req", "hid"), None),
        P(("req", "hid")),
        P(),
        P(),
        P(),
        P(),
        P(),
        P(),
        P(),
        P(),
        P(("req", "hid"), None),
        P(("req", "hid"), None),
        P(("req", "hid"), None),
    )
    return jax.shard_map(
        per_device,
        mesh=mesh,
        in_specs=placed,
        out_specs=(P(("req", "hid"), None), P(("req", "hid"), None)),
        check_vma=False,
    )
```

```python
import jax
import jax.numpy as jnp
from jax import lax
from jax.experimental import pallas as pl
from jax.experimental.pallas import tpu as pltpu
from jax.sharding import PartitionSpec as P

H = 24
KVH = 8
HD = 64


EPSILON = 1e-05
ROPE_BASE = 1000000.0
NEG_FILL = -1e30
SCORE_SCALE = 0.125


def rms_scale(values, gain):
    mean_sq = jnp.mean(values * values, axis=-1, keepdims=True)
    return values * lax.rsqrt(mean_sq + EPSILON) * gain


def seg_positions(seg_ids):
    indices = jnp.arange(seg_ids.shape[0], dtype=jnp.int32)
    is_first = jnp.concatenate([jnp.ones((1,), bool), seg_ids[1:] != seg_ids[:-1]])
    seg_begin = lax.cummax(jnp.where(is_first, indices, jnp.zeros_like(indices)), axis=0)
    return indices - seg_begin


def rotate(heads, positions):
    half_dim = heads.shape[-1] // 2
    inv_freq = ROPE_BASE ** (-(jnp.arange(half_dim, dtype=jnp.float32) * 2.0) / (2.0 * half_dim))
    angles = positions.astype(jnp.float32)[:, None] * inv_freq[None, :]
    cos_val = jnp.cos(angles)[:, None, :]
    sin_val = jnp.sin(angles)[:, None, :]
    left = heads[..., :half_dim]
    right = heads[..., half_dim:]
    return jnp.concatenate(
        [left * cos_val - right * sin_val, right * cos_val + left * sin_val], axis=-1
    )


def block_length(shard_rows):
    return 4 * shard_rows


def key_block(running, key_blk, val_blk, key_idx, q_grid, seg_start, query_idx):
    run_peak, run_total, run_acc = running
    k_grid = key_blk.reshape(-1, KVH, HD).transpose(1, 0, 2)
    v_grid = val_blk.reshape(-1, KVH, HD).transpose(1, 0, 2)
    scores = (
        jnp.einsum("kgqd,kcd->kgqc", q_grid, k_grid, preferred_element_type=jnp.float32)
        * SCORE_SCALE
    )
    allowed = (key_idx[None, :] <= query_idx[:, None]) & (key_idx[None, :] >= seg_start[:, None])
    scores = jnp.where(allowed, scores, NEG_FILL)
    new_peak = jnp.maximum(run_peak, jnp.max(scores, axis=-1))
    weights = jnp.where(allowed, jnp.exp(scores - new_peak[..., None]), 0.0)
    factor = jnp.exp(run_peak - new_peak)
    new_total = run_total * factor + jnp.sum(weights, axis=-1)
    product = jnp.einsum(
        "kgqc,kcd->kgqd", weights.astype(jnp.bfloat16), v_grid, preferred_element_type=jnp.float32
    )
    return (new_peak, new_total, run_acc * factor[..., None] + product)


KEY_TILE = 512


def flash_kernel(bounds_ref, q_ref, k_ref, v_ref, qi_ref, ss_ref, o_ref, m_sc, l_sc, acc_sc):
    kb = pl.program_id(1)
    k_start = kb * KEY_TILE

    @pl.when(kb == 0)
    def _():
        m_sc[...] = jnp.full(m_sc.shape, NEG_FILL, jnp.float32)
        l_sc[...] = jnp.zeros(l_sc.shape, jnp.float32)
        acc_sc[...] = jnp.zeros(acc_sc.shape, jnp.float32)

    @pl.when((k_start <= bounds_ref[1]) & (k_start + KEY_TILE > bounds_ref[0]))
    def _():
        scores = (
            lax.dot_general(
                q_ref[0], k_ref[0], (((1,), (1,)), ((), ())), preferred_element_type=jnp.float32
            )
            * SCORE_SCALE
        )
        key_idx = k_start + lax.broadcasted_iota(jnp.int32, scores.shape, 1)
        allowed = (key_idx <= qi_ref[...]) & (key_idx >= ss_ref[...])
        scores = jnp.where(allowed, scores, NEG_FILL)
        m_prev = m_sc[...]
        m_new = jnp.maximum(m_prev, jnp.max(scores, axis=1, keepdims=True))
        weights = jnp.where(allowed, jnp.exp(scores - m_new), 0.0)
        factor = jnp.exp(m_prev - m_new)
        l_sc[...] = l_sc[...] * factor + jnp.sum(weights, axis=1, keepdims=True)
        acc_sc[...] = acc_sc[...] * factor + jnp.dot(
            weights.astype(jnp.bfloat16), v_ref[0], preferred_element_type=jnp.float32
        )
        m_sc[...] = m_new

    @pl.when(kb == pl.num_programs(1) - 1)
    def _():
        o_ref[0] = (acc_sc[...] / l_sc[...]).astype(o_ref.dtype)


def flash_attention(q_heads, k_heads, v_heads, q_rows, starts, bounds):
    heads, rows, dim = q_heads.shape
    key_count = k_heads.shape[1]
    blocks = key_count // KEY_TILE

    def kv_map(h, kb, b_ref):
        first = b_ref[0] // KEY_TILE
        last = b_ref[1] // KEY_TILE
        return (h, jnp.minimum(jnp.maximum(kb, first), last), 0)

    grid_spec = pltpu.PrefetchScalarGridSpec(
        num_scalar_prefetch=1,
        grid=(heads, blocks),
        in_specs=[
            pl.BlockSpec((1, rows, dim), lambda h, kb, b_ref: (h, 0, 0)),
            pl.BlockSpec((1, KEY_TILE, dim), kv_map),
            pl.BlockSpec((1, KEY_TILE, dim), kv_map),
            pl.BlockSpec((rows, 1), lambda h, kb, b_ref: (0, 0)),
            pl.BlockSpec((rows, 1), lambda h, kb, b_ref: (0, 0)),
        ],
        out_specs=pl.BlockSpec((1, rows, dim), lambda h, kb, b_ref: (h, 0, 0)),
        scratch_shapes=[
            pltpu.VMEM((rows, 1), jnp.float32),
            pltpu.VMEM((rows, 1), jnp.float32),
            pltpu.VMEM((rows, dim), jnp.float32),
        ],
    )
    return pl.pallas_call(
        flash_kernel,
        out_shape=jax.ShapeDtypeStruct((heads, rows, dim), jnp.bfloat16),
        grid_spec=grid_spec,
    )(bounds, q_heads, k_heads, v_heads, q_rows, starts)


def unit_terms(pieces, gathered):
    gate_part, up_part, down_part = pieces
    contract = (((1,), (1,)), ((), ()))
    gate_act = lax.dot_general(gathered, gate_part, contract, preferred_element_type=jnp.float32)
    up_act = lax.dot_general(gathered, up_part, contract, preferred_element_type=jnp.float32)
    hidden = (jax.nn.silu(gate_act) * up_act).astype(jnp.bfloat16)
    return jnp.dot(hidden, down_part, preferred_element_type=jnp.float32)


def gather_by_shifts(part, axis):
    count = lax.psum(1, axis)
    me = lax.axis_index(axis)
    received = [part]
    for shift in range(1, count):
        pairs = [(src, (src + shift) % count) for src in range(count)]
        received.append(lax.ppermute(part, axis, pairs))
    stacked = jnp.stack(received)
    order = (me - jnp.arange(count, dtype=jnp.int32)) % count
    return jnp.take(stacked, order, axis=0).reshape(-1)


def per_device(
    tokens,
    segment,
    attn_gain,
    w_query,
    w_key,
    w_value,
    q_gain,
    k_gain,
    w_out,
    ffn_gain,
    w_gate,
    w_up,
    w_down,
):
    shard_rows = tokens.shape[0]
    groups = H // KVH
    row_base = lax.axis_index("hid") * shard_rows
    group_seg = gather_by_shifts(segment, "hid")
    positions = lax.dynamic_slice_in_dim(seg_positions(group_seg), row_base, shard_rows)
    query_idx = row_base + jnp.arange(shard_rows, dtype=jnp.int32)
    seg_start = query_idx - positions
    resid = tokens.astype(jnp.float32)
    normed = rms_scale(resid, attn_gain).astype(jnp.bfloat16)
    q_raw = jnp.dot(normed, w_query, preferred_element_type=jnp.float32).reshape(shard_rows, H, HD)
    k_raw = jnp.dot(normed, w_key, preferred_element_type=jnp.float32).reshape(shard_rows, KVH, HD)
    queries = rotate(rms_scale(q_raw, q_gain), positions).astype(jnp.bfloat16)
    key_heads = (
        rotate(rms_scale(k_raw, k_gain), positions)
        .astype(jnp.bfloat16)
        .reshape(shard_rows, KVH * HD)
    )
    values = jnp.dot(normed, w_value, preferred_element_type=jnp.float32).astype(jnp.bfloat16)
    kv_cache = jnp.concatenate([key_heads, values], axis=1)
    q_grid = queries.reshape(shard_rows, KVH, groups, HD).transpose(1, 2, 0, 3)
    kv_part = lax.all_gather(kv_cache, "hid", axis=0, tiled=True)
    unit_rows = lax.all_gather(
        jnp.concatenate([w_gate, w_up, w_down], axis=1), "hid", axis=0, tiled=True
    )
    width = w_gate.shape[1]
    gate_rows = unit_rows[:, :width]
    up_rows = unit_rows[:, width : 2 * width]
    down_rows = unit_rows[:, 2 * width :]
    key_count = kv_part.shape[0]
    k_heads = kv_part[:, : KVH * HD].reshape(key_count, KVH, HD).transpose(1, 0, 2)
    v_heads = kv_part[:, KVH * HD :].reshape(key_count, KVH, HD).transpose(1, 0, 2)
    q_rows = jnp.tile(query_idx, groups).reshape(groups * shard_rows, 1)
    starts = jnp.tile(seg_start, groups).reshape(groups * shard_rows, 1)
    bounds = jnp.stack([jnp.min(seg_start), row_base + shard_rows - 1])
    attn_heads = flash_attention(
        q_grid.reshape(KVH, groups * shard_rows, HD), k_heads, v_heads, q_rows, starts, bounds
    )
    attended = (
        attn_heads.reshape(KVH, groups, shard_rows, HD)
        .transpose(2, 0, 1, 3)
        .reshape(shard_rows, H * HD)
    )
    after_attn = (resid + jnp.dot(attended, w_out, preferred_element_type=jnp.float32)).astype(
        jnp.bfloat16
    )
    after_f32 = lax.optimization_barrier(after_attn).astype(jnp.float32)
    mlp_in = rms_scale(after_f32, ffn_gain).astype(jnp.bfloat16)
    gathered = lax.all_gather(mlp_in, "req", axis=0, tiled=True)
    unit_sum = unit_terms(
        (gate_rows, up_rows, down_rows),
        gathered,
    )
    own_share = lax.psum_scatter(
        unit_sum.astype(jnp.bfloat16), "req", scatter_dimension=0, tiled=True
    ).astype(jnp.float32)
    mixed = (after_f32 + own_share).astype(jnp.bfloat16)
    return (mixed, kv_cache)


def solution(mesh):
    placed = (
        P(("req", "hid"), None),
        P(("req", "hid")),
        P(),
        P(),
        P(),
        P(),
        P(),
        P(),
        P(),
        P(),
        P(("req", "hid"), None),
        P(("req", "hid"), None),
        P(("req", "hid"), None),
    )
    return jax.shard_map(
        per_device,
        mesh=mesh,
        in_specs=placed,
        out_specs=(P(("req", "hid"), None), P(("req", "hid"), None)),
        check_vma=False,
    )
```

```python
import jax
import jax.numpy as jnp
from jax import lax
from jax.experimental import pallas as pl
from jax.experimental.pallas import tpu as pltpu
from jax.sharding import PartitionSpec as P

H = 24
KVH = 8
HD = 64


EPSILON = 1e-05
ROPE_BASE = 1000000.0
NEG_FILL = -1e30
SCORE_SCALE = 0.125


def rms_scale(values, gain):
    mean_sq = jnp.mean(values * values, axis=-1, keepdims=True)
    return values * lax.rsqrt(mean_sq + EPSILON) * gain


def seg_positions(seg_ids):
    indices = jnp.arange(seg_ids.shape[0], dtype=jnp.int32)
    is_first = jnp.concatenate([jnp.ones((1,), bool), seg_ids[1:] != seg_ids[:-1]])
    seg_begin = lax.cummax(jnp.where(is_first, indices, jnp.zeros_like(indices)), axis=0)
    return indices - seg_begin


def rotate(heads, positions):
    half_dim = heads.shape[-1] // 2
    inv_freq = ROPE_BASE ** (-(jnp.arange(half_dim, dtype=jnp.float32) * 2.0) / (2.0 * half_dim))
    angles = positions.astype(jnp.float32)[:, None] * inv_freq[None, :]
    cos_val = jnp.cos(angles)[:, None, :]
    sin_val = jnp.sin(angles)[:, None, :]
    left = heads[..., :half_dim]
    right = heads[..., half_dim:]
    return jnp.concatenate(
        [left * cos_val - right * sin_val, right * cos_val + left * sin_val], axis=-1
    )


SHARDS_PER_TILE = 4


def flash_kernel(bounds_ref, q_ref, k_ref, v_ref, qi_ref, ss_ref, o_ref, m_sc, l_sc, acc_sc):
    kb = pl.program_id(1)
    tile = k_ref.shape[0] * k_ref.shape[2]
    k_start = kb * tile

    @pl.when(kb == 0)
    def _():
        m_sc[...] = jnp.full(m_sc.shape, NEG_FILL, jnp.float32)
        l_sc[...] = jnp.zeros(l_sc.shape, jnp.float32)
        acc_sc[...] = jnp.zeros(acc_sc.shape, jnp.float32)

    @pl.when((k_start <= bounds_ref[1]) & (k_start + tile > bounds_ref[0]))
    def _():
        k_blk = k_ref[...].reshape(tile, k_ref.shape[3])
        v_blk = v_ref[...].reshape(tile, v_ref.shape[3])
        scores = (
            lax.dot_general(
                q_ref[0], k_blk, (((1,), (1,)), ((), ())), preferred_element_type=jnp.float32
            )
            * SCORE_SCALE
        )
        key_idx = k_start + lax.broadcasted_iota(jnp.int32, scores.shape, 1)
        allowed = (key_idx <= qi_ref[...]) & (key_idx >= ss_ref[...])
        scores = jnp.where(allowed, scores, NEG_FILL)
        m_prev = m_sc[...]
        m_new = jnp.maximum(m_prev, jnp.max(scores, axis=1, keepdims=True))
        weights = jnp.where(allowed, jnp.exp(scores - m_new), 0.0)
        factor = jnp.exp(m_prev - m_new)
        l_sc[...] = l_sc[...] * factor + jnp.sum(weights, axis=1, keepdims=True)
        acc_sc[...] = acc_sc[...] * factor + jnp.dot(
            weights.astype(jnp.bfloat16), v_blk, preferred_element_type=jnp.float32
        )
        m_sc[...] = m_new

    @pl.when(kb == pl.num_programs(1) - 1)
    def _():
        o_ref[0] = (acc_sc[...] / l_sc[...]).astype(o_ref.dtype)


def flash_attention(q_heads, k_grid, kv_grid, q_rows, starts, bounds):
    heads, rows, dim = q_heads.shape
    shards, _, shard_len, _ = k_grid.shape
    tile = SHARDS_PER_TILE * shard_len
    blocks = shards // SHARDS_PER_TILE

    def clamp(kb, b_ref):
        first = b_ref[0] // tile
        last = b_ref[1] // tile
        return jnp.minimum(jnp.maximum(kb, first), last)

    grid_spec = pltpu.PrefetchScalarGridSpec(
        num_scalar_prefetch=1,
        grid=(heads, blocks),
        in_specs=[
            pl.BlockSpec((1, rows, dim), lambda h, kb, b_ref: (h, 0, 0)),
            pl.BlockSpec(
                (SHARDS_PER_TILE, 1, shard_len, dim),
                lambda h, kb, b_ref: (clamp(kb, b_ref), h, 0, 0),
            ),
            pl.BlockSpec(
                (SHARDS_PER_TILE, 1, shard_len, dim),
                lambda h, kb, b_ref: (clamp(kb, b_ref), heads + h, 0, 0),
            ),
            pl.BlockSpec((rows, 1), lambda h, kb, b_ref: (0, 0)),
            pl.BlockSpec((rows, 1), lambda h, kb, b_ref: (0, 0)),
        ],
        out_specs=pl.BlockSpec((1, rows, dim), lambda h, kb, b_ref: (h, 0, 0)),
        scratch_shapes=[
            pltpu.VMEM((rows, 1), jnp.float32),
            pltpu.VMEM((rows, 1), jnp.float32),
            pltpu.VMEM((rows, dim), jnp.float32),
        ],
    )
    return pl.pallas_call(
        flash_kernel,
        out_shape=jax.ShapeDtypeStruct((heads, rows, dim), jnp.bfloat16),
        grid_spec=grid_spec,
    )(bounds, q_heads, k_grid, kv_grid, q_rows, starts)


def rotate_grid(heads, positions):
    half_dim = heads.shape[-1] // 2
    inv_freq = ROPE_BASE ** (-(jnp.arange(half_dim, dtype=jnp.float32) * 2.0) / (2.0 * half_dim))
    angles = positions.astype(jnp.float32)[:, None, :, None] * inv_freq
    cos_val = jnp.cos(angles)
    sin_val = jnp.sin(angles)
    left = heads[..., :half_dim]
    right = heads[..., half_dim:]
    return jnp.concatenate(
        [left * cos_val - right * sin_val, right * cos_val + left * sin_val], axis=-1
    )


def unit_terms(pieces, gathered):
    gate_part, up_part, down_part = pieces
    contract = (((1,), (1,)), ((), ()))
    gate_act = lax.dot_general(gathered, gate_part, contract, preferred_element_type=jnp.float32)
    up_act = lax.dot_general(gathered, up_part, contract, preferred_element_type=jnp.float32)
    hidden = (jax.nn.silu(gate_act) * up_act).astype(jnp.bfloat16)
    return jnp.dot(hidden, down_part, preferred_element_type=jnp.float32)


def gather_by_shifts(part, axis):
    count = lax.psum(1, axis)
    me = lax.axis_index(axis)
    received = [part]
    for shift in range(1, count):
        pairs = [(src, (src + shift) % count) for src in range(count)]
        received.append(lax.ppermute(part, axis, pairs))
    stacked = jnp.stack(received)
    order = (me - jnp.arange(count, dtype=jnp.int32)) % count
    return jnp.take(stacked, order, axis=0).reshape(-1)


def per_device(
    tokens,
    segment,
    attn_gain,
    w_query,
    w_key,
    w_value,
    q_gain,
    k_gain,
    w_out,
    ffn_gain,
    w_gate,
    w_up,
    w_down,
):
    shard_rows = tokens.shape[0]
    groups = H // KVH
    row_base = lax.axis_index("hid") * shard_rows
    group_seg = gather_by_shifts(segment, "hid")
    positions = lax.dynamic_slice_in_dim(seg_positions(group_seg), row_base, shard_rows)
    query_idx = row_base + jnp.arange(shard_rows, dtype=jnp.int32)
    seg_start = query_idx - positions
    resid = tokens.astype(jnp.float32)
    normed = rms_scale(resid, attn_gain).astype(jnp.bfloat16)
    q_raw = jnp.dot(normed, w_query, preferred_element_type=jnp.float32).reshape(shard_rows, H, HD)
    k_raw = jnp.dot(normed, w_key, preferred_element_type=jnp.float32).reshape(shard_rows, KVH, HD)
    k_normed = rms_scale(k_raw, k_gain)
    values = jnp.dot(normed, w_value, preferred_element_type=jnp.float32).astype(jnp.bfloat16)
    send = jnp.concatenate(
        [k_normed.astype(jnp.bfloat16).reshape(shard_rows, KVH * HD), values], axis=1
    )
    kv_grid = lax.all_gather(
        send.reshape(shard_rows, 2 * KVH, HD).transpose(1, 0, 2), "hid", axis=0, tiled=False
    )
    queries = rotate(rms_scale(q_raw, q_gain), positions).astype(jnp.bfloat16)
    key_heads = rotate(k_normed, positions).astype(jnp.bfloat16).reshape(shard_rows, KVH * HD)
    kv_cache = jnp.concatenate([key_heads, values], axis=1)
    q_grid = queries.reshape(shard_rows, KVH, groups, HD).transpose(1, 2, 0, 3)
    hid_count = kv_grid.shape[0]
    key_pos = seg_positions(group_seg).reshape(hid_count, shard_rows)
    k_grid = rotate_grid(kv_grid[:, :KVH].astype(jnp.float32), key_pos).astype(jnp.bfloat16)
    unit_rows = lax.all_gather(
        jnp.concatenate([w_gate, w_up, w_down], axis=1), "hid", axis=0, tiled=True
    )
    width = w_gate.shape[1]
    gate_rows = unit_rows[:, :width]
    up_rows = unit_rows[:, width : 2 * width]
    down_rows = unit_rows[:, 2 * width :]
    q_rows = jnp.tile(query_idx, groups).reshape(groups * shard_rows, 1)
    starts = jnp.tile(seg_start, groups).reshape(groups * shard_rows, 1)
    bounds = jnp.stack([jnp.min(seg_start), row_base + shard_rows - 1])
    attn_heads = flash_attention(
        q_grid.reshape(KVH, groups * shard_rows, HD), k_grid, kv_grid, q_rows, starts, bounds
    )
    attended = (
        attn_heads.reshape(KVH, groups, shard_rows, HD)
        .transpose(2, 0, 1, 3)
        .reshape(shard_rows, H * HD)
    )
    after_attn = (resid + jnp.dot(attended, w_out, preferred_element_type=jnp.float32)).astype(
        jnp.bfloat16
    )
    after_f32 = lax.optimization_barrier(after_attn).astype(jnp.float32)
    mlp_in = rms_scale(after_f32, ffn_gain).astype(jnp.bfloat16)
    gathered = lax.all_gather(mlp_in, "req", axis=0, tiled=True)
    unit_sum = unit_terms(
        (gate_rows, up_rows, down_rows),
        gathered,
    )
    own_share = lax.psum_scatter(
        unit_sum.astype(jnp.bfloat16), "req", scatter_dimension=0, tiled=True
    ).astype(jnp.float32)
    mixed = (after_f32 + own_share).astype(jnp.bfloat16)
    return (mixed, kv_cache)


def solution(mesh):
    placed = (
        P(("req", "hid"), None),
        P(("req", "hid")),
        P(),
        P(),
        P(),
        P(),
        P(),
        P(),
        P(),
        P(),
        P(("req", "hid"), None),
        P(("req", "hid"), None),
        P(("req", "hid"), None),
    )
    return jax.shard_map(
        per_device,
        mesh=mesh,
        in_specs=placed,
        out_specs=(P(("req", "hid"), None), P(("req", "hid"), None)),
        check_vma=False,
    )
```

```python
import jax
import jax.numpy as jnp
from jax import lax
from jax.experimental import pallas as pl
from jax.experimental.pallas import tpu as pltpu
from jax.sharding import PartitionSpec as P

H = 24
KVH = 8
HD = 64


EPSILON = 1e-05
ROPE_BASE = 1000000.0
NEG_FILL = -1e30
SCORE_SCALE = 0.125


def rms_scale(values, gain):
    mean_sq = jnp.mean(values * values, axis=-1, keepdims=True)
    return values * lax.rsqrt(mean_sq + EPSILON) * gain


def seg_positions(seg_ids):
    indices = jnp.arange(seg_ids.shape[0], dtype=jnp.int32)
    is_first = jnp.concatenate([jnp.ones((1,), bool), seg_ids[1:] != seg_ids[:-1]])
    seg_begin = lax.cummax(jnp.where(is_first, indices, jnp.zeros_like(indices)), axis=0)
    return indices - seg_begin


def rotate(heads, positions):
    half_dim = heads.shape[-1] // 2
    inv_freq = ROPE_BASE ** (-(jnp.arange(half_dim, dtype=jnp.float32) * 2.0) / (2.0 * half_dim))
    angles = positions.astype(jnp.float32)[:, None] * inv_freq[None, :]
    cos_val = jnp.cos(angles)[:, None, :]
    sin_val = jnp.sin(angles)[:, None, :]
    left = heads[..., :half_dim]
    right = heads[..., half_dim:]
    return jnp.concatenate(
        [left * cos_val - right * sin_val, right * cos_val + left * sin_val], axis=-1
    )


SHARDS_PER_TILE = 4
LANES = 128


def flash_kernel(
    bounds_ref, q_ref, k_ref, v_ref, cos_ref, sin_ref, swap_ref, qi_ref, ss_ref, o_ref,
    m_sc, l_sc, acc_sc,
):
    kb = pl.program_id(1)
    pair = q_ref.shape[1]
    tile = k_ref.shape[0] * k_ref.shape[1]
    k_start = kb * tile

    @pl.when(kb == 0)
    def _():
        m_sc[...] = jnp.full(m_sc.shape, NEG_FILL, jnp.float32)
        l_sc[...] = jnp.zeros(l_sc.shape, jnp.float32)
        acc_sc[...] = jnp.zeros(acc_sc.shape, jnp.float32)

    @pl.when((k_start <= bounds_ref[1]) & (k_start + tile > bounds_ref[0]))
    def _():
        k_raw = k_ref[...].reshape(tile, LANES)
        v_blk = v_ref[...].reshape(tile, LANES)
        swapped = jnp.dot(k_raw, swap_ref[...], preferred_element_type=jnp.float32)
        k_rot = (
            k_raw.astype(jnp.float32) * cos_ref[...].reshape(tile, LANES)
            + swapped * sin_ref[...].reshape(tile, LANES)
        ).astype(jnp.bfloat16)
        key_idx = k_start + lax.broadcasted_iota(jnp.int32, (q_ref.shape[2], tile), 1)
        allowed = (key_idx <= qi_ref[...]) & (key_idx >= ss_ref[...])
        for a in range(pair):
            scores = (
                lax.dot_general(
                    q_ref[0, a], k_rot, (((1,), (1,)), ((), ())),
                    preferred_element_type=jnp.float32,
                )
                * SCORE_SCALE
            )
            scores = jnp.where(allowed, scores, NEG_FILL)
            m_prev = m_sc[a]
            m_new = jnp.maximum(m_prev, jnp.max(scores, axis=1, keepdims=True))
            weights = jnp.where(allowed, jnp.exp(scores - m_new), 0.0)
            factor = jnp.exp(m_prev - m_new)
            l_sc[a] = l_sc[a] * factor + jnp.sum(weights, axis=1, keepdims=True)
            acc_sc[a] = acc_sc[a] * factor + jnp.dot(
                weights.astype(jnp.bfloat16), v_blk, preferred_element_type=jnp.float32
            )
            m_sc[a] = m_new

    @pl.when(kb == pl.num_programs(1) - 1)
    def _():
        width = LANES // pair
        lane = lax.broadcasted_iota(jnp.int32, acc_sc.shape[1:], 1)
        out = jnp.zeros(acc_sc.shape[1:], jnp.float32)
        for a in range(pair):
            out = jnp.where(lane // width == a, acc_sc[a] / l_sc[a], out)
        o_ref[0] = out.astype(o_ref.dtype)


def flash_attention(q_pad, kv_rows, cos_rows, sin_rows, swap, q_rows, starts, bounds):
    pairs, pair, rows, _ = q_pad.shape
    shards, shard_len, width = kv_rows.shape
    tile = SHARDS_PER_TILE * shard_len
    blocks = shards // SHARDS_PER_TILE
    v_col = width // (2 * LANES)

    def clamp(kb, b_ref):
        first = b_ref[0] // tile
        last = b_ref[1] // tile
        return jnp.minimum(jnp.maximum(kb, first), last)

    grid_spec = pltpu.PrefetchScalarGridSpec(
        num_scalar_prefetch=1,
        grid=(pairs, blocks),
        in_specs=[
            pl.BlockSpec((1, pair, rows, LANES), lambda p, kb, b_ref: (p, 0, 0, 0)),
            pl.BlockSpec(
                (SHARDS_PER_TILE, shard_len, LANES),
                lambda p, kb, b_ref: (clamp(kb, b_ref), 0, p),
            ),
            pl.BlockSpec(
                (SHARDS_PER_TILE, shard_len, LANES),
                lambda p, kb, b_ref: (clamp(kb, b_ref), 0, v_col + p),
            ),
            pl.BlockSpec(
                (SHARDS_PER_TILE, shard_len, LANES),
                lambda p, kb, b_ref: (clamp(kb, b_ref), 0, 0),
            ),
            pl.BlockSpec(
                (SHARDS_PER_TILE, shard_len, LANES),
                lambda p, kb, b_ref: (clamp(kb, b_ref), 0, 0),
            ),
            pl.BlockSpec((LANES, LANES), lambda p, kb, b_ref: (0, 0)),
            pl.BlockSpec((rows, 1), lambda p, kb, b_ref: (0, 0)),
            pl.BlockSpec((rows, 1), lambda p, kb, b_ref: (0, 0)),
        ],
        out_specs=pl.BlockSpec((1, rows, LANES), lambda p, kb, b_ref: (p, 0, 0)),
        scratch_shapes=[
            pltpu.VMEM((pair, rows, 1), jnp.float32),
            pltpu.VMEM((pair, rows, 1), jnp.float32),
            pltpu.VMEM((pair, rows, LANES), jnp.float32),
        ],
    )
    return pl.pallas_call(
        flash_kernel,
        out_shape=jax.ShapeDtypeStruct((pairs, rows, LANES), jnp.bfloat16),
        grid_spec=grid_spec,
    )(bounds, q_pad, kv_rows, kv_rows, cos_rows, sin_rows, swap, q_rows, starts)


def rotation_tables(positions, width):
    half_dim = HD // 2
    inv_freq = ROPE_BASE ** (-(jnp.arange(half_dim, dtype=jnp.float32) * 2.0) / (2.0 * half_dim))
    angles = positions.astype(jnp.float32)[..., None] * inv_freq
    reps = width // half_dim
    cos_val = jnp.tile(jnp.cos(angles), (1,) * positions.ndim + (reps,))
    sin_val = jnp.tile(jnp.sin(angles), (1,) * positions.ndim + (reps,))
    return cos_val, sin_val


def swap_matrix(width):
    src = jnp.arange(width)[:, None]
    dst = jnp.arange(width)[None, :]
    half_dim = HD // 2
    first = (dst % HD) < half_dim
    neg = first & (src == dst + half_dim)
    pos = (~first) & (src == dst - half_dim)
    return (pos.astype(jnp.float32) - neg.astype(jnp.float32)).astype(jnp.bfloat16)


def unit_terms(pieces, gathered):
    gate_part, up_part, down_part = pieces
    contract = (((1,), (1,)), ((), ()))
    gate_act = lax.dot_general(gathered, gate_part, contract, preferred_element_type=jnp.float32)
    up_act = lax.dot_general(gathered, up_part, contract, preferred_element_type=jnp.float32)
    hidden = (jax.nn.silu(gate_act) * up_act).astype(jnp.bfloat16)
    return jnp.dot(hidden, down_part, preferred_element_type=jnp.float32)


def gather_by_shifts(part, axis):
    count = lax.psum(1, axis)
    me = lax.axis_index(axis)
    received = [part]
    for shift in range(1, count):
        pairs = [(src, (src + shift) % count) for src in range(count)]
        received.append(lax.ppermute(part, axis, pairs))
    stacked = jnp.stack(received)
    order = (me - jnp.arange(count, dtype=jnp.int32)) % count
    return jnp.take(stacked, order, axis=0).reshape(-1)


def per_device(
    tokens,
    segment,
    attn_gain,
    w_query,
    w_key,
    w_value,
    q_gain,
    k_gain,
    w_out,
    ffn_gain,
    w_gate,
    w_up,
    w_down,
):
    shard_rows = tokens.shape[0]
    groups = H // KVH
    row_base = lax.axis_index("hid") * shard_rows
    group_seg = gather_by_shifts(segment, "hid")
    positions = lax.dynamic_slice_in_dim(seg_positions(group_seg), row_base, shard_rows)
    query_idx = row_base + jnp.arange(shard_rows, dtype=jnp.int32)
    seg_start = query_idx - positions
    resid = tokens.astype(jnp.float32)
    normed = rms_scale(resid, attn_gain).astype(jnp.bfloat16)
    q_raw = jnp.dot(normed, w_query, preferred_element_type=jnp.float32).reshape(shard_rows, H, HD)
    k_raw = jnp.dot(normed, w_key, preferred_element_type=jnp.float32).reshape(shard_rows, KVH, HD)
    k_normed = rms_scale(k_raw, k_gain)
    values = jnp.dot(normed, w_value, preferred_element_type=jnp.float32).astype(jnp.bfloat16)
    send = jnp.concatenate(
        [k_normed.astype(jnp.bfloat16).reshape(shard_rows, KVH * HD), values], axis=1
    )
    kv_rows = lax.all_gather(send, "hid", axis=0, tiled=False)
    unit_rows = lax.all_gather(
        jnp.concatenate([w_gate, w_up, w_down], axis=1), "hid", axis=0, tiled=True
    )
    width = w_gate.shape[1]
    gate_rows = unit_rows[:, :width]
    up_rows = unit_rows[:, width : 2 * width]
    down_rows = unit_rows[:, 2 * width :]
    queries = rotate(rms_scale(q_raw, q_gain), positions).astype(jnp.bfloat16)
    key_heads = rotate(k_normed, positions).astype(jnp.bfloat16).reshape(shard_rows, KVH * HD)
    kv_cache = jnp.concatenate([key_heads, values], axis=1)
    hid_count = kv_rows.shape[0]
    pair = LANES // HD
    pairs = KVH // pair
    q5 = queries.reshape(shard_rows, pairs, pair, groups, HD).transpose(1, 2, 3, 0, 4)
    q5 = q5.reshape(pairs, pair, groups * shard_rows, 1, HD)
    slot = (jnp.arange(pair)[:, None] == jnp.arange(pair)[None, :]).astype(jnp.bfloat16)
    q_pad = (q5 * slot[None, :, None, :, None]).reshape(pairs, pair, groups * shard_rows, LANES)
    key_pos = seg_positions(group_seg).reshape(hid_count, shard_rows)
    cos_rows, sin_rows = rotation_tables(key_pos, LANES)
    q_rows = jnp.tile(query_idx, groups).reshape(groups * shard_rows, 1)
    starts = jnp.tile(seg_start, groups).reshape(groups * shard_rows, 1)
    bounds = jnp.stack([jnp.min(seg_start), row_base + shard_rows - 1])
    attn_pairs = flash_attention(
        q_pad, kv_rows, cos_rows, sin_rows, swap_matrix(LANES), q_rows, starts, bounds
    )
    attended = (
        attn_pairs.reshape(pairs, groups, shard_rows, pair, HD)
        .transpose(2, 0, 3, 1, 4)
        .reshape(shard_rows, H * HD)
    )
    after_attn = (resid + jnp.dot(attended, w_out, preferred_element_type=jnp.float32)).astype(
        jnp.bfloat16
    )
    after_f32 = lax.optimization_barrier(after_attn).astype(jnp.float32)
    mlp_in = rms_scale(after_f32, ffn_gain).astype(jnp.bfloat16)
    gathered = lax.all_gather(mlp_in, "req", axis=0, tiled=True)
    unit_sum = unit_terms(
        (gate_rows, up_rows, down_rows),
        gathered,
    )
    own_share = lax.psum_scatter(
        unit_sum.astype(jnp.bfloat16), "req", scatter_dimension=0, tiled=True
    ).astype(jnp.float32)
    mixed = (after_f32 + own_share).astype(jnp.bfloat16)
    return (mixed, kv_cache)


def solution(mesh):
    placed = (
        P(("req", "hid"), None),
        P(("req", "hid")),
        P(),
        P(),
        P(),
        P(),
        P(),
        P(),
        P(),
        P(),
        P(("req", "hid"), None),
        P(("req", "hid"), None),
        P(("req", "hid"), None),
    )
    return jax.shard_map(
        per_device,
        mesh=mesh,
        in_specs=placed,
        out_specs=(P(("req", "hid"), None), P(("req", "hid"), None)),
        check_vma=False,
    )
```

```python
import jax
import jax.numpy as jnp
from jax import lax
from jax.experimental import pallas as pl
from jax.experimental.pallas import tpu as pltpu
from jax.sharding import PartitionSpec as P

H = 24
KVH = 8
HD = 64


EPSILON = 1e-05
ROPE_BASE = 1000000.0
NEG_FILL = -1e30
SCORE_SCALE = 0.125


def rms_scale(values, gain):
    mean_sq = jnp.mean(values * values, axis=-1, keepdims=True)
    return values * lax.rsqrt(mean_sq + EPSILON) * gain


def seg_positions(seg_ids):
    indices = jnp.arange(seg_ids.shape[0], dtype=jnp.int32)
    is_first = jnp.concatenate([jnp.ones((1,), bool), seg_ids[1:] != seg_ids[:-1]])
    seg_begin = lax.cummax(jnp.where(is_first, indices, jnp.zeros_like(indices)), axis=0)
    return indices - seg_begin


def rotate(heads, positions):
    half_dim = heads.shape[-1] // 2
    inv_freq = ROPE_BASE ** (-(jnp.arange(half_dim, dtype=jnp.float32) * 2.0) / (2.0 * half_dim))
    angles = positions.astype(jnp.float32)[:, None] * inv_freq[None, :]
    cos_val = jnp.cos(angles)[:, None, :]
    sin_val = jnp.sin(angles)[:, None, :]
    left = heads[..., :half_dim]
    right = heads[..., half_dim:]
    return jnp.concatenate(
        [left * cos_val - right * sin_val, right * cos_val + left * sin_val], axis=-1
    )


SHARDS_PER_TILE = 4
LANES = 128


def flash_kernel(
    bounds_ref, q_ref, k_ref, v_ref, cos_ref, sin_ref, swap_ref, qi_ref, ss_ref, o_ref,
    m_sc, l_sc, acc_sc,
):
    kb = pl.program_id(1)
    pair = q_ref.shape[1]
    tile = k_ref.shape[0] * k_ref.shape[1]
    k_start = kb * tile

    @pl.when(kb == 0)
    def _():
        m_sc[...] = jnp.full(m_sc.shape, NEG_FILL, jnp.float32)
        l_sc[...] = jnp.zeros(l_sc.shape, jnp.float32)
        acc_sc[...] = jnp.zeros(acc_sc.shape, jnp.float32)

    @pl.when((k_start <= bounds_ref[1]) & (k_start + tile > bounds_ref[0]))
    def _():
        k_raw = k_ref[...].reshape(tile, LANES)
        v_blk = v_ref[...].reshape(tile, LANES)
        swapped = jnp.dot(k_raw, swap_ref[...], preferred_element_type=jnp.float32)
        k_rot = (
            k_raw.astype(jnp.float32) * cos_ref[...].reshape(tile, LANES)
            + swapped * sin_ref[...].reshape(tile, LANES)
        ).astype(jnp.bfloat16)
        key_idx = k_start + lax.broadcasted_iota(jnp.int32, (q_ref.shape[2], tile), 1)
        allowed = (key_idx <= qi_ref[...]) & (key_idx >= ss_ref[...])
        for a in range(pair):
            scores = (
                lax.dot_general(
                    q_ref[0, a], k_rot, (((1,), (1,)), ((), ())),
                    preferred_element_type=jnp.float32,
                )
                * SCORE_SCALE
            )
            scores = jnp.where(allowed, scores, NEG_FILL)
            m_prev = m_sc[a]
            m_new = jnp.maximum(m_prev, jnp.max(scores, axis=1, keepdims=True))
            weights = jnp.where(allowed, jnp.exp(scores - m_new), 0.0)
            factor = jnp.exp(m_prev - m_new)
            l_sc[a] = l_sc[a] * factor + jnp.sum(weights, axis=1, keepdims=True)
            acc_sc[a] = acc_sc[a] * factor + jnp.dot(
                weights.astype(jnp.bfloat16), v_blk, preferred_element_type=jnp.float32
            )
            m_sc[a] = m_new

    @pl.when(kb == pl.num_programs(1) - 1)
    def _():
        width = LANES // pair
        lane = lax.broadcasted_iota(jnp.int32, acc_sc.shape[1:], 1)
        out = jnp.zeros(acc_sc.shape[1:], jnp.float32)
        for a in range(pair):
            out = jnp.where(lane // width == a, acc_sc[a] / l_sc[a], out)
        o_ref[0] = out.astype(o_ref.dtype)


def flash_attention(q_pad, kv_rows, shard_len, cos_rows, sin_rows, swap, q_rows, starts, bounds):
    pairs, pair, rows, _ = q_pad.shape
    shards, _, width = kv_rows.shape
    tile = SHARDS_PER_TILE * shard_len
    blocks = shards // SHARDS_PER_TILE
    v_col = width // (2 * LANES)

    def clamp(kb, b_ref):
        first = b_ref[0] // tile
        last = b_ref[1] // tile
        return jnp.minimum(jnp.maximum(kb, first), last)

    grid_spec = pltpu.PrefetchScalarGridSpec(
        num_scalar_prefetch=1,
        grid=(pairs, blocks),
        in_specs=[
            pl.BlockSpec((1, pair, rows, LANES), lambda p, kb, b_ref: (p, 0, 0, 0)),
            pl.BlockSpec(
                (SHARDS_PER_TILE, shard_len, LANES),
                lambda p, kb, b_ref: (clamp(kb, b_ref), 0, p),
            ),
            pl.BlockSpec(
                (SHARDS_PER_TILE, shard_len, LANES),
                lambda p, kb, b_ref: (clamp(kb, b_ref), 0, v_col + p),
            ),
            pl.BlockSpec(
                (SHARDS_PER_TILE, shard_len, LANES),
                lambda p, kb, b_ref: (clamp(kb, b_ref), 0, 0),
            ),
            pl.BlockSpec(
                (SHARDS_PER_TILE, shard_len, LANES),
                lambda p, kb, b_ref: (clamp(kb, b_ref), 0, 0),
            ),
            pl.BlockSpec((LANES, LANES), lambda p, kb, b_ref: (0, 0)),
            pl.BlockSpec((rows, 1), lambda p, kb, b_ref: (0, 0)),
            pl.BlockSpec((rows, 1), lambda p, kb, b_ref: (0, 0)),
        ],
        out_specs=pl.BlockSpec((1, rows, LANES), lambda p, kb, b_ref: (p, 0, 0)),
        scratch_shapes=[
            pltpu.VMEM((pair, rows, 1), jnp.float32),
            pltpu.VMEM((pair, rows, 1), jnp.float32),
            pltpu.VMEM((pair, rows, LANES), jnp.float32),
        ],
    )
    return pl.pallas_call(
        flash_kernel,
        out_shape=jax.ShapeDtypeStruct((pairs, rows, LANES), jnp.bfloat16),
        grid_spec=grid_spec,
    )(bounds, q_pad, kv_rows, kv_rows, cos_rows, sin_rows, swap, q_rows, starts)


def rotation_tables(positions, width):
    half_dim = HD // 2
    inv_freq = ROPE_BASE ** (-(jnp.arange(half_dim, dtype=jnp.float32) * 2.0) / (2.0 * half_dim))
    angles = positions.astype(jnp.float32)[..., None] * inv_freq
    reps = width // half_dim
    cos_val = jnp.tile(jnp.cos(angles), (1,) * positions.ndim + (reps,))
    sin_val = jnp.tile(jnp.sin(angles), (1,) * positions.ndim + (reps,))
    return cos_val, sin_val


def swap_matrix(width):
    src = jnp.arange(width)[:, None]
    dst = jnp.arange(width)[None, :]
    half_dim = HD // 2
    first = (dst % HD) < half_dim
    neg = first & (src == dst + half_dim)
    pos = (~first) & (src == dst - half_dim)
    return (pos.astype(jnp.float32) - neg.astype(jnp.float32)).astype(jnp.bfloat16)


def unit_terms(pieces, gathered):
    gate_part, up_part, down_part = pieces
    contract = (((1,), (1,)), ((), ()))
    gate_act = lax.dot_general(gathered, gate_part, contract, preferred_element_type=jnp.float32)
    up_act = lax.dot_general(gathered, up_part, contract, preferred_element_type=jnp.float32)
    hidden = (jax.nn.silu(gate_act) * up_act).astype(jnp.bfloat16)
    return jnp.dot(hidden, down_part, preferred_element_type=jnp.float32)


def gather_by_shifts(part, axis):
    count = lax.psum(1, axis)
    me = lax.axis_index(axis)
    received = [part]
    for shift in range(1, count):
        pairs = [(src, (src + shift) % count) for src in range(count)]
        received.append(lax.ppermute(part, axis, pairs))
    stacked = jnp.stack(received)
    order = (me - jnp.arange(count, dtype=jnp.int32)) % count
    return jnp.take(stacked, order, axis=0).reshape(-1)


def per_device(
    tokens,
    segment,
    attn_gain,
    w_query,
    w_key,
    w_value,
    q_gain,
    k_gain,
    w_out,
    ffn_gain,
    w_gate,
    w_up,
    w_down,
):
    shard_rows = tokens.shape[0]
    groups = H // KVH
    row_base = lax.axis_index("hid") * shard_rows
    group_seg = gather_by_shifts(segment, "hid")
    positions = lax.dynamic_slice_in_dim(seg_positions(group_seg), row_base, shard_rows)
    query_idx = row_base + jnp.arange(shard_rows, dtype=jnp.int32)
    seg_start = query_idx - positions
    resid = tokens.astype(jnp.float32)
    normed = rms_scale(resid, attn_gain).astype(jnp.bfloat16)
    q_raw = jnp.dot(normed, w_query, preferred_element_type=jnp.float32).reshape(shard_rows, H, HD)
    k_raw = jnp.dot(normed, w_key, preferred_element_type=jnp.float32).reshape(shard_rows, KVH, HD)
    k_normed = rms_scale(k_raw, k_gain)
    values = jnp.dot(normed, w_value, preferred_element_type=jnp.float32).astype(jnp.bfloat16)
    send = jnp.concatenate(
        [k_normed.astype(jnp.bfloat16).reshape(shard_rows, KVH * HD), values], axis=1
    )
    unit_local = jnp.concatenate([w_gate, w_up, w_down], axis=1)
    kv_rows = lax.all_gather(
        jnp.concatenate([send, unit_local.reshape(-1, send.shape[1])], axis=0),
        "hid", axis=0, tiled=False,
    )
    unit_rows = kv_rows[:, shard_rows:].reshape(-1, unit_local.shape[1])
    width = w_gate.shape[1]
    gate_rows = unit_rows[:, :width]
    up_rows = unit_rows[:, width : 2 * width]
    down_rows = unit_rows[:, 2 * width :]
    queries = rotate(rms_scale(q_raw, q_gain), positions).astype(jnp.bfloat16)
    key_heads = rotate(k_normed, positions).astype(jnp.bfloat16).reshape(shard_rows, KVH * HD)
    kv_cache = jnp.concatenate([key_heads, values], axis=1)
    hid_count = kv_rows.shape[0]
    pair = LANES // HD
    pairs = KVH // pair
    q5 = queries.reshape(shard_rows, pairs, pair, groups, HD).transpose(1, 2, 3, 0, 4)
    q5 = q5.reshape(pairs, pair, groups * shard_rows, 1, HD)
    slot = (jnp.arange(pair)[:, None] == jnp.arange(pair)[None, :]).astype(jnp.bfloat16)
    q_pad = (q5 * slot[None, :, None, :, None]).reshape(pairs, pair, groups * shard_rows, LANES)
    key_pos = seg_positions(group_seg).reshape(hid_count, shard_rows)
    cos_rows, sin_rows = rotation_tables(key_pos, LANES)
    q_rows = jnp.tile(query_idx, groups).reshape(groups * shard_rows, 1)
    starts = jnp.tile(seg_start, groups).reshape(groups * shard_rows, 1)
    bounds = jnp.stack([jnp.min(seg_start), row_base + shard_rows - 1])
    attn_pairs = flash_attention(
        q_pad, kv_rows, shard_rows, cos_rows, sin_rows, swap_matrix(LANES), q_rows, starts, bounds
    )
    attended = (
        attn_pairs.reshape(pairs, groups, shard_rows, pair, HD)
        .transpose(2, 0, 3, 1, 4)
        .reshape(shard_rows, H * HD)
    )
    after_attn = (resid + jnp.dot(attended, w_out, preferred_element_type=jnp.float32)).astype(
        jnp.bfloat16
    )
    after_f32 = lax.optimization_barrier(after_attn).astype(jnp.float32)
    mlp_in = rms_scale(after_f32, ffn_gain).astype(jnp.bfloat16)
    gathered = lax.all_gather(mlp_in, "req", axis=0, tiled=True)
    unit_sum = unit_terms(
        (gate_rows, up_rows, down_rows),
        gathered,
    )
    own_share = lax.psum_scatter(
        unit_sum.astype(jnp.bfloat16), "req", scatter_dimension=0, tiled=True
    ).astype(jnp.float32)
    mixed = (after_f32 + own_share).astype(jnp.bfloat16)
    return (mixed, kv_cache)


def solution(mesh):
    placed = (
        P(("req", "hid"), None),
        P(("req", "hid")),
        P(),
        P(),
        P(),
        P(),
        P(),
        P(),
        P(),
        P(),
        P(("req", "hid"), None),
        P(("req", "hid"), None),
        P(("req", "hid"), None),
    )
    return jax.shard_map(
        per_device,
        mesh=mesh,
        in_specs=placed,
        out_specs=(P(("req", "hid"), None), P(("req", "hid"), None)),
        check_vma=False,
    )
```

```python
import jax
import jax.numpy as jnp
from jax import lax
from jax.experimental import pallas as pl
from jax.experimental.pallas import tpu as pltpu
from jax.sharding import PartitionSpec as P

H = 24
KVH = 8
HD = 64


EPSILON = 1e-05
ROPE_BASE = 1000000.0
NEG_FILL = -1e30
SCORE_SCALE = 0.125


def rms_scale(values, gain):
    mean_sq = jnp.mean(values * values, axis=-1, keepdims=True)
    return values * lax.rsqrt(mean_sq + EPSILON) * gain


def seg_positions(seg_ids):
    indices = jnp.arange(seg_ids.shape[0], dtype=jnp.int32)
    is_first = jnp.concatenate([jnp.ones((1,), bool), seg_ids[1:] != seg_ids[:-1]])
    seg_begin = lax.cummax(jnp.where(is_first, indices, jnp.zeros_like(indices)), axis=0)
    return indices - seg_begin


def rotate(heads, positions):
    half_dim = heads.shape[-1] // 2
    inv_freq = ROPE_BASE ** (-(jnp.arange(half_dim, dtype=jnp.float32) * 2.0) / (2.0 * half_dim))
    angles = positions.astype(jnp.float32)[:, None] * inv_freq[None, :]
    cos_val = jnp.cos(angles)[:, None, :]
    sin_val = jnp.sin(angles)[:, None, :]
    left = heads[..., :half_dim]
    right = heads[..., half_dim:]
    return jnp.concatenate(
        [left * cos_val - right * sin_val, right * cos_val + left * sin_val], axis=-1
    )


SHARDS_PER_TILE = 4
LANES = 128


def flash_kernel(
    bounds_ref, q_ref, k_ref, v_ref, cos_ref, sin_ref, swap_ref, qi_ref, ss_ref, o_ref,
    m_sc, l_sc, acc_sc,
):
    kb = pl.program_id(1)
    pair = q_ref.shape[1]
    tile = k_ref.shape[0] * k_ref.shape[1]
    k_start = kb * tile

    @pl.when(kb == 0)
    def _():
        m_sc[...] = jnp.full(m_sc.shape, NEG_FILL, jnp.float32)
        l_sc[...] = jnp.zeros(l_sc.shape, jnp.float32)
        acc_sc[...] = jnp.zeros(acc_sc.shape, jnp.float32)

    needed = (k_start <= bounds_ref[1]) & (k_start + tile > bounds_ref[0])
    open_tile = (k_start + tile - 1 <= bounds_ref[2]) & (k_start >= bounds_ref[3])

    def rotated_keys():
        k_raw = k_ref[...].reshape(tile, LANES)
        swapped = jnp.dot(k_raw, swap_ref[...], preferred_element_type=jnp.float32)
        return (
            k_raw.astype(jnp.float32) * cos_ref[...].reshape(tile, LANES)
            + swapped * sin_ref[...].reshape(tile, LANES)
        ).astype(jnp.bfloat16)

    def update(a, k_rot, v_blk, allowed):
        scores = lax.dot_general(
            q_ref[0, a], k_rot, (((1,), (1,)), ((), ())), preferred_element_type=jnp.float32
        )
        if allowed is not None:
            scores = jnp.where(allowed, scores, NEG_FILL)
        m_prev = m_sc[a]
        m_new = jnp.maximum(m_prev, jnp.max(scores, axis=1, keepdims=True))
        weights = jnp.exp(scores - m_new)
        if allowed is not None:
            weights = jnp.where(allowed, weights, 0.0)
        factor = jnp.exp(m_prev - m_new)
        l_sc[a] = l_sc[a] * factor + jnp.sum(weights, axis=1, keepdims=True)
        acc_sc[a] = acc_sc[a] * factor + jnp.dot(
            weights.astype(jnp.bfloat16), v_blk, preferred_element_type=jnp.float32
        )
        m_sc[a] = m_new

    @pl.when(needed & open_tile)
    def _():
        k_rot = rotated_keys()
        v_blk = v_ref[...].reshape(tile, LANES)
        for a in range(pair):
            update(a, k_rot, v_blk, None)

    @pl.when(needed & jnp.logical_not(open_tile))
    def _():
        k_rot = rotated_keys()
        v_blk = v_ref[...].reshape(tile, LANES)
        key_idx = k_start + lax.broadcasted_iota(jnp.int32, (q_ref.shape[2], tile), 1)
        allowed = (key_idx <= qi_ref[...]) & (key_idx >= ss_ref[...])
        for a in range(pair):
            update(a, k_rot, v_blk, allowed)

    @pl.when(kb == pl.num_programs(1) - 1)
    def _():
        width = LANES // pair
        lane = lax.broadcasted_iota(jnp.int32, acc_sc.shape[1:], 1)
        out = jnp.zeros(acc_sc.shape[1:], jnp.float32)
        for a in range(pair):
            out = jnp.where(lane // width == a, acc_sc[a] / l_sc[a], out)
        o_ref[0] = out.astype(o_ref.dtype)


def flash_attention(q_pad, kv_rows, shard_len, cos_rows, sin_rows, swap, q_rows, starts, bounds):
    pairs, pair, rows, _ = q_pad.shape
    shards, _, width = kv_rows.shape
    tile = SHARDS_PER_TILE * shard_len
    blocks = shards // SHARDS_PER_TILE
    v_col = width // (2 * LANES)

    def clamp(kb, b_ref):
        first = b_ref[0] // tile
        last = b_ref[1] // tile
        return jnp.minimum(jnp.maximum(kb, first), last)

    grid_spec = pltpu.PrefetchScalarGridSpec(
        num_scalar_prefetch=1,
        grid=(pairs, blocks),
        in_specs=[
            pl.BlockSpec((1, pair, rows, LANES), lambda p, kb, b_ref: (p, 0, 0, 0)),
            pl.BlockSpec(
                (SHARDS_PER_TILE, shard_len, LANES),
                lambda p, kb, b_ref: (clamp(kb, b_ref), 0, p),
            ),
            pl.BlockSpec(
                (SHARDS_PER_TILE, shard_len, LANES),
                lambda p, kb, b_ref: (clamp(kb, b_ref), 0, v_col + p),
            ),
            pl.BlockSpec(
                (SHARDS_PER_TILE, shard_len, LANES),
                lambda p, kb, b_ref: (clamp(kb, b_ref), 0, 0),
            ),
            pl.BlockSpec(
                (SHARDS_PER_TILE, shard_len, LANES),
                lambda p, kb, b_ref: (clamp(kb, b_ref), 0, 0),
            ),
            pl.BlockSpec((LANES, LANES), lambda p, kb, b_ref: (0, 0)),
            pl.BlockSpec((rows, 1), lambda p, kb, b_ref: (0, 0)),
            pl.BlockSpec((rows, 1), lambda p, kb, b_ref: (0, 0)),
        ],
        out_specs=pl.BlockSpec((1, rows, LANES), lambda p, kb, b_ref: (p, 0, 0)),
        scratch_shapes=[
            pltpu.VMEM((pair, rows, 1), jnp.float32),
            pltpu.VMEM((pair, rows, 1), jnp.float32),
            pltpu.VMEM((pair, rows, LANES), jnp.float32),
        ],
    )
    return pl.pallas_call(
        flash_kernel,
        out_shape=jax.ShapeDtypeStruct((pairs, rows, LANES), jnp.bfloat16),
        grid_spec=grid_spec,
    )(bounds, q_pad, kv_rows, kv_rows, cos_rows, sin_rows, swap, q_rows, starts)


def rotation_tables(positions, width):
    half_dim = HD // 2
    inv_freq = ROPE_BASE ** (-(jnp.arange(half_dim, dtype=jnp.float32) * 2.0) / (2.0 * half_dim))
    angles = positions.astype(jnp.float32)[..., None] * inv_freq
    reps = width // half_dim
    cos_val = jnp.tile(jnp.cos(angles), (1,) * positions.ndim + (reps,))
    sin_val = jnp.tile(jnp.sin(angles), (1,) * positions.ndim + (reps,))
    return cos_val, sin_val


def swap_matrix(width):
    src = jnp.arange(width)[:, None]
    dst = jnp.arange(width)[None, :]
    half_dim = HD // 2
    first = (dst % HD) < half_dim
    neg = first & (src == dst + half_dim)
    pos = (~first) & (src == dst - half_dim)
    return (pos.astype(jnp.float32) - neg.astype(jnp.float32)).astype(jnp.bfloat16)


def unit_terms(pieces, gathered):
    gate_part, up_part, down_part = pieces
    contract = (((1,), (1,)), ((), ()))
    gate_act = lax.dot_general(gathered, gate_part, contract, preferred_element_type=jnp.float32)
    up_act = lax.dot_general(gathered, up_part, contract, preferred_element_type=jnp.float32)
    hidden = (jax.nn.silu(gate_act) * up_act).astype(jnp.bfloat16)
    return jnp.dot(hidden, down_part, preferred_element_type=jnp.float32)


def gather_by_shifts(part, axis):
    count = lax.psum(1, axis)
    me = lax.axis_index(axis)
    received = [part]
    for shift in range(1, count):
        pairs = [(src, (src + shift) % count) for src in range(count)]
        received.append(lax.ppermute(part, axis, pairs))
    stacked = jnp.stack(received)
    order = (me - jnp.arange(count, dtype=jnp.int32)) % count
    return jnp.take(stacked, order, axis=0).reshape(-1)


def per_device(
    tokens,
    segment,
    attn_gain,
    w_query,
    w_key,
    w_value,
    q_gain,
    k_gain,
    w_out,
    ffn_gain,
    w_gate,
    w_up,
    w_down,
):
    shard_rows = tokens.shape[0]
    groups = H // KVH
    row_base = lax.axis_index("hid") * shard_rows
    group_seg = gather_by_shifts(segment, "hid")
    positions = lax.dynamic_slice_in_dim(seg_positions(group_seg), row_base, shard_rows)
    query_idx = row_base + jnp.arange(shard_rows, dtype=jnp.int32)
    seg_start = query_idx - positions
    resid = tokens.astype(jnp.float32)
    normed = rms_scale(resid, attn_gain).astype(jnp.bfloat16)
    q_raw = jnp.dot(normed, w_query, preferred_element_type=jnp.float32).reshape(shard_rows, H, HD)
    k_raw = jnp.dot(normed, w_key, preferred_element_type=jnp.float32).reshape(shard_rows, KVH, HD)
    k_normed = rms_scale(k_raw, k_gain)
    values = jnp.dot(normed, w_value, preferred_element_type=jnp.float32).astype(jnp.bfloat16)
    send = jnp.concatenate(
        [k_normed.astype(jnp.bfloat16).reshape(shard_rows, KVH * HD), values], axis=1
    )
    unit_local = jnp.concatenate([w_gate, w_up, w_down], axis=1)
    kv_rows = lax.all_gather(
        jnp.concatenate([send, unit_local.reshape(-1, send.shape[1])], axis=0),
        "hid", axis=0, tiled=False,
    )
    unit_rows = kv_rows[:, shard_rows:].reshape(-1, unit_local.shape[1])
    width = w_gate.shape[1]
    gate_rows = unit_rows[:, :width]
    up_rows = unit_rows[:, width : 2 * width]
    down_rows = unit_rows[:, 2 * width :]
    queries = rotate(rms_scale(q_raw, q_gain), positions).astype(jnp.bfloat16)
    key_heads = rotate(k_normed, positions).astype(jnp.bfloat16).reshape(shard_rows, KVH * HD)
    kv_cache = jnp.concatenate([key_heads, values], axis=1)
    hid_count = kv_rows.shape[0]
    pair = LANES // HD
    pairs = KVH // pair
    q5 = queries.reshape(shard_rows, pairs, pair, groups, HD).transpose(1, 2, 3, 0, 4)
    q5 = q5.reshape(pairs, pair, groups * shard_rows, 1, HD)
    slot = (jnp.arange(pair)[:, None] == jnp.arange(pair)[None, :]) * SCORE_SCALE
    slot = slot.astype(jnp.bfloat16)
    q_pad = (q5 * slot[None, :, None, :, None]).reshape(pairs, pair, groups * shard_rows, LANES)
    key_pos = seg_positions(group_seg).reshape(hid_count, shard_rows)
    cos_rows, sin_rows = rotation_tables(key_pos, LANES)
    q_rows = jnp.tile(query_idx, groups).reshape(groups * shard_rows, 1)
    starts = jnp.tile(seg_start, groups).reshape(groups * shard_rows, 1)
    bounds = jnp.stack(
        [jnp.min(seg_start), row_base + shard_rows - 1, row_base, jnp.max(seg_start)]
    )
    attn_pairs = flash_attention(
        q_pad, kv_rows, shard_rows, cos_rows, sin_rows, swap_matrix(LANES), q_rows, starts, bounds
    )
    attended = (
        attn_pairs.reshape(pairs, groups, shard_rows, pair, HD)
        .transpose(2, 0, 3, 1, 4)
        .reshape(shard_rows, H * HD)
    )
    after_attn = (resid + jnp.dot(attended, w_out, preferred_element_type=jnp.float32)).astype(
        jnp.bfloat16
    )
    after_f32 = lax.optimization_barrier(after_attn).astype(jnp.float32)
    mlp_in = rms_scale(after_f32, ffn_gain).astype(jnp.bfloat16)
    gathered = lax.all_gather(mlp_in, "req", axis=0, tiled=True)
    unit_sum = unit_terms(
        (gate_rows, up_rows, down_rows),
        gathered,
    )
    own_share = lax.psum_scatter(
        unit_sum.astype(jnp.bfloat16), "req", scatter_dimension=0, tiled=True
    ).astype(jnp.float32)
    mixed = (after_f32 + own_share).astype(jnp.bfloat16)
    return (mixed, kv_cache)


def solution(mesh):
    placed = (
        P(("req", "hid"), None),
        P(("req", "hid")),
        P(),
        P(),
        P(),
        P(),
        P(),
        P(),
        P(),
        P(),
        P(("req", "hid"), None),
        P(("req", "hid"), None),
        P(("req", "hid"), None),
    )
    return jax.shard_map(
        per_device,
        mesh=mesh,
        in_specs=placed,
        out_specs=(P(("req", "hid"), None), P(("req", "hid"), None)),
        check_vma=False,
    )
```

```python
import jax
import jax.numpy as jnp
from jax import lax
from jax.experimental import pallas as pl
from jax.experimental.pallas import tpu as pltpu
from jax.sharding import PartitionSpec as P

H = 24
KVH = 8
HD = 64


EPSILON = 1e-05
ROPE_BASE = 1000000.0
NEG_FILL = -1e30
SCORE_SCALE = 0.125


def rms_scale(values, gain):
    mean_sq = jnp.mean(values * values, axis=-1, keepdims=True)
    return values * lax.rsqrt(mean_sq + EPSILON) * gain


def seg_positions(seg_ids):
    indices = jnp.arange(seg_ids.shape[0], dtype=jnp.int32)
    is_first = jnp.concatenate([jnp.ones((1,), bool), seg_ids[1:] != seg_ids[:-1]])
    seg_begin = lax.cummax(jnp.where(is_first, indices, jnp.zeros_like(indices)), axis=0)
    return indices - seg_begin


def rotate(heads, positions):
    half_dim = heads.shape[-1] // 2
    inv_freq = ROPE_BASE ** (-(jnp.arange(half_dim, dtype=jnp.float32) * 2.0) / (2.0 * half_dim))
    angles = positions.astype(jnp.float32)[:, None] * inv_freq[None, :]
    cos_val = jnp.cos(angles)[:, None, :]
    sin_val = jnp.sin(angles)[:, None, :]
    left = heads[..., :half_dim]
    right = heads[..., half_dim:]
    return jnp.concatenate(
        [left * cos_val - right * sin_val, right * cos_val + left * sin_val], axis=-1
    )


SHARDS_PER_TILE = 4
LANES = 128


def flash_kernel(
    bounds_ref, q_ref, k_ref, v_ref, cos_ref, sin_ref, swap_ref, qi_ref, ss_ref, o_ref,
    m_sc, l_sc, acc_sc,
):
    kb = pl.program_id(1)
    pair = q_ref.shape[1]
    tile = k_ref.shape[0] * k_ref.shape[1]
    k_start = kb * tile

    @pl.when(kb == 0)
    def _():
        m_sc[...] = jnp.full(m_sc.shape, NEG_FILL, jnp.float32)
        l_sc[...] = jnp.zeros(l_sc.shape, jnp.float32)
        acc_sc[...] = jnp.zeros(acc_sc.shape, jnp.float32)

    needed = (k_start <= bounds_ref[1]) & (k_start + tile > bounds_ref[0])
    open_tile = (k_start + tile - 1 <= bounds_ref[2]) & (k_start >= bounds_ref[3])

    def rotated_keys():
        k_raw = k_ref[...].reshape(tile, LANES)
        swapped = jnp.dot(k_raw, swap_ref[...], preferred_element_type=jnp.float32)
        return (
            k_raw.astype(jnp.float32) * cos_ref[...].reshape(tile, LANES)
            + swapped * sin_ref[...].reshape(tile, LANES)
        ).astype(jnp.bfloat16)

    def update(a, k_rot, v_blk, allowed):
        scores = lax.dot_general(
            q_ref[0, a], k_rot, (((1,), (1,)), ((), ())), preferred_element_type=jnp.float32
        )
        if allowed is not None:
            scores = jnp.where(allowed, scores, NEG_FILL)
        m_prev = m_sc[a]
        m_new = jnp.maximum(m_prev, jnp.max(scores, axis=1, keepdims=True))
        weights = jnp.exp(scores - m_new)
        if allowed is not None:
            weights = jnp.where(allowed, weights, 0.0)
        factor = jnp.exp(m_prev - m_new)
        l_sc[a] = l_sc[a] * factor + jnp.sum(weights, axis=1, keepdims=True)
        acc_sc[a] = acc_sc[a] * factor + jnp.dot(
            weights.astype(jnp.bfloat16), v_blk, preferred_element_type=jnp.float32
        )
        m_sc[a] = m_new

    @pl.when(needed & open_tile)
    def _():
        k_rot = rotated_keys()
        v_blk = v_ref[...].reshape(tile, LANES)
        for a in range(pair):
            update(a, k_rot, v_blk, None)

    @pl.when(needed & jnp.logical_not(open_tile))
    def _():
        k_rot = rotated_keys()
        v_blk = v_ref[...].reshape(tile, LANES)
        key_idx = k_start + lax.broadcasted_iota(jnp.int32, (q_ref.shape[2], tile), 1)
        allowed = (key_idx <= qi_ref[...]) & (key_idx >= ss_ref[...])
        for a in range(pair):
            update(a, k_rot, v_blk, allowed)

    @pl.when(kb == pl.num_programs(1) - 1)
    def _():
        width = LANES // pair
        lane = lax.broadcasted_iota(jnp.int32, acc_sc.shape[1:], 1)
        out = jnp.zeros(acc_sc.shape[1:], jnp.float32)
        for a in range(pair):
            out = jnp.where(lane // width == a, acc_sc[a] / l_sc[a], out)
        o_ref[0] = out.astype(o_ref.dtype)


def flash_attention(q_pad, kv_rows, shard_len, cos_rows, sin_rows, swap, q_rows, starts, bounds):
    pairs, pair, rows, _ = q_pad.shape
    shards, _, width = kv_rows.shape
    tile = SHARDS_PER_TILE * shard_len
    blocks = shards // SHARDS_PER_TILE
    v_col = width // (2 * LANES)

    def clamp(kb, b_ref):
        first = b_ref[0] // tile
        last = b_ref[1] // tile
        return jnp.minimum(jnp.maximum(kb, first), last)

    grid_spec = pltpu.PrefetchScalarGridSpec(
        num_scalar_prefetch=1,
        grid=(pairs, blocks),
        in_specs=[
            pl.BlockSpec((1, pair, rows, LANES), lambda p, kb, b_ref: (p, 0, 0, 0)),
            pl.BlockSpec(
                (SHARDS_PER_TILE, shard_len, LANES),
                lambda p, kb, b_ref: (clamp(kb, b_ref), 0, p),
            ),
            pl.BlockSpec(
                (SHARDS_PER_TILE, shard_len, LANES),
                lambda p, kb, b_ref: (clamp(kb, b_ref), 0, v_col + p),
            ),
            pl.BlockSpec(
                (SHARDS_PER_TILE, shard_len, LANES),
                lambda p, kb, b_ref: (clamp(kb, b_ref), 0, 0),
            ),
            pl.BlockSpec(
                (SHARDS_PER_TILE, shard_len, LANES),
                lambda p, kb, b_ref: (clamp(kb, b_ref), 0, 0),
            ),
            pl.BlockSpec((LANES, LANES), lambda p, kb, b_ref: (0, 0)),
            pl.BlockSpec((rows, 1), lambda p, kb, b_ref: (0, 0)),
            pl.BlockSpec((rows, 1), lambda p, kb, b_ref: (0, 0)),
        ],
        out_specs=pl.BlockSpec((1, rows, LANES), lambda p, kb, b_ref: (p, 0, 0)),
        scratch_shapes=[
            pltpu.VMEM((pair, rows, 1), jnp.float32),
            pltpu.VMEM((pair, rows, 1), jnp.float32),
            pltpu.VMEM((pair, rows, LANES), jnp.float32),
        ],
    )
    return pl.pallas_call(
        flash_kernel,
        out_shape=jax.ShapeDtypeStruct((pairs, rows, LANES), jnp.bfloat16),
        grid_spec=grid_spec,
    )(bounds, q_pad, kv_rows, kv_rows, cos_rows, sin_rows, swap, q_rows, starts)


def rotation_tables(positions, width):
    half_dim = HD // 2
    inv_freq = ROPE_BASE ** (-(jnp.arange(half_dim, dtype=jnp.float32) * 2.0) / (2.0 * half_dim))
    angles = positions.astype(jnp.float32)[..., None] * inv_freq
    reps = width // half_dim
    cos_val = jnp.tile(jnp.cos(angles), (1,) * positions.ndim + (reps,))
    sin_val = jnp.tile(jnp.sin(angles), (1,) * positions.ndim + (reps,))
    return cos_val, sin_val


def swap_matrix(width):
    src = jnp.arange(width)[:, None]
    dst = jnp.arange(width)[None, :]
    half_dim = HD // 2
    first = (dst % HD) < half_dim
    neg = first & (src == dst + half_dim)
    pos = (~first) & (src == dst - half_dim)
    return (pos.astype(jnp.float32) - neg.astype(jnp.float32)).astype(jnp.bfloat16)


def unit_terms(pieces, gathered):
    gate_part, up_part, down_part = pieces
    contract = (((1,), (1,)), ((), ()))
    gate_act = lax.dot_general(gathered, gate_part, contract, preferred_element_type=jnp.float32)
    up_act = lax.dot_general(gathered, up_part, contract, preferred_element_type=jnp.float32)
    hidden = lax.optimization_barrier((jax.nn.silu(gate_act) * up_act).astype(jnp.bfloat16))
    return jnp.dot(hidden, down_part, preferred_element_type=jnp.float32)


def gather_by_shifts(part, axis):
    count = lax.psum(1, axis)
    me = lax.axis_index(axis)
    received = [part]
    for shift in range(1, count):
        pairs = [(src, (src + shift) % count) for src in range(count)]
        received.append(lax.ppermute(part, axis, pairs))
    stacked = jnp.stack(received)
    order = (me - jnp.arange(count, dtype=jnp.int32)) % count
    return jnp.take(stacked, order, axis=0).reshape(-1)


def per_device(
    tokens,
    segment,
    attn_gain,
    w_query,
    w_key,
    w_value,
    q_gain,
    k_gain,
    w_out,
    ffn_gain,
    w_gate,
    w_up,
    w_down,
):
    shard_rows = tokens.shape[0]
    groups = H // KVH
    row_base = lax.axis_index("hid") * shard_rows
    group_seg = gather_by_shifts(segment, "hid")
    positions = lax.dynamic_slice_in_dim(seg_positions(group_seg), row_base, shard_rows)
    query_idx = row_base + jnp.arange(shard_rows, dtype=jnp.int32)
    seg_start = query_idx - positions
    resid = tokens.astype(jnp.float32)
    normed = rms_scale(resid, attn_gain).astype(jnp.bfloat16)
    q_raw = jnp.dot(normed, w_query, preferred_element_type=jnp.float32).reshape(shard_rows, H, HD)
    k_raw = jnp.dot(normed, w_key, preferred_element_type=jnp.float32).reshape(shard_rows, KVH, HD)
    k_normed = rms_scale(k_raw, k_gain)
    values = jnp.dot(normed, w_value, preferred_element_type=jnp.float32).astype(jnp.bfloat16)
    send = jnp.concatenate(
        [k_normed.astype(jnp.bfloat16).reshape(shard_rows, KVH * HD), values], axis=1
    )
    unit_local = jnp.concatenate([w_gate, w_up, w_down], axis=1)
    kv_rows = lax.all_gather(
        jnp.concatenate([send, unit_local.reshape(-1, send.shape[1])], axis=0),
        "hid", axis=0, tiled=False,
    )
    unit_rows = kv_rows[:, shard_rows:].reshape(-1, unit_local.shape[1])
    width = w_gate.shape[1]
    gate_rows = unit_rows[:, :width]
    up_rows = unit_rows[:, width : 2 * width]
    down_rows = unit_rows[:, 2 * width :]
    queries = rotate(rms_scale(q_raw, q_gain), positions).astype(jnp.bfloat16)
    key_heads = rotate(k_normed, positions).astype(jnp.bfloat16).reshape(shard_rows, KVH * HD)
    kv_cache = jnp.concatenate([key_heads, values], axis=1)
    hid_count = kv_rows.shape[0]
    pair = LANES // HD
    pairs = KVH // pair
    q5 = queries.reshape(shard_rows, pairs, pair, groups, HD).transpose(1, 2, 3, 0, 4)
    q5 = q5.reshape(pairs, pair, groups * shard_rows, 1, HD)
    slot = (jnp.arange(pair)[:, None] == jnp.arange(pair)[None, :]) * SCORE_SCALE
    slot = slot.astype(jnp.bfloat16)
    q_pad = (q5 * slot[None, :, None, :, None]).reshape(pairs, pair, groups * shard_rows, LANES)
    key_pos = seg_positions(group_seg).reshape(hid_count, shard_rows)
    cos_rows, sin_rows = rotation_tables(key_pos, LANES)
    q_rows = jnp.tile(query_idx, groups).reshape(groups * shard_rows, 1)
    starts = jnp.tile(seg_start, groups).reshape(groups * shard_rows, 1)
    bounds = jnp.stack(
        [jnp.min(seg_start), row_base + shard_rows - 1, row_base, jnp.max(seg_start)]
    )
    attn_pairs = flash_attention(
        q_pad, kv_rows, shard_rows, cos_rows, sin_rows, swap_matrix(LANES), q_rows, starts, bounds
    )
    attended = (
        attn_pairs.reshape(pairs, groups, shard_rows, pair, HD)
        .transpose(2, 0, 3, 1, 4)
        .reshape(shard_rows, H * HD)
    )
    after_attn = (resid + jnp.dot(attended, w_out, preferred_element_type=jnp.float32)).astype(
        jnp.bfloat16
    )
    after_f32 = lax.optimization_barrier(after_attn).astype(jnp.float32)
    mlp_in = rms_scale(after_f32, ffn_gain).astype(jnp.bfloat16)
    gathered = lax.all_gather(mlp_in, "req", axis=0, tiled=True)
    unit_sum = unit_terms(
        (gate_rows, up_rows, down_rows),
        gathered,
    )
    own_share = lax.psum_scatter(
        unit_sum.astype(jnp.bfloat16), "req", scatter_dimension=0, tiled=True
    ).astype(jnp.float32)
    mixed = (after_f32 + own_share).astype(jnp.bfloat16)
    return (mixed, kv_cache)


def solution(mesh):
    placed = (
        P(("req", "hid"), None),
        P(("req", "hid")),
        P(),
        P(),
        P(),
        P(),
        P(),
        P(),
        P(),
        P(),
        P(("req", "hid"), None),
        P(("req", "hid"), None),
        P(("req", "hid"), None),
    )
    return jax.shard_map(
        per_device,
        mesh=mesh,
        in_specs=placed,
        out_specs=(P(("req", "hid"), None), P(("req", "hid"), None)),
        check_vma=False,
    )
```

```python
import jax
import jax.numpy as jnp
from jax import lax
from jax.experimental import pallas as pl
from jax.experimental.pallas import tpu as pltpu
from jax.sharding import PartitionSpec as P

H = 24
KVH = 8
HD = 64


EPSILON = 1e-05
ROPE_BASE = 1000000.0
NEG_FILL = -1e30
SCORE_SCALE = 0.125


def rms_scale(values, gain):
    mean_sq = jnp.mean(values * values, axis=-1, keepdims=True)
    return values * lax.rsqrt(mean_sq + EPSILON) * gain


def seg_positions(seg_ids):
    indices = jnp.arange(seg_ids.shape[0], dtype=jnp.int32)
    is_first = jnp.concatenate([jnp.ones((1,), bool), seg_ids[1:] != seg_ids[:-1]])
    seg_begin = lax.cummax(jnp.where(is_first, indices, jnp.zeros_like(indices)), axis=0)
    return indices - seg_begin


def rotate(heads, positions):
    half_dim = heads.shape[-1] // 2
    inv_freq = ROPE_BASE ** (-(jnp.arange(half_dim, dtype=jnp.float32) * 2.0) / (2.0 * half_dim))
    angles = positions.astype(jnp.float32)[:, None] * inv_freq[None, :]
    cos_val = jnp.cos(angles)[:, None, :]
    sin_val = jnp.sin(angles)[:, None, :]
    left = heads[..., :half_dim]
    right = heads[..., half_dim:]
    return jnp.concatenate(
        [left * cos_val - right * sin_val, right * cos_val + left * sin_val], axis=-1
    )


SHARDS_PER_TILE = 8
LANES = 128


def flash_kernel(
    bounds_ref, q_ref, k_ref, v_ref, cos_ref, sin_ref, swap_ref, qi_ref, ss_ref, o_ref,
    m_sc, l_sc, acc_sc,
):
    kb = pl.program_id(1)
    pair = q_ref.shape[1]
    tile = k_ref.shape[0] * k_ref.shape[1]
    k_start = kb * tile

    @pl.when(kb == 0)
    def _():
        m_sc[...] = jnp.full(m_sc.shape, NEG_FILL, jnp.float32)
        l_sc[...] = jnp.zeros(l_sc.shape, jnp.float32)
        acc_sc[...] = jnp.zeros(acc_sc.shape, jnp.float32)

    needed = (k_start <= bounds_ref[1]) & (k_start + tile > bounds_ref[0])
    open_tile = (k_start + tile - 1 <= bounds_ref[2]) & (k_start >= bounds_ref[3])

    def rotated_keys():
        k_raw = k_ref[...].reshape(tile, LANES)
        swapped = jnp.dot(k_raw, swap_ref[...], preferred_element_type=jnp.float32)
        return (
            k_raw.astype(jnp.float32) * cos_ref[...].reshape(tile, LANES)
            + swapped * sin_ref[...].reshape(tile, LANES)
        ).astype(jnp.bfloat16)

    def update(a, k_rot, v_blk, allowed):
        scores = lax.dot_general(
            q_ref[0, a], k_rot, (((1,), (1,)), ((), ())), preferred_element_type=jnp.float32
        )
        if allowed is not None:
            scores = jnp.where(allowed, scores, NEG_FILL)
        m_prev = m_sc[a]
        m_new = jnp.maximum(m_prev, jnp.max(scores, axis=1, keepdims=True))
        weights = jnp.exp(scores - m_new)
        if allowed is not None:
            weights = jnp.where(allowed, weights, 0.0)
        factor = jnp.exp(m_prev - m_new)
        l_sc[a] = l_sc[a] * factor + jnp.sum(weights, axis=1, keepdims=True)
        acc_sc[a] = acc_sc[a] * factor + jnp.dot(
            weights.astype(jnp.bfloat16), v_blk, preferred_element_type=jnp.float32
        )
        m_sc[a] = m_new

    @pl.when(needed & open_tile)
    def _():
        k_rot = rotated_keys()
        v_blk = v_ref[...].reshape(tile, LANES)
        for a in range(pair):
            update(a, k_rot, v_blk, None)

    @pl.when(needed & jnp.logical_not(open_tile))
    def _():
        k_rot = rotated_keys()
        v_blk = v_ref[...].reshape(tile, LANES)
        key_idx = k_start + lax.broadcasted_iota(jnp.int32, (q_ref.shape[2], tile), 1)
        allowed = (key_idx <= qi_ref[...]) & (key_idx >= ss_ref[...])
        for a in range(pair):
            update(a, k_rot, v_blk, allowed)

    @pl.when(kb == pl.num_programs(1) - 1)
    def _():
        width = LANES // pair
        lane = lax.broadcasted_iota(jnp.int32, acc_sc.shape[1:], 1)
        out = jnp.zeros(acc_sc.shape[1:], jnp.float32)
        for a in range(pair):
            out = jnp.where(lane // width == a, acc_sc[a] / l_sc[a], out)
        o_ref[0] = out.astype(o_ref.dtype)


def flash_attention(q_pad, kv_rows, shard_len, cos_rows, sin_rows, swap, q_rows, starts, bounds):
    pairs, pair, rows, _ = q_pad.shape
    shards, _, width = kv_rows.shape
    tile = SHARDS_PER_TILE * shard_len
    blocks = shards // SHARDS_PER_TILE
    v_col = width // (2 * LANES)

    def clamp(kb, b_ref):
        first = b_ref[0] // tile
        last = b_ref[1] // tile
        return jnp.minimum(jnp.maximum(kb, first), last)

    grid_spec = pltpu.PrefetchScalarGridSpec(
        num_scalar_prefetch=1,
        grid=(pairs, blocks),
        in_specs=[
            pl.BlockSpec((1, pair, rows, LANES), lambda p, kb, b_ref: (p, 0, 0, 0)),
            pl.BlockSpec(
                (SHARDS_PER_TILE, shard_len, LANES),
                lambda p, kb, b_ref: (clamp(kb, b_ref), 0, p),
            ),
            pl.BlockSpec(
                (SHARDS_PER_TILE, shard_len, LANES),
                lambda p, kb, b_ref: (clamp(kb, b_ref), 0, v_col + p),
            ),
            pl.BlockSpec(
                (SHARDS_PER_TILE, shard_len, LANES),
                lambda p, kb, b_ref: (clamp(kb, b_ref), 0, 0),
            ),
            pl.BlockSpec(
                (SHARDS_PER_TILE, shard_len, LANES),
                lambda p, kb, b_ref: (clamp(kb, b_ref), 0, 0),
            ),
            pl.BlockSpec((LANES, LANES), lambda p, kb, b_ref: (0, 0)),
            pl.BlockSpec((rows, 1), lambda p, kb, b_ref: (0, 0)),
            pl.BlockSpec((rows, 1), lambda p, kb, b_ref: (0, 0)),
        ],
        out_specs=pl.BlockSpec((1, rows, LANES), lambda p, kb, b_ref: (p, 0, 0)),
        scratch_shapes=[
            pltpu.VMEM((pair, rows, 1), jnp.float32),
            pltpu.VMEM((pair, rows, 1), jnp.float32),
            pltpu.VMEM((pair, rows, LANES), jnp.float32),
        ],
    )
    return pl.pallas_call(
        flash_kernel,
        out_shape=jax.ShapeDtypeStruct((pairs, rows, LANES), jnp.bfloat16),
        grid_spec=grid_spec,
    )(bounds, q_pad, kv_rows, kv_rows, cos_rows, sin_rows, swap, q_rows, starts)


def rotation_tables(positions, width):
    half_dim = HD // 2
    inv_freq = ROPE_BASE ** (-(jnp.arange(half_dim, dtype=jnp.float32) * 2.0) / (2.0 * half_dim))
    angles = positions.astype(jnp.float32)[..., None] * inv_freq
    reps = width // half_dim
    cos_val = jnp.tile(jnp.cos(angles), (1,) * positions.ndim + (reps,))
    sin_val = jnp.tile(jnp.sin(angles), (1,) * positions.ndim + (reps,))
    return cos_val, sin_val


def swap_matrix(width):
    src = jnp.arange(width)[:, None]
    dst = jnp.arange(width)[None, :]
    half_dim = HD // 2
    first = (dst % HD) < half_dim
    neg = first & (src == dst + half_dim)
    pos = (~first) & (src == dst - half_dim)
    return (pos.astype(jnp.float32) - neg.astype(jnp.float32)).astype(jnp.bfloat16)


def unit_terms(pieces, gathered):
    gate_part, up_part, down_part = pieces
    contract = (((1,), (1,)), ((), ()))
    gate_act = lax.dot_general(gathered, gate_part, contract, preferred_element_type=jnp.float32)
    up_act = lax.dot_general(gathered, up_part, contract, preferred_element_type=jnp.float32)
    hidden = lax.optimization_barrier((jax.nn.silu(gate_act) * up_act).astype(jnp.bfloat16))
    return jnp.dot(hidden, down_part, preferred_element_type=jnp.float32)


def gather_by_shifts(part, axis):
    count = lax.psum(1, axis)
    me = lax.axis_index(axis)
    received = [part]
    for shift in range(1, count):
        pairs = [(src, (src + shift) % count) for src in range(count)]
        received.append(lax.ppermute(part, axis, pairs))
    stacked = jnp.stack(received)
    order = (me - jnp.arange(count, dtype=jnp.int32)) % count
    return jnp.take(stacked, order, axis=0).reshape(-1)


def per_device(
    tokens,
    segment,
    attn_gain,
    w_query,
    w_key,
    w_value,
    q_gain,
    k_gain,
    w_out,
    ffn_gain,
    w_gate,
    w_up,
    w_down,
):
    shard_rows = tokens.shape[0]
    groups = H // KVH
    row_base = lax.axis_index("hid") * shard_rows
    group_seg = gather_by_shifts(segment, "hid")
    positions = lax.dynamic_slice_in_dim(seg_positions(group_seg), row_base, shard_rows)
    query_idx = row_base + jnp.arange(shard_rows, dtype=jnp.int32)
    seg_start = query_idx - positions
    resid = tokens.astype(jnp.float32)
    normed = rms_scale(resid, attn_gain).astype(jnp.bfloat16)
    q_raw = jnp.dot(normed, w_query, preferred_element_type=jnp.float32).reshape(shard_rows, H, HD)
    k_raw = jnp.dot(normed, w_key, preferred_element_type=jnp.float32).reshape(shard_rows, KVH, HD)
    k_normed = rms_scale(k_raw, k_gain)
    values = jnp.dot(normed, w_value, preferred_element_type=jnp.float32).astype(jnp.bfloat16)
    send = jnp.concatenate(
        [k_normed.astype(jnp.bfloat16).reshape(shard_rows, KVH * HD), values], axis=1
    )
    unit_local = jnp.concatenate([w_gate, w_up, w_down], axis=1)
    kv_rows = lax.all_gather(
        jnp.concatenate([send, unit_local.reshape(-1, send.shape[1])], axis=0),
        "hid", axis=0, tiled=False,
    )
    unit_rows = kv_rows[:, shard_rows:].reshape(-1, unit_local.shape[1])
    width = w_gate.shape[1]
    gate_rows = unit_rows[:, :width]
    up_rows = unit_rows[:, width : 2 * width]
    down_rows = unit_rows[:, 2 * width :]
    queries = rotate(rms_scale(q_raw, q_gain), positions).astype(jnp.bfloat16)
    key_heads = rotate(k_normed, positions).astype(jnp.bfloat16).reshape(shard_rows, KVH * HD)
    kv_cache = jnp.concatenate([key_heads, values], axis=1)
    hid_count = kv_rows.shape[0]
    pair = LANES // HD
    pairs = KVH // pair
    q5 = queries.reshape(shard_rows, pairs, pair, groups, HD).transpose(1, 2, 3, 0, 4)
    q5 = q5.reshape(pairs, pair, groups * shard_rows, 1, HD)
    slot = (jnp.arange(pair)[:, None] == jnp.arange(pair)[None, :]) * SCORE_SCALE
    slot = slot.astype(jnp.bfloat16)
    q_pad = (q5 * slot[None, :, None, :, None]).reshape(pairs, pair, groups * shard_rows, LANES)
    key_pos = seg_positions(group_seg).reshape(hid_count, shard_rows)
    cos_rows, sin_rows = rotation_tables(key_pos, LANES)
    q_rows = jnp.tile(query_idx, groups).reshape(groups * shard_rows, 1)
    starts = jnp.tile(seg_start, groups).reshape(groups * shard_rows, 1)
    bounds = jnp.stack(
        [jnp.min(seg_start), row_base + shard_rows - 1, row_base, jnp.max(seg_start)]
    )
    attn_pairs = flash_attention(
        q_pad, kv_rows, shard_rows, cos_rows, sin_rows, swap_matrix(LANES), q_rows, starts, bounds
    )
    attended = (
        attn_pairs.reshape(pairs, groups, shard_rows, pair, HD)
        .transpose(2, 0, 3, 1, 4)
        .reshape(shard_rows, H * HD)
    )
    after_attn = (resid + jnp.dot(attended, w_out, preferred_element_type=jnp.float32)).astype(
        jnp.bfloat16
    )
    after_f32 = lax.optimization_barrier(after_attn).astype(jnp.float32)
    mlp_in = rms_scale(after_f32, ffn_gain).astype(jnp.bfloat16)
    gathered = lax.all_gather(mlp_in, "req", axis=0, tiled=True)
    unit_sum = unit_terms(
        (gate_rows, up_rows, down_rows),
        gathered,
    )
    own_share = lax.psum_scatter(
        unit_sum.astype(jnp.bfloat16), "req", scatter_dimension=0, tiled=True
    ).astype(jnp.float32)
    mixed = (after_f32 + own_share).astype(jnp.bfloat16)
    return (mixed, kv_cache)


def solution(mesh):
    placed = (
        P(("req", "hid"), None),
        P(("req", "hid")),
        P(),
        P(),
        P(),
        P(),
        P(),
        P(),
        P(),
        P(),
        P(("req", "hid"), None),
        P(("req", "hid"), None),
        P(("req", "hid"), None),
    )
    return jax.shard_map(
        per_device,
        mesh=mesh,
        in_specs=placed,
        out_specs=(P(("req", "hid"), None), P(("req", "hid"), None)),
        check_vma=False,
    )
```

```python
import jax
import jax.numpy as jnp
from jax import lax
from jax.experimental import pallas as pl
from jax.experimental.pallas import tpu as pltpu
from jax.sharding import PartitionSpec as P

H = 24
KVH = 8
HD = 64


EPSILON = 1e-05
ROPE_BASE = 1000000.0
NEG_FILL = -1e30
SCORE_SCALE = 0.125


def rms_scale(values, gain):
    mean_sq = jnp.mean(values * values, axis=-1, keepdims=True)
    return values * lax.rsqrt(mean_sq + EPSILON) * gain


def seg_positions(seg_ids):
    indices = jnp.arange(seg_ids.shape[0], dtype=jnp.int32)
    is_first = jnp.concatenate([jnp.ones((1,), bool), seg_ids[1:] != seg_ids[:-1]])
    seg_begin = lax.cummax(jnp.where(is_first, indices, jnp.zeros_like(indices)), axis=0)
    return indices - seg_begin


def rotate(heads, positions):
    half_dim = heads.shape[-1] // 2
    inv_freq = ROPE_BASE ** (-(jnp.arange(half_dim, dtype=jnp.float32) * 2.0) / (2.0 * half_dim))
    angles = positions.astype(jnp.float32)[:, None] * inv_freq[None, :]
    cos_val = jnp.cos(angles)[:, None, :]
    sin_val = jnp.sin(angles)[:, None, :]
    left = heads[..., :half_dim]
    right = heads[..., half_dim:]
    return jnp.concatenate(
        [left * cos_val - right * sin_val, right * cos_val + left * sin_val], axis=-1
    )


SHARDS_PER_TILE = 8
LANES = 128


def flash_kernel(
    bounds_ref, q_ref, k_ref, v_ref, cos_ref, sin_ref, swap_ref, qi_ref, ss_ref, o_ref,
    m_sc, l_sc, acc_sc,
):
    kb = pl.program_id(1)
    pair = q_ref.shape[1]
    tile = k_ref.shape[0] * k_ref.shape[1]
    k_start = kb * tile

    @pl.when(kb == 0)
    def _():
        m_sc[...] = jnp.full(m_sc.shape, NEG_FILL, jnp.float32)
        l_sc[...] = jnp.zeros(l_sc.shape, jnp.float32)
        acc_sc[...] = jnp.zeros(acc_sc.shape, jnp.float32)

    needed = (k_start <= bounds_ref[1]) & (k_start + tile > bounds_ref[0])
    open_tile = (k_start + tile - 1 <= bounds_ref[2]) & (k_start >= bounds_ref[3])

    def rotated_keys():
        k_raw = k_ref[...].reshape(tile, LANES)
        swapped = jnp.dot(k_raw, swap_ref[...], preferred_element_type=jnp.float32)
        return (
            k_raw.astype(jnp.float32) * cos_ref[...].reshape(tile, LANES)
            + swapped * sin_ref[...].reshape(tile, LANES)
        ).astype(jnp.bfloat16)

    def update(a, k_rot, v_blk, allowed):
        scores = lax.dot_general(
            q_ref[0, a], k_rot, (((1,), (1,)), ((), ())), preferred_element_type=jnp.float32
        )
        if allowed is not None:
            scores = jnp.where(allowed, scores, NEG_FILL)
        m_prev = m_sc[a]
        m_new = jnp.maximum(m_prev, jnp.max(scores, axis=1, keepdims=True))
        weights = jnp.exp(scores - m_new)
        if allowed is not None:
            weights = jnp.where(allowed, weights, 0.0)
        factor = jnp.exp(m_prev - m_new)
        l_sc[a] = l_sc[a] * factor + jnp.sum(weights, axis=1, keepdims=True)
        acc_sc[a] = acc_sc[a] * factor + jnp.dot(
            weights.astype(jnp.bfloat16), v_blk, preferred_element_type=jnp.float32
        )
        m_sc[a] = m_new

    @pl.when(needed & open_tile)
    def _():
        k_rot = rotated_keys()
        v_blk = v_ref[...].reshape(tile, LANES)
        for a in range(pair):
            update(a, k_rot, v_blk, None)

    @pl.when(needed & jnp.logical_not(open_tile))
    def _():
        k_rot = rotated_keys()
        v_blk = v_ref[...].reshape(tile, LANES)
        key_idx = k_start + lax.broadcasted_iota(jnp.int32, (q_ref.shape[2], tile), 1)
        allowed = (key_idx <= qi_ref[...]) & (key_idx >= ss_ref[...])
        for a in range(pair):
            update(a, k_rot, v_blk, allowed)

    @pl.when(kb == pl.num_programs(1) - 1)
    def _():
        width = LANES // pair
        lane = lax.broadcasted_iota(jnp.int32, acc_sc.shape[1:], 1)
        out = jnp.zeros(acc_sc.shape[1:], jnp.float32)
        for a in range(pair):
            out = jnp.where(lane // width == a, acc_sc[a] / l_sc[a], out)
        o_ref[0] = out.astype(o_ref.dtype)


def flash_attention(q_pad, kv_rows, shard_len, cos_rows, sin_rows, swap, q_rows, starts, bounds):
    pairs, pair, rows, _ = q_pad.shape
    shards, _, width = kv_rows.shape
    tile = SHARDS_PER_TILE * shard_len
    blocks = shards // SHARDS_PER_TILE
    v_col = width // (2 * LANES)

    def clamp(kb, b_ref):
        first = b_ref[0] // tile
        last = b_ref[1] // tile
        return jnp.minimum(jnp.maximum(kb, first), last)

    grid_spec = pltpu.PrefetchScalarGridSpec(
        num_scalar_prefetch=1,
        grid=(pairs, blocks),
        in_specs=[
            pl.BlockSpec((1, pair, rows, LANES), lambda p, kb, b_ref: (p, 0, 0, 0)),
            pl.BlockSpec(
                (SHARDS_PER_TILE, shard_len, LANES),
                lambda p, kb, b_ref: (clamp(kb, b_ref), 0, p),
            ),
            pl.BlockSpec(
                (SHARDS_PER_TILE, shard_len, LANES),
                lambda p, kb, b_ref: (clamp(kb, b_ref), 0, v_col + p),
            ),
            pl.BlockSpec(
                (SHARDS_PER_TILE, shard_len, LANES),
                lambda p, kb, b_ref: (clamp(kb, b_ref), 0, 0),
            ),
            pl.BlockSpec(
                (SHARDS_PER_TILE, shard_len, LANES),
                lambda p, kb, b_ref: (clamp(kb, b_ref), 0, 0),
            ),
            pl.BlockSpec((LANES, LANES), lambda p, kb, b_ref: (0, 0)),
            pl.BlockSpec((rows, 1), lambda p, kb, b_ref: (0, 0)),
            pl.BlockSpec((rows, 1), lambda p, kb, b_ref: (0, 0)),
        ],
        out_specs=pl.BlockSpec((1, rows, LANES), lambda p, kb, b_ref: (p, 0, 0)),
        scratch_shapes=[
            pltpu.VMEM((pair, rows, 1), jnp.float32),
            pltpu.VMEM((pair, rows, 1), jnp.float32),
            pltpu.VMEM((pair, rows, LANES), jnp.float32),
        ],
    )
    return pl.pallas_call(
        flash_kernel,
        out_shape=jax.ShapeDtypeStruct((pairs, rows, LANES), jnp.bfloat16),
        grid_spec=grid_spec,
    )(bounds, q_pad, kv_rows, kv_rows, cos_rows, sin_rows, swap, q_rows, starts)


def rotation_tables(positions, width):
    half_dim = HD // 2
    inv_freq = ROPE_BASE ** (-(jnp.arange(half_dim, dtype=jnp.float32) * 2.0) / (2.0 * half_dim))
    angles = positions.astype(jnp.float32)[..., None] * inv_freq
    reps = width // half_dim
    cos_val = jnp.tile(jnp.cos(angles), (1,) * positions.ndim + (reps,))
    sin_val = jnp.tile(jnp.sin(angles), (1,) * positions.ndim + (reps,))
    return cos_val, sin_val


def swap_matrix(width):
    src = jnp.arange(width)[:, None]
    dst = jnp.arange(width)[None, :]
    half_dim = HD // 2
    first = (dst % HD) < half_dim
    neg = first & (src == dst + half_dim)
    pos = (~first) & (src == dst - half_dim)
    return (pos.astype(jnp.float32) - neg.astype(jnp.float32)).astype(jnp.bfloat16)


def unit_terms(pieces, gathered):
    gate_part, up_part, down_part = pieces
    contract = (((1,), (1,)), ((), ()))
    gate_act = lax.dot_general(gathered, gate_part, contract, preferred_element_type=jnp.float32)
    up_act = lax.dot_general(gathered, up_part, contract, preferred_element_type=jnp.float32)
    hidden = lax.optimization_barrier((jax.nn.silu(gate_act) * up_act).astype(jnp.bfloat16))
    return jnp.dot(hidden, down_part, preferred_element_type=jnp.float32)


def per_device(
    tokens,
    segment,
    attn_gain,
    w_query,
    w_key,
    w_value,
    q_gain,
    k_gain,
    w_out,
    ffn_gain,
    w_gate,
    w_up,
    w_down,
):
    shard_rows = tokens.shape[0]
    groups = H // KVH
    row_base = lax.axis_index("hid") * shard_rows
    resid = tokens.astype(jnp.float32)
    normed = rms_scale(resid, attn_gain).astype(jnp.bfloat16)
    q_raw = jnp.dot(normed, w_query, preferred_element_type=jnp.float32).reshape(shard_rows, H, HD)
    k_raw = jnp.dot(normed, w_key, preferred_element_type=jnp.float32).reshape(shard_rows, KVH, HD)
    k_normed = rms_scale(k_raw, k_gain)
    values = jnp.dot(normed, w_value, preferred_element_type=jnp.float32).astype(jnp.bfloat16)
    send = jnp.concatenate(
        [k_normed.astype(jnp.bfloat16).reshape(shard_rows, KVH * HD), values], axis=1
    )
    seg_row = jnp.zeros((1, send.shape[1]), jnp.bfloat16)
    seg_row = lax.dynamic_update_slice(seg_row, segment.astype(jnp.bfloat16)[None], (0, 0))
    kv_rows = lax.all_gather(
        jnp.concatenate([send, seg_row], axis=0), "hid", axis=0, tiled=False
    )
    group_seg = kv_rows[:, shard_rows, :shard_rows].reshape(-1).astype(jnp.int32)
    group_pos = seg_positions(group_seg)
    positions = lax.dynamic_slice_in_dim(group_pos, row_base, shard_rows)
    query_idx = row_base + jnp.arange(shard_rows, dtype=jnp.int32)
    seg_start = query_idx - positions
    unit_rows = lax.all_gather(
        jnp.concatenate([w_gate, w_up, w_down], axis=1), "hid", axis=0, tiled=True
    )
    width = w_gate.shape[1]
    gate_rows = unit_rows[:, :width]
    up_rows = unit_rows[:, width : 2 * width]
    down_rows = unit_rows[:, 2 * width :]
    queries = rotate(rms_scale(q_raw, q_gain), positions).astype(jnp.bfloat16)
    key_heads = rotate(k_normed, positions).astype(jnp.bfloat16).reshape(shard_rows, KVH * HD)
    kv_cache = jnp.concatenate([key_heads, values], axis=1)
    hid_count = kv_rows.shape[0]
    pair = LANES // HD
    pairs = KVH // pair
    q5 = queries.reshape(shard_rows, pairs, pair, groups, HD).transpose(1, 2, 3, 0, 4)
    q5 = q5.reshape(pairs, pair, groups * shard_rows, 1, HD)
    slot = (jnp.arange(pair)[:, None] == jnp.arange(pair)[None, :]) * SCORE_SCALE
    slot = slot.astype(jnp.bfloat16)
    q_pad = (q5 * slot[None, :, None, :, None]).reshape(pairs, pair, groups * shard_rows, LANES)
    key_pos = group_pos.reshape(hid_count, shard_rows)
    cos_rows, sin_rows = rotation_tables(key_pos, LANES)
    q_rows = jnp.tile(query_idx, groups).reshape(groups * shard_rows, 1)
    starts = jnp.tile(seg_start, groups).reshape(groups * shard_rows, 1)
    bounds = jnp.stack(
        [jnp.min(seg_start), row_base + shard_rows - 1, row_base, jnp.max(seg_start)]
    )
    attn_pairs = flash_attention(
        q_pad, kv_rows, shard_rows, cos_rows, sin_rows, swap_matrix(LANES), q_rows, starts, bounds
    )
    attended = (
        attn_pairs.reshape(pairs, groups, shard_rows, pair, HD)
        .transpose(2, 0, 3, 1, 4)
        .reshape(shard_rows, H * HD)
    )
    after_attn = (resid + jnp.dot(attended, w_out, preferred_element_type=jnp.float32)).astype(
        jnp.bfloat16
    )
    after_f32 = lax.optimization_barrier(after_attn).astype(jnp.float32)
    mlp_in = rms_scale(after_f32, ffn_gain).astype(jnp.bfloat16)
    gathered = lax.all_gather(mlp_in, "req", axis=0, tiled=True)
    unit_sum = unit_terms(
        (gate_rows, up_rows, down_rows),
        gathered,
    )
    own_share = lax.psum_scatter(
        unit_sum.astype(jnp.bfloat16), "req", scatter_dimension=0, tiled=True
    ).astype(jnp.float32)
    mixed = (after_f32 + own_share).astype(jnp.bfloat16)
    return (mixed, kv_cache)


def solution(mesh):
    placed = (
        P(("req", "hid"), None),
        P(("req", "hid")),
        P(),
        P(),
        P(),
        P(),
        P(),
        P(),
        P(),
        P(),
        P(("req", "hid"), None),
        P(("req", "hid"), None),
        P(("req", "hid"), None),
    )
    return jax.shard_map(
        per_device,
        mesh=mesh,
        in_specs=placed,
        out_specs=(P(("req", "hid"), None), P(("req", "hid"), None)),
        check_vma=False,
    )
```

```python
import jax
import jax.numpy as jnp
from jax import lax
from jax.experimental import pallas as pl
from jax.experimental.pallas import tpu as pltpu
from jax.sharding import PartitionSpec as P

H = 24
KVH = 8
HD = 64


EPSILON = 1e-05
ROPE_BASE = 1000000.0
NEG_FILL = -1e30
SCORE_SCALE = 0.125


def rms_scale(values, gain):
    mean_sq = jnp.mean(values * values, axis=-1, keepdims=True)
    return values * lax.rsqrt(mean_sq + EPSILON) * gain


def seg_positions(seg_ids):
    indices = jnp.arange(seg_ids.shape[0], dtype=jnp.int32)
    is_first = jnp.concatenate([jnp.ones((1,), bool), seg_ids[1:] != seg_ids[:-1]])
    seg_begin = lax.cummax(jnp.where(is_first, indices, jnp.zeros_like(indices)), axis=0)
    return indices - seg_begin


def rotate(heads, positions):
    half_dim = heads.shape[-1] // 2
    inv_freq = ROPE_BASE ** (-(jnp.arange(half_dim, dtype=jnp.float32) * 2.0) / (2.0 * half_dim))
    angles = positions.astype(jnp.float32)[:, None] * inv_freq[None, :]
    cos_val = jnp.cos(angles)[:, None, :]
    sin_val = jnp.sin(angles)[:, None, :]
    left = heads[..., :half_dim]
    right = heads[..., half_dim:]
    return jnp.concatenate(
        [left * cos_val - right * sin_val, right * cos_val + left * sin_val], axis=-1
    )


SHARDS_PER_TILE = 8
LANES = 128


def flash_kernel(
    bounds_ref, q_ref, k_ref, v_ref, cos_ref, sin_ref, swap_ref, qi_ref, ss_ref, o_ref,
    m_sc, l_sc, acc_sc,
):
    kb = pl.program_id(1)
    pair = q_ref.shape[1]
    tile = k_ref.shape[0] * k_ref.shape[1]
    k_start = kb * tile

    @pl.when(kb == 0)
    def _():
        m_sc[...] = jnp.full(m_sc.shape, NEG_FILL, jnp.float32)
        l_sc[...] = jnp.zeros(l_sc.shape, jnp.float32)
        acc_sc[...] = jnp.zeros(acc_sc.shape, jnp.float32)

    needed = (k_start <= bounds_ref[1]) & (k_start + tile > bounds_ref[0])
    open_tile = (k_start + tile - 1 <= bounds_ref[2]) & (k_start >= bounds_ref[3])

    def rotated_keys():
        k_raw = k_ref[...].reshape(tile, LANES)
        swapped = jnp.dot(k_raw, swap_ref[...], preferred_element_type=jnp.float32)
        return (
            k_raw.astype(jnp.float32) * cos_ref[...].reshape(tile, LANES)
            + swapped * sin_ref[...].reshape(tile, LANES)
        ).astype(jnp.bfloat16)

    def update(a, k_rot, v_blk, allowed):
        scores = lax.dot_general(
            q_ref[0, a], k_rot, (((1,), (1,)), ((), ())), preferred_element_type=jnp.float32
        )
        if allowed is not None:
            scores = jnp.where(allowed, scores, NEG_FILL)
        m_prev = m_sc[a]
        m_new = jnp.maximum(m_prev, jnp.max(scores, axis=1, keepdims=True))
        weights = jnp.exp(scores - m_new)
        if allowed is not None:
            weights = jnp.where(allowed, weights, 0.0)
        factor = jnp.exp(m_prev - m_new)
        l_sc[a] = l_sc[a] * factor + jnp.sum(weights, axis=1, keepdims=True)
        acc_sc[a] = acc_sc[a] * factor + jnp.dot(
            weights.astype(jnp.bfloat16), v_blk, preferred_element_type=jnp.float32
        )
        m_sc[a] = m_new

    @pl.when(needed & open_tile)
    def _():
        k_rot = rotated_keys()
        v_blk = v_ref[...].reshape(tile, LANES)
        for a in range(pair):
            update(a, k_rot, v_blk, None)

    @pl.when(needed & jnp.logical_not(open_tile))
    def _():
        k_rot = rotated_keys()
        v_blk = v_ref[...].reshape(tile, LANES)
        key_idx = k_start + lax.broadcasted_iota(jnp.int32, (q_ref.shape[2], tile), 1)
        allowed = (key_idx <= qi_ref[...]) & (key_idx >= ss_ref[...])
        for a in range(pair):
            update(a, k_rot, v_blk, allowed)

    @pl.when(kb == pl.num_programs(1) - 1)
    def _():
        width = LANES // pair
        lane = lax.broadcasted_iota(jnp.int32, acc_sc.shape[1:], 1)
        out = jnp.zeros(acc_sc.shape[1:], jnp.float32)
        for a in range(pair):
            out = jnp.where(lane // width == a, acc_sc[a] / l_sc[a], out)
        o_ref[0] = out.astype(o_ref.dtype)


def flash_attention(q_pad, kv_rows, shard_len, cos_rows, sin_rows, swap, q_rows, starts, bounds):
    pairs, pair, rows, _ = q_pad.shape
    shards, _, width = kv_rows.shape
    tile = SHARDS_PER_TILE * shard_len
    blocks = shards // SHARDS_PER_TILE
    v_col = width // (2 * LANES)

    def clamp(kb, b_ref):
        first = b_ref[0] // tile
        last = b_ref[1] // tile
        return jnp.minimum(jnp.maximum(kb, first), last)

    grid_spec = pltpu.PrefetchScalarGridSpec(
        num_scalar_prefetch=1,
        grid=(pairs, blocks),
        in_specs=[
            pl.BlockSpec((1, pair, rows, LANES), lambda p, kb, b_ref: (p, 0, 0, 0)),
            pl.BlockSpec(
                (SHARDS_PER_TILE, shard_len, LANES),
                lambda p, kb, b_ref: (clamp(kb, b_ref), 0, p),
            ),
            pl.BlockSpec(
                (SHARDS_PER_TILE, shard_len, LANES),
                lambda p, kb, b_ref: (clamp(kb, b_ref), 0, v_col + p),
            ),
            pl.BlockSpec(
                (SHARDS_PER_TILE, shard_len, LANES),
                lambda p, kb, b_ref: (clamp(kb, b_ref), 0, 0),
            ),
            pl.BlockSpec(
                (SHARDS_PER_TILE, shard_len, LANES),
                lambda p, kb, b_ref: (clamp(kb, b_ref), 0, 0),
            ),
            pl.BlockSpec((LANES, LANES), lambda p, kb, b_ref: (0, 0)),
            pl.BlockSpec((rows, 1), lambda p, kb, b_ref: (0, 0)),
            pl.BlockSpec((rows, 1), lambda p, kb, b_ref: (0, 0)),
        ],
        out_specs=pl.BlockSpec((1, rows, LANES), lambda p, kb, b_ref: (p, 0, 0)),
        scratch_shapes=[
            pltpu.VMEM((pair, rows, 1), jnp.float32),
            pltpu.VMEM((pair, rows, 1), jnp.float32),
            pltpu.VMEM((pair, rows, LANES), jnp.float32),
        ],
    )
    return pl.pallas_call(
        flash_kernel,
        out_shape=jax.ShapeDtypeStruct((pairs, rows, LANES), jnp.bfloat16),
        grid_spec=grid_spec,
    )(bounds, q_pad, kv_rows, kv_rows, cos_rows, sin_rows, swap, q_rows, starts)


def rotation_tables(positions, width):
    half_dim = HD // 2
    inv_freq = ROPE_BASE ** (-(jnp.arange(half_dim, dtype=jnp.float32) * 2.0) / (2.0 * half_dim))
    angles = positions.astype(jnp.float32)[..., None] * jnp.tile(inv_freq, width // half_dim)
    return jnp.cos(angles), jnp.sin(angles)


def swap_matrix(width):
    src = jnp.arange(width)[:, None]
    dst = jnp.arange(width)[None, :]
    half_dim = HD // 2
    first = (dst % HD) < half_dim
    neg = first & (src == dst + half_dim)
    pos = (~first) & (src == dst - half_dim)
    return (pos.astype(jnp.float32) - neg.astype(jnp.float32)).astype(jnp.bfloat16)


def unit_terms(pieces, gathered):
    gate_part, up_part, down_part = pieces
    contract = (((1,), (1,)), ((), ()))
    gate_act = lax.dot_general(gathered, gate_part, contract, preferred_element_type=jnp.float32)
    up_act = lax.dot_general(gathered, up_part, contract, preferred_element_type=jnp.float32)
    hidden = lax.optimization_barrier((jax.nn.silu(gate_act) * up_act).astype(jnp.bfloat16))
    return jnp.dot(hidden, down_part, preferred_element_type=jnp.float32)


def per_device(
    tokens,
    segment,
    attn_gain,
    w_query,
    w_key,
    w_value,
    q_gain,
    k_gain,
    w_out,
    ffn_gain,
    w_gate,
    w_up,
    w_down,
):
    shard_rows = tokens.shape[0]
    groups = H // KVH
    row_base = lax.axis_index("hid") * shard_rows
    resid = tokens.astype(jnp.float32)
    normed = rms_scale(resid, attn_gain).astype(jnp.bfloat16)
    q_raw = jnp.dot(normed, w_query, preferred_element_type=jnp.float32).reshape(shard_rows, H, HD)
    k_raw = jnp.dot(normed, w_key, preferred_element_type=jnp.float32).reshape(shard_rows, KVH, HD)
    k_normed = rms_scale(k_raw, k_gain)
    values = jnp.dot(normed, w_value, preferred_element_type=jnp.float32).astype(jnp.bfloat16)
    send = jnp.concatenate(
        [k_normed.astype(jnp.bfloat16).reshape(shard_rows, KVH * HD), values], axis=1
    )
    seg_row = jnp.zeros((1, send.shape[1]), jnp.bfloat16)
    seg_row = lax.dynamic_update_slice(seg_row, segment.astype(jnp.bfloat16)[None], (0, 0))
    kv_rows = lax.all_gather(
        jnp.concatenate([send, seg_row], axis=0), "hid", axis=0, tiled=False
    )
    group_seg = kv_rows[:, shard_rows, :shard_rows].reshape(-1).astype(jnp.int32)
    group_pos = seg_positions(group_seg)
    positions = lax.dynamic_slice_in_dim(group_pos, row_base, shard_rows)
    query_idx = row_base + jnp.arange(shard_rows, dtype=jnp.int32)
    seg_start = query_idx - positions
    unit_rows = lax.all_gather(
        jnp.concatenate([w_gate, w_up, w_down], axis=1), "hid", axis=0, tiled=True
    )
    width = w_gate.shape[1]
    gate_rows = unit_rows[:, :width]
    up_rows = unit_rows[:, width : 2 * width]
    down_rows = unit_rows[:, 2 * width :]
    queries = rotate(rms_scale(q_raw, q_gain), positions).astype(jnp.bfloat16)
    key_heads = rotate(k_normed, positions).astype(jnp.bfloat16).reshape(shard_rows, KVH * HD)
    kv_cache = jnp.concatenate([key_heads, values], axis=1)
    hid_count = kv_rows.shape[0]
    pair = LANES // HD
    pairs = KVH // pair
    q5 = queries.reshape(shard_rows, pairs, pair, groups, HD).transpose(1, 2, 3, 0, 4)
    q5 = q5.reshape(pairs, pair, groups * shard_rows, 1, HD)
    slot = (jnp.arange(pair)[:, None] == jnp.arange(pair)[None, :]) * SCORE_SCALE
    slot = slot.astype(jnp.bfloat16)
    q_pad = (q5 * slot[None, :, None, :, None]).reshape(pairs, pair, groups * shard_rows, LANES)
    key_pos = group_pos.reshape(hid_count, shard_rows)
    cos_rows, sin_rows = rotation_tables(key_pos, LANES)
    q_rows = jnp.tile(query_idx, groups).reshape(groups * shard_rows, 1)
    starts = jnp.tile(seg_start, groups).reshape(groups * shard_rows, 1)
    bounds = jnp.stack(
        [jnp.min(seg_start), row_base + shard_rows - 1, row_base, jnp.max(seg_start)]
    )
    attn_pairs = flash_attention(
        q_pad, kv_rows, shard_rows, cos_rows, sin_rows, swap_matrix(LANES), q_rows, starts, bounds
    )
    attended = (
        attn_pairs.reshape(pairs, groups, shard_rows, pair, HD)
        .transpose(2, 0, 3, 1, 4)
        .reshape(shard_rows, H * HD)
    )
    after_attn = (resid + jnp.dot(attended, w_out, preferred_element_type=jnp.float32)).astype(
        jnp.bfloat16
    )
    after_f32 = lax.optimization_barrier(after_attn).astype(jnp.float32)
    mlp_in = rms_scale(after_f32, ffn_gain).astype(jnp.bfloat16)
    gathered = lax.all_gather(mlp_in, "req", axis=0, tiled=True)
    unit_sum = unit_terms(
        (gate_rows, up_rows, down_rows),
        gathered,
    )
    own_share = lax.psum_scatter(
        unit_sum.astype(jnp.bfloat16), "req", scatter_dimension=0, tiled=True
    ).astype(jnp.float32)
    mixed = (after_f32 + own_share).astype(jnp.bfloat16)
    return (mixed, kv_cache)


def solution(mesh):
    placed = (
        P(("req", "hid"), None),
        P(("req", "hid")),
        P(),
        P(),
        P(),
        P(),
        P(),
        P(),
        P(),
        P(),
        P(("req", "hid"), None),
        P(("req", "hid"), None),
        P(("req", "hid"), None),
    )
    return jax.shard_map(
        per_device,
        mesh=mesh,
        in_specs=placed,
        out_specs=(P(("req", "hid"), None), P(("req", "hid"), None)),
        check_vma=False,
    )
```

```python
import jax
import jax.numpy as jnp
from jax import lax
from jax.experimental import pallas as pl
from jax.experimental.pallas import tpu as pltpu
from jax.sharding import PartitionSpec as P

H = 24
KVH = 8
HD = 64


EPSILON = 1e-05
ROPE_BASE = 1000000.0
NEG_FILL = -1e30
SCORE_SCALE = 0.125


def rms_scale(values, gain):
    mean_sq = jnp.mean(values * values, axis=-1, keepdims=True)
    return values * lax.rsqrt(mean_sq + EPSILON) * gain


def seg_positions(seg_ids):
    indices = jnp.arange(seg_ids.shape[0], dtype=jnp.int32)
    is_first = jnp.concatenate([jnp.ones((1,), bool), seg_ids[1:] != seg_ids[:-1]])
    seg_begin = lax.cummax(jnp.where(is_first, indices, jnp.zeros_like(indices)), axis=0)
    return indices - seg_begin


def rotate(heads, positions):
    half_dim = heads.shape[-1] // 2
    inv_freq = ROPE_BASE ** (-(jnp.arange(half_dim, dtype=jnp.float32) * 2.0) / (2.0 * half_dim))
    angles = positions.astype(jnp.float32)[:, None] * inv_freq[None, :]
    cos_val = jnp.cos(angles)[:, None, :]
    sin_val = jnp.sin(angles)[:, None, :]
    left = heads[..., :half_dim]
    right = heads[..., half_dim:]
    return jnp.concatenate(
        [left * cos_val - right * sin_val, right * cos_val + left * sin_val], axis=-1
    )


SHARDS_PER_TILE = 8
LANES = 128


def flash_kernel(
    bounds_ref, q_ref, k_ref, v_ref, cos_ref, sin_ref, swap_ref, qi_ref, ss_ref, o_ref,
    m_sc, l_sc, acc_sc,
):
    kb = pl.program_id(1)
    pair = q_ref.shape[1]
    tile = k_ref.shape[0] * k_ref.shape[1]
    k_start = kb * tile

    @pl.when(kb == 0)
    def _():
        m_sc[...] = jnp.full(m_sc.shape, NEG_FILL, jnp.float32)
        l_sc[...] = jnp.zeros(l_sc.shape, jnp.float32)
        acc_sc[...] = jnp.zeros(acc_sc.shape, jnp.float32)

    needed = (k_start <= bounds_ref[1]) & (k_start + tile > bounds_ref[0])
    open_tile = (k_start + tile - 1 <= bounds_ref[2]) & (k_start >= bounds_ref[3])

    def rotated_keys():
        k_raw = k_ref[...].reshape(tile, LANES)
        swapped = jnp.dot(k_raw, swap_ref[...], preferred_element_type=jnp.float32)
        return (
            k_raw.astype(jnp.float32) * cos_ref[...].reshape(tile, LANES)
            + swapped * sin_ref[...].reshape(tile, LANES)
        ).astype(jnp.bfloat16)

    def update(a, k_rot, v_blk, allowed):
        scores = lax.dot_general(
            q_ref[0, a], k_rot, (((1,), (1,)), ((), ())), preferred_element_type=jnp.float32
        )
        if allowed is not None:
            scores = jnp.where(allowed, scores, NEG_FILL)
        m_prev = m_sc[a]
        m_new = jnp.maximum(m_prev, jnp.max(scores, axis=1, keepdims=True))
        weights = jnp.exp(scores - m_new)
        if allowed is not None:
            weights = jnp.where(allowed, weights, 0.0)
        factor = jnp.exp(m_prev - m_new)
        l_sc[a] = l_sc[a] * factor + jnp.sum(weights, axis=1, keepdims=True)
        acc_sc[a] = acc_sc[a] * factor + jnp.dot(
            weights.astype(jnp.bfloat16), v_blk, preferred_element_type=jnp.float32
        )
        m_sc[a] = m_new

    @pl.when(needed & open_tile)
    def _():
        k_rot = rotated_keys()
        v_blk = v_ref[...].reshape(tile, LANES)
        for a in range(pair):
            update(a, k_rot, v_blk, None)

    @pl.when(needed & jnp.logical_not(open_tile))
    def _():
        k_rot = rotated_keys()
        v_blk = v_ref[...].reshape(tile, LANES)
        key_idx = k_start + lax.broadcasted_iota(jnp.int32, (q_ref.shape[2], tile), 1)
        allowed = (key_idx <= qi_ref[...]) & (key_idx >= ss_ref[...])
        for a in range(pair):
            update(a, k_rot, v_blk, allowed)

    @pl.when(kb == pl.num_programs(1) - 1)
    def _():
        width = LANES // pair
        lane = lax.broadcasted_iota(jnp.int32, acc_sc.shape[1:], 1)
        out = jnp.zeros(acc_sc.shape[1:], jnp.float32)
        for a in range(pair):
            out = jnp.where(lane // width == a, acc_sc[a] / l_sc[a], out)
        o_ref[0] = out.astype(o_ref.dtype)


def flash_attention(q_pad, kv_rows, shard_len, cos_rows, sin_rows, swap, q_rows, starts, bounds):
    pairs, pair, rows, _ = q_pad.shape
    shards, _, width = kv_rows.shape
    tile = SHARDS_PER_TILE * shard_len
    blocks = shards // SHARDS_PER_TILE
    v_col = width // (2 * LANES)

    def clamp(kb, b_ref):
        first = b_ref[0] // tile
        last = b_ref[1] // tile
        return jnp.minimum(jnp.maximum(kb, first), last)

    grid_spec = pltpu.PrefetchScalarGridSpec(
        num_scalar_prefetch=1,
        grid=(pairs, blocks),
        in_specs=[
            pl.BlockSpec((1, pair, rows, LANES), lambda p, kb, b_ref: (p, 0, 0, 0)),
            pl.BlockSpec(
                (SHARDS_PER_TILE, shard_len, LANES),
                lambda p, kb, b_ref: (clamp(kb, b_ref), 0, p),
            ),
            pl.BlockSpec(
                (SHARDS_PER_TILE, shard_len, LANES),
                lambda p, kb, b_ref: (clamp(kb, b_ref), 0, v_col + p),
            ),
            pl.BlockSpec(
                (SHARDS_PER_TILE, shard_len, LANES),
                lambda p, kb, b_ref: (clamp(kb, b_ref), 0, 0),
            ),
            pl.BlockSpec(
                (SHARDS_PER_TILE, shard_len, LANES),
                lambda p, kb, b_ref: (clamp(kb, b_ref), 0, 0),
            ),
            pl.BlockSpec((LANES, LANES), lambda p, kb, b_ref: (0, 0)),
            pl.BlockSpec((rows, 1), lambda p, kb, b_ref: (0, 0)),
            pl.BlockSpec((rows, 1), lambda p, kb, b_ref: (0, 0)),
        ],
        out_specs=pl.BlockSpec((1, rows, LANES), lambda p, kb, b_ref: (p, 0, 0)),
        scratch_shapes=[
            pltpu.VMEM((pair, rows, 1), jnp.float32),
            pltpu.VMEM((pair, rows, 1), jnp.float32),
            pltpu.VMEM((pair, rows, LANES), jnp.float32),
        ],
    )
    return pl.pallas_call(
        flash_kernel,
        out_shape=jax.ShapeDtypeStruct((pairs, rows, LANES), jnp.bfloat16),
        grid_spec=grid_spec,
    )(bounds, q_pad, kv_rows, kv_rows, cos_rows, sin_rows, swap, q_rows, starts)


def rotation_tables(positions, width):
    half_dim = HD // 2
    inv_freq = ROPE_BASE ** (-(jnp.arange(half_dim, dtype=jnp.float32) * 2.0) / (2.0 * half_dim))
    angles = positions.astype(jnp.float32)[..., None] * jnp.tile(inv_freq, width // half_dim)
    return jnp.cos(angles), jnp.sin(angles)


def swap_matrix(width):
    src = jnp.arange(width)[:, None]
    dst = jnp.arange(width)[None, :]
    half_dim = HD // 2
    first = (dst % HD) < half_dim
    neg = first & (src == dst + half_dim)
    pos = (~first) & (src == dst - half_dim)
    return (pos.astype(jnp.float32) - neg.astype(jnp.float32)).astype(jnp.bfloat16)


def unit_terms(pieces, gathered):
    gate_part, up_part, down_part = pieces
    contract = (((1,), (1,)), ((), ()))
    gate_act = lax.dot_general(gathered, gate_part, contract, preferred_element_type=jnp.float32)
    up_act = lax.dot_general(gathered, up_part, contract, preferred_element_type=jnp.float32)
    hidden = lax.optimization_barrier((jax.nn.silu(gate_act) * up_act).astype(jnp.bfloat16))
    return jnp.dot(hidden, down_part, preferred_element_type=jnp.float32)


def per_device(
    tokens,
    segment,
    attn_gain,
    w_query,
    w_key,
    w_value,
    q_gain,
    k_gain,
    w_out,
    ffn_gain,
    w_gate,
    w_up,
    w_down,
):
    shard_rows = tokens.shape[0]
    groups = H // KVH
    row_base = lax.axis_index("hid") * shard_rows
    resid = tokens.astype(jnp.float32)
    normed = rms_scale(resid, attn_gain).astype(jnp.bfloat16)
    q_raw = jnp.dot(normed, w_query, preferred_element_type=jnp.float32).reshape(shard_rows, H, HD)
    k_raw = jnp.dot(normed, w_key, preferred_element_type=jnp.float32).reshape(shard_rows, KVH, HD)
    k_normed = rms_scale(k_raw, k_gain)
    values = jnp.dot(normed, w_value, preferred_element_type=jnp.float32).astype(jnp.bfloat16)
    send = jnp.concatenate(
        [k_normed.astype(jnp.bfloat16).reshape(shard_rows, KVH * HD), values], axis=1
    )
    seg_row = jnp.zeros((1, send.shape[1]), jnp.bfloat16)
    seg_row = lax.dynamic_update_slice(seg_row, segment.astype(jnp.bfloat16)[None], (0, 0))
    kv_rows = lax.all_gather(
        jnp.concatenate([send, seg_row], axis=0), "hid", axis=0, tiled=False
    )
    group_seg = kv_rows[:, shard_rows, :shard_rows].reshape(-1).astype(jnp.int32)
    group_pos = seg_positions(group_seg)
    positions = lax.dynamic_slice_in_dim(group_pos, row_base, shard_rows)
    query_idx = row_base + jnp.arange(shard_rows, dtype=jnp.int32)
    seg_start = query_idx - positions
    unit_rows = lax.all_gather(
        jnp.concatenate([w_gate, w_up, w_down], axis=1), "hid", axis=0, tiled=True
    )
    width = w_gate.shape[1]
    gate_rows = unit_rows[:, :width]
    up_rows = unit_rows[:, width : 2 * width]
    down_rows = unit_rows[:, 2 * width :]
    queries = rotate(rms_scale(q_raw, q_gain), positions).astype(jnp.bfloat16)
    key_heads = rotate(k_normed, positions).astype(jnp.bfloat16).reshape(shard_rows, KVH * HD)
    kv_cache = jnp.concatenate([key_heads, values], axis=1)
    hid_count = kv_rows.shape[0]
    pair = LANES // HD
    pairs = KVH // pair
    q5 = queries.reshape(shard_rows, pairs, pair, groups, HD).transpose(1, 2, 3, 0, 4)
    q5 = q5.reshape(pairs, pair, groups * shard_rows, 1, HD)
    slot = (jnp.arange(pair)[:, None] == jnp.arange(pair)[None, :]) * SCORE_SCALE
    slot = slot.astype(jnp.bfloat16)
    q_pad = (q5 * slot[None, :, None, :, None]).reshape(pairs, pair, groups * shard_rows, LANES)
    cos_all, sin_all = rotation_tables(jnp.arange(group_pos.shape[0], dtype=jnp.int32), LANES)
    cos_rows = jnp.take(cos_all, group_pos, axis=0).reshape(hid_count, shard_rows, LANES)
    sin_rows = jnp.take(sin_all, group_pos, axis=0).reshape(hid_count, shard_rows, LANES)
    q_rows = jnp.tile(query_idx, groups).reshape(groups * shard_rows, 1)
    starts = jnp.tile(seg_start, groups).reshape(groups * shard_rows, 1)
    bounds = jnp.stack(
        [jnp.min(seg_start), row_base + shard_rows - 1, row_base, jnp.max(seg_start)]
    )
    attn_pairs = flash_attention(
        q_pad, kv_rows, shard_rows, cos_rows, sin_rows, swap_matrix(LANES), q_rows, starts, bounds
    )
    attended = (
        attn_pairs.reshape(pairs, groups, shard_rows, pair, HD)
        .transpose(2, 0, 3, 1, 4)
        .reshape(shard_rows, H * HD)
    )
    after_attn = (resid + jnp.dot(attended, w_out, preferred_element_type=jnp.float32)).astype(
        jnp.bfloat16
    )
    after_f32 = lax.optimization_barrier(after_attn).astype(jnp.float32)
    mlp_in = rms_scale(after_f32, ffn_gain).astype(jnp.bfloat16)
    gathered = lax.all_gather(mlp_in, "req", axis=0, tiled=True)
    unit_sum = unit_terms(
        (gate_rows, up_rows, down_rows),
        gathered,
    )
    own_share = lax.psum_scatter(
        unit_sum.astype(jnp.bfloat16), "req", scatter_dimension=0, tiled=True
    ).astype(jnp.float32)
    mixed = (after_f32 + own_share).astype(jnp.bfloat16)
    return (mixed, kv_cache)


def solution(mesh):
    placed = (
        P(("req", "hid"), None),
        P(("req", "hid")),
        P(),
        P(),
        P(),
        P(),
        P(),
        P(),
        P(),
        P(),
        P(("req", "hid"), None),
        P(("req", "hid"), None),
        P(("req", "hid"), None),
    )
    return jax.shard_map(
        per_device,
        mesh=mesh,
        in_specs=placed,
        out_specs=(P(("req", "hid"), None), P(("req", "hid"), None)),
        check_vma=False,
    )
```

```python
import jax
import jax.numpy as jnp
from jax import lax
from jax.experimental import pallas as pl
from jax.experimental.pallas import tpu as pltpu
from jax.sharding import PartitionSpec as P

H = 24
KVH = 8
HD = 64


EPSILON = 1e-05
ROPE_BASE = 1000000.0
NEG_FILL = -1e30
SCORE_SCALE = 0.125


def rms_scale(values, gain):
    mean_sq = jnp.mean(values * values, axis=-1, keepdims=True)
    return values * lax.rsqrt(mean_sq + EPSILON) * gain


def seg_positions(seg_ids):
    indices = jnp.arange(seg_ids.shape[0], dtype=jnp.int32)
    is_first = jnp.concatenate([jnp.ones((1,), bool), seg_ids[1:] != seg_ids[:-1]])
    seg_begin = lax.cummax(jnp.where(is_first, indices, jnp.zeros_like(indices)), axis=0)
    return indices - seg_begin


def rotate(heads, positions):
    half_dim = heads.shape[-1] // 2
    inv_freq = ROPE_BASE ** (-(jnp.arange(half_dim, dtype=jnp.float32) * 2.0) / (2.0 * half_dim))
    angles = positions.astype(jnp.float32)[:, None] * inv_freq[None, :]
    cos_val = jnp.cos(angles)[:, None, :]
    sin_val = jnp.sin(angles)[:, None, :]
    left = heads[..., :half_dim]
    right = heads[..., half_dim:]
    return jnp.concatenate(
        [left * cos_val - right * sin_val, right * cos_val + left * sin_val], axis=-1
    )


SHARDS_PER_TILE = 8
LANES = 128


def flash_kernel(
    bounds_ref, q_ref, k_ref, v_ref, cos_ref, sin_ref, swap_ref, qi_ref, ss_ref, o_ref,
    m_sc, l_sc, acc_sc,
):
    kb = pl.program_id(1)
    pair = q_ref.shape[1]
    tile = k_ref.shape[0] * k_ref.shape[1]
    k_start = kb * tile

    @pl.when(kb == 0)
    def _():
        m_sc[...] = jnp.full(m_sc.shape, 0.5 * NEG_FILL, jnp.float32)
        l_sc[...] = jnp.zeros(l_sc.shape, jnp.float32)
        acc_sc[...] = jnp.zeros(acc_sc.shape, jnp.float32)

    needed = (k_start <= bounds_ref[1]) & (k_start + tile > bounds_ref[0])
    open_tile = (k_start + tile - 1 <= bounds_ref[2]) & (k_start >= bounds_ref[3])

    def rotated_keys():
        k_raw = k_ref[...].reshape(tile, LANES)
        swapped = jnp.dot(k_raw, swap_ref[...], preferred_element_type=jnp.float32)
        return (
            k_raw.astype(jnp.float32) * cos_ref[...].reshape(tile, LANES)
            + swapped * sin_ref[...].reshape(tile, LANES)
        ).astype(jnp.bfloat16)

    def update(a, k_rot, v_blk, allowed):
        scores = lax.dot_general(
            q_ref[0, a], k_rot, (((1,), (1,)), ((), ())), preferred_element_type=jnp.float32
        )
        if allowed is not None:
            scores = jnp.where(allowed, scores, NEG_FILL)
        m_prev = m_sc[a]
        m_new = jnp.maximum(m_prev, jnp.max(scores, axis=1, keepdims=True))
        weights = jnp.exp(scores - m_new)
        factor = jnp.exp(m_prev - m_new)
        width = LANES // pair
        lane = lax.broadcasted_iota(jnp.int32, v_blk.shape, 1)
        v_ext = jnp.where(lane // width == a, v_blk, jnp.ones_like(v_blk))
        prod = jnp.dot(weights.astype(jnp.bfloat16), v_ext, preferred_element_type=jnp.float32)
        other = (1 - a) * width
        l_sc[a] = l_sc[a] * factor + prod[:, other : other + 1]
        acc_sc[a] = acc_sc[a] * factor + prod
        m_sc[a] = m_new

    @pl.when(needed & open_tile)
    def _():
        k_rot = rotated_keys()
        v_blk = v_ref[...].reshape(tile, LANES)
        for a in range(pair):
            update(a, k_rot, v_blk, None)

    @pl.when(needed & jnp.logical_not(open_tile))
    def _():
        k_rot = rotated_keys()
        v_blk = v_ref[...].reshape(tile, LANES)
        key_idx = k_start + lax.broadcasted_iota(jnp.int32, (q_ref.shape[2], tile), 1)
        allowed = (key_idx <= qi_ref[...]) & (key_idx >= ss_ref[...])
        for a in range(pair):
            update(a, k_rot, v_blk, allowed)

    @pl.when(kb == pl.num_programs(1) - 1)
    def _():
        width = LANES // pair
        lane = lax.broadcasted_iota(jnp.int32, acc_sc.shape[1:], 1)
        out = jnp.zeros(acc_sc.shape[1:], jnp.float32)
        for a in range(pair):
            out = jnp.where(lane // width == a, acc_sc[a] / l_sc[a], out)
        o_ref[0] = out.astype(o_ref.dtype)


def flash_attention(q_pad, kv_rows, shard_len, cos_rows, sin_rows, swap, q_rows, starts, bounds):
    pairs, pair, rows, _ = q_pad.shape
    shards, _, width = kv_rows.shape
    tile = SHARDS_PER_TILE * shard_len
    blocks = shards // SHARDS_PER_TILE
    v_col = width // (2 * LANES)

    def clamp(kb, b_ref):
        first = b_ref[0] // tile
        last = b_ref[1] // tile
        return jnp.minimum(jnp.maximum(kb, first), last)

    grid_spec = pltpu.PrefetchScalarGridSpec(
        num_scalar_prefetch=1,
        grid=(pairs, blocks),
        in_specs=[
            pl.BlockSpec((1, pair, rows, LANES), lambda p, kb, b_ref: (p, 0, 0, 0)),
            pl.BlockSpec(
                (SHARDS_PER_TILE, shard_len, LANES),
                lambda p, kb, b_ref: (clamp(kb, b_ref), 0, p),
            ),
            pl.BlockSpec(
                (SHARDS_PER_TILE, shard_len, LANES),
                lambda p, kb, b_ref: (clamp(kb, b_ref), 0, v_col + p),
            ),
            pl.BlockSpec(
                (SHARDS_PER_TILE, shard_len, LANES),
                lambda p, kb, b_ref: (clamp(kb, b_ref), 0, 0),
            ),
            pl.BlockSpec(
                (SHARDS_PER_TILE, shard_len, LANES),
                lambda p, kb, b_ref: (clamp(kb, b_ref), 0, 0),
            ),
            pl.BlockSpec((LANES, LANES), lambda p, kb, b_ref: (0, 0)),
            pl.BlockSpec((rows, 1), lambda p, kb, b_ref: (0, 0)),
            pl.BlockSpec((rows, 1), lambda p, kb, b_ref: (0, 0)),
        ],
        out_specs=pl.BlockSpec((1, rows, LANES), lambda p, kb, b_ref: (p, 0, 0)),
        scratch_shapes=[
            pltpu.VMEM((pair, rows, 1), jnp.float32),
            pltpu.VMEM((pair, rows, 1), jnp.float32),
            pltpu.VMEM((pair, rows, LANES), jnp.float32),
        ],
    )
    return pl.pallas_call(
        flash_kernel,
        out_shape=jax.ShapeDtypeStruct((pairs, rows, LANES), jnp.bfloat16),
        grid_spec=grid_spec,
    )(bounds, q_pad, kv_rows, kv_rows, cos_rows, sin_rows, swap, q_rows, starts)


def rotation_tables(positions, width):
    half_dim = HD // 2
    inv_freq = ROPE_BASE ** (-(jnp.arange(half_dim, dtype=jnp.float32) * 2.0) / (2.0 * half_dim))
    angles = positions.astype(jnp.float32)[..., None] * jnp.tile(inv_freq, width // half_dim)
    return jnp.cos(angles), jnp.sin(angles)


def swap_matrix(width):
    src = jnp.arange(width)[:, None]
    dst = jnp.arange(width)[None, :]
    half_dim = HD // 2
    first = (dst % HD) < half_dim
    neg = first & (src == dst + half_dim)
    pos = (~first) & (src == dst - half_dim)
    return (pos.astype(jnp.float32) - neg.astype(jnp.float32)).astype(jnp.bfloat16)


def unit_terms(pieces, gathered):
    gate_part, up_part, down_part = pieces
    contract = (((1,), (1,)), ((), ()))
    gate_act = lax.dot_general(gathered, gate_part, contract, preferred_element_type=jnp.float32)
    up_act = lax.dot_general(gathered, up_part, contract, preferred_element_type=jnp.float32)
    hidden = lax.optimization_barrier((jax.nn.silu(gate_act) * up_act).astype(jnp.bfloat16))
    return jnp.dot(hidden, down_part, preferred_element_type=jnp.float32)


def per_device(
    tokens,
    segment,
    attn_gain,
    w_query,
    w_key,
    w_value,
    q_gain,
    k_gain,
    w_out,
    ffn_gain,
    w_gate,
    w_up,
    w_down,
):
    shard_rows = tokens.shape[0]
    groups = H // KVH
    row_base = lax.axis_index("hid") * shard_rows
    resid = tokens.astype(jnp.float32)
    normed = rms_scale(resid, attn_gain).astype(jnp.bfloat16)
    q_raw = jnp.dot(normed, w_query, preferred_element_type=jnp.float32).reshape(shard_rows, H, HD)
    k_raw = jnp.dot(normed, w_key, preferred_element_type=jnp.float32).reshape(shard_rows, KVH, HD)
    k_normed = rms_scale(k_raw, k_gain)
    values = jnp.dot(normed, w_value, preferred_element_type=jnp.float32).astype(jnp.bfloat16)
    send = jnp.concatenate(
        [k_normed.astype(jnp.bfloat16).reshape(shard_rows, KVH * HD), values], axis=1
    )
    seg_row = jnp.zeros((1, send.shape[1]), jnp.bfloat16)
    seg_row = lax.dynamic_update_slice(seg_row, segment.astype(jnp.bfloat16)[None], (0, 0))
    kv_rows = lax.all_gather(
        jnp.concatenate([send, seg_row], axis=0), "hid", axis=0, tiled=False
    )
    group_seg = kv_rows[:, shard_rows, :shard_rows].reshape(-1).astype(jnp.int32)
    group_pos = seg_positions(group_seg)
    positions = lax.dynamic_slice_in_dim(group_pos, row_base, shard_rows)
    query_idx = row_base + jnp.arange(shard_rows, dtype=jnp.int32)
    seg_start = query_idx - positions
    unit_rows = lax.all_gather(
        jnp.concatenate([w_gate, w_up, w_down], axis=1), "hid", axis=0, tiled=True
    )
    width = w_gate.shape[1]
    gate_rows = unit_rows[:, :width]
    up_rows = unit_rows[:, width : 2 * width]
    down_rows = unit_rows[:, 2 * width :]
    queries = rotate(rms_scale(q_raw, q_gain), positions).astype(jnp.bfloat16)
    key_heads = rotate(k_normed, positions).astype(jnp.bfloat16).reshape(shard_rows, KVH * HD)
    kv_cache = jnp.concatenate([key_heads, values], axis=1)
    hid_count = kv_rows.shape[0]
    pair = LANES // HD
    pairs = KVH // pair
    q5 = queries.reshape(shard_rows, pairs, pair, groups, HD).transpose(1, 2, 3, 0, 4)
    q5 = q5.reshape(pairs, pair, groups * shard_rows, 1, HD)
    slot = (jnp.arange(pair)[:, None] == jnp.arange(pair)[None, :]) * SCORE_SCALE
    slot = slot.astype(jnp.bfloat16)
    q_pad = (q5 * slot[None, :, None, :, None]).reshape(pairs, pair, groups * shard_rows, LANES)
    key_pos = group_pos.reshape(hid_count, shard_rows)
    cos_rows, sin_rows = rotation_tables(key_pos, LANES)
    q_rows = jnp.tile(query_idx, groups).reshape(groups * shard_rows, 1)
    starts = jnp.tile(seg_start, groups).reshape(groups * shard_rows, 1)
    bounds = jnp.stack(
        [jnp.min(seg_start), row_base + shard_rows - 1, row_base, jnp.max(seg_start)]
    )
    attn_pairs = flash_attention(
        q_pad, kv_rows, shard_rows, cos_rows, sin_rows, swap_matrix(LANES), q_rows, starts, bounds
    )
    attended = (
        attn_pairs.reshape(pairs, groups, shard_rows, pair, HD)
        .transpose(2, 0, 3, 1, 4)
        .reshape(shard_rows, H * HD)
    )
    after_attn = (resid + jnp.dot(attended, w_out, preferred_element_type=jnp.float32)).astype(
        jnp.bfloat16
    )
    after_f32 = lax.optimization_barrier(after_attn).astype(jnp.float32)
    mlp_in = rms_scale(after_f32, ffn_gain).astype(jnp.bfloat16)
    gathered = lax.all_gather(mlp_in, "req", axis=0, tiled=True)
    unit_sum = unit_terms(
        (gate_rows, up_rows, down_rows),
        gathered,
    )
    own_share = lax.psum_scatter(
        unit_sum.astype(jnp.bfloat16), "req", scatter_dimension=0, tiled=True
    ).astype(jnp.float32)
    mixed = (after_f32 + own_share).astype(jnp.bfloat16)
    return (mixed, kv_cache)


def solution(mesh):
    placed = (
        P(("req", "hid"), None),
        P(("req", "hid")),
        P(),
        P(),
        P(),
        P(),
        P(),
        P(),
        P(),
        P(),
        P(("req", "hid"), None),
        P(("req", "hid"), None),
        P(("req", "hid"), None),
    )
    return jax.shard_map(
        per_device,
        mesh=mesh,
        in_specs=placed,
        out_specs=(P(("req", "hid"), None), P(("req", "hid"), None)),
        check_vma=False,
    )
```

```python
import jax
import jax.numpy as jnp
from jax import lax
from jax.experimental import pallas as pl
from jax.experimental.pallas import tpu as pltpu
from jax.sharding import PartitionSpec as P

H = 24
KVH = 8
HD = 64


EPSILON = 1e-05
ROPE_BASE = 1000000.0
NEG_FILL = -1e30
SCORE_SCALE = 0.125


def rms_scale(values, gain):
    mean_sq = jnp.mean(values * values, axis=-1, keepdims=True)
    return values * lax.rsqrt(mean_sq + EPSILON) * gain


def seg_positions(seg_ids):
    indices = jnp.arange(seg_ids.shape[0], dtype=jnp.int32)
    is_first = jnp.concatenate([jnp.ones((1,), bool), seg_ids[1:] != seg_ids[:-1]])
    seg_begin = lax.cummax(jnp.where(is_first, indices, jnp.zeros_like(indices)), axis=0)
    return indices - seg_begin


def rotate(heads, positions):
    half_dim = heads.shape[-1] // 2
    inv_freq = ROPE_BASE ** (-(jnp.arange(half_dim, dtype=jnp.float32) * 2.0) / (2.0 * half_dim))
    angles = positions.astype(jnp.float32)[:, None] * inv_freq[None, :]
    cos_val = jnp.cos(angles)[:, None, :]
    sin_val = jnp.sin(angles)[:, None, :]
    left = heads[..., :half_dim]
    right = heads[..., half_dim:]
    return jnp.concatenate(
        [left * cos_val - right * sin_val, right * cos_val + left * sin_val], axis=-1
    )


SHARDS_PER_TILE = 8
LANES = 128


def flash_kernel(
    bounds_ref, q_ref, k_ref, v_ref, cos_ref, sin_ref, swap_ref, qi_ref, ss_ref, o_ref,
    m_sc, l_sc, acc_sc,
):
    kb = pl.program_id(1)
    pair = q_ref.shape[1]
    tile = k_ref.shape[0] * k_ref.shape[1]
    k_start = kb * tile

    @pl.when(kb == 0)
    def _():
        m_sc[...] = jnp.full(m_sc.shape, 0.5 * NEG_FILL, jnp.float32)
        l_sc[...] = jnp.zeros(l_sc.shape, jnp.float32)
        acc_sc[...] = jnp.zeros(acc_sc.shape, jnp.float32)

    needed = (k_start <= bounds_ref[1]) & (k_start + tile > bounds_ref[0])
    open_tile = (k_start + tile - 1 <= bounds_ref[2]) & (k_start >= bounds_ref[3])

    def rotated_keys():
        k_raw = k_ref[...].reshape(tile, LANES)
        swapped = jnp.dot(k_raw, swap_ref[...], preferred_element_type=jnp.float32)
        cos_half = cos_ref[...].reshape(tile, HD)
        sin_half = sin_ref[...].reshape(tile, HD)
        reps = LANES // HD
        return (
            k_raw.astype(jnp.float32) * jnp.concatenate([cos_half] * reps, axis=1)
            + swapped * jnp.concatenate([sin_half] * reps, axis=1)
        ).astype(jnp.bfloat16)

    def update(a, k_rot, v_blk, allowed):
        scores = lax.dot_general(
            q_ref[0, a], k_rot, (((1,), (1,)), ((), ())), preferred_element_type=jnp.float32
        )
        if allowed is not None:
            scores = jnp.where(allowed, scores, NEG_FILL)
        m_prev = m_sc[a]
        m_new = jnp.maximum(m_prev, jnp.max(scores, axis=1, keepdims=True))
        weights = jnp.exp(scores - m_new)
        factor = jnp.exp(m_prev - m_new)
        width = LANES // pair
        lane = lax.broadcasted_iota(jnp.int32, v_blk.shape, 1)
        v_ext = jnp.where(lane // width == a, v_blk, jnp.ones_like(v_blk))
        prod = jnp.dot(weights.astype(jnp.bfloat16), v_ext, preferred_element_type=jnp.float32)
        other = (1 - a) * width
        l_sc[a] = l_sc[a] * factor + prod[:, other : other + 1]
        acc_sc[a] = acc_sc[a] * factor + prod
        m_sc[a] = m_new

    @pl.when(needed & open_tile)
    def _():
        k_rot = rotated_keys()
        v_blk = v_ref[...].reshape(tile, LANES)
        for a in range(pair):
            update(a, k_rot, v_blk, None)

    @pl.when(needed & jnp.logical_not(open_tile))
    def _():
        k_rot = rotated_keys()
        v_blk = v_ref[...].reshape(tile, LANES)
        key_idx = k_start + lax.broadcasted_iota(jnp.int32, (q_ref.shape[2], tile), 1)
        allowed = (key_idx <= qi_ref[...]) & (key_idx >= ss_ref[...])
        for a in range(pair):
            update(a, k_rot, v_blk, allowed)

    @pl.when(kb == pl.num_programs(1) - 1)
    def _():
        width = LANES // pair
        lane = lax.broadcasted_iota(jnp.int32, acc_sc.shape[1:], 1)
        out = jnp.zeros(acc_sc.shape[1:], jnp.float32)
        for a in range(pair):
            out = jnp.where(lane // width == a, acc_sc[a] / l_sc[a], out)
        o_ref[0] = out.astype(o_ref.dtype)


def flash_attention(q_pad, kv_rows, shard_len, cos_rows, sin_rows, swap, q_rows, starts, bounds):
    pairs, pair, rows, _ = q_pad.shape
    shards, _, width = kv_rows.shape
    tile = SHARDS_PER_TILE * shard_len
    blocks = shards // SHARDS_PER_TILE
    v_col = width // (2 * LANES)

    def clamp(kb, b_ref):
        first = b_ref[0] // tile
        last = b_ref[1] // tile
        return jnp.minimum(jnp.maximum(kb, first), last)

    grid_spec = pltpu.PrefetchScalarGridSpec(
        num_scalar_prefetch=1,
        grid=(pairs, blocks),
        in_specs=[
            pl.BlockSpec((1, pair, rows, LANES), lambda p, kb, b_ref: (p, 0, 0, 0)),
            pl.BlockSpec(
                (SHARDS_PER_TILE, shard_len, LANES),
                lambda p, kb, b_ref: (clamp(kb, b_ref), 0, p),
            ),
            pl.BlockSpec(
                (SHARDS_PER_TILE, shard_len, LANES),
                lambda p, kb, b_ref: (clamp(kb, b_ref), 0, v_col + p),
            ),
            pl.BlockSpec(
                (SHARDS_PER_TILE, shard_len, HD),
                lambda p, kb, b_ref: (clamp(kb, b_ref), 0, 0),
            ),
            pl.BlockSpec(
                (SHARDS_PER_TILE, shard_len, HD),
                lambda p, kb, b_ref: (clamp(kb, b_ref), 0, 0),
            ),
            pl.BlockSpec((LANES, LANES), lambda p, kb, b_ref: (0, 0)),
            pl.BlockSpec((rows, 1), lambda p, kb, b_ref: (0, 0)),
            pl.BlockSpec((rows, 1), lambda p, kb, b_ref: (0, 0)),
        ],
        out_specs=pl.BlockSpec((1, rows, LANES), lambda p, kb, b_ref: (p, 0, 0)),
        scratch_shapes=[
            pltpu.VMEM((pair, rows, 1), jnp.float32),
            pltpu.VMEM((pair, rows, 1), jnp.float32),
            pltpu.VMEM((pair, rows, LANES), jnp.float32),
        ],
    )
    return pl.pallas_call(
        flash_kernel,
        out_shape=jax.ShapeDtypeStruct((pairs, rows, LANES), jnp.bfloat16),
        grid_spec=grid_spec,
    )(bounds, q_pad, kv_rows, kv_rows, cos_rows, sin_rows, swap, q_rows, starts)


def rotation_tables(positions, width):
    half_dim = HD // 2
    inv_freq = ROPE_BASE ** (-(jnp.arange(half_dim, dtype=jnp.float32) * 2.0) / (2.0 * half_dim))
    angles = positions.astype(jnp.float32)[..., None] * jnp.tile(inv_freq, width // half_dim)
    return jnp.cos(angles), jnp.sin(angles)


def swap_matrix(width):
    src = jnp.arange(width)[:, None]
    dst = jnp.arange(width)[None, :]
    half_dim = HD // 2
    first = (dst % HD) < half_dim
    neg = first & (src == dst + half_dim)
    pos = (~first) & (src == dst - half_dim)
    return (pos.astype(jnp.float32) - neg.astype(jnp.float32)).astype(jnp.bfloat16)


def unit_terms(pieces, gathered):
    gate_part, up_part, down_part = pieces
    contract = (((1,), (1,)), ((), ()))
    gate_act = lax.dot_general(gathered, gate_part, contract, preferred_element_type=jnp.float32)
    up_act = lax.dot_general(gathered, up_part, contract, preferred_element_type=jnp.float32)
    hidden = lax.optimization_barrier((jax.nn.silu(gate_act) * up_act).astype(jnp.bfloat16))
    return jnp.dot(hidden, down_part, preferred_element_type=jnp.float32)


def per_device(
    tokens,
    segment,
    attn_gain,
    w_query,
    w_key,
    w_value,
    q_gain,
    k_gain,
    w_out,
    ffn_gain,
    w_gate,
    w_up,
    w_down,
):
    shard_rows = tokens.shape[0]
    groups = H // KVH
    row_base = lax.axis_index("hid") * shard_rows
    resid = tokens.astype(jnp.float32)
    normed = rms_scale(resid, attn_gain).astype(jnp.bfloat16)
    q_raw = jnp.dot(normed, w_query, preferred_element_type=jnp.float32).reshape(shard_rows, H, HD)
    k_raw = jnp.dot(normed, w_key, preferred_element_type=jnp.float32).reshape(shard_rows, KVH, HD)
    k_normed = rms_scale(k_raw, k_gain)
    values = jnp.dot(normed, w_value, preferred_element_type=jnp.float32).astype(jnp.bfloat16)
    send = jnp.concatenate(
        [k_normed.astype(jnp.bfloat16).reshape(shard_rows, KVH * HD), values], axis=1
    )
    seg_row = jnp.zeros((1, send.shape[1]), jnp.bfloat16)
    seg_row = lax.dynamic_update_slice(seg_row, segment.astype(jnp.bfloat16)[None], (0, 0))
    kv_rows = lax.all_gather(
        jnp.concatenate([send, seg_row], axis=0), "hid", axis=0, tiled=False
    )
    group_seg = kv_rows[:, shard_rows, :shard_rows].reshape(-1).astype(jnp.int32)
    group_pos = seg_positions(group_seg)
    positions = lax.dynamic_slice_in_dim(group_pos, row_base, shard_rows)
    query_idx = row_base + jnp.arange(shard_rows, dtype=jnp.int32)
    seg_start = query_idx - positions
    unit_rows = lax.all_gather(
        jnp.concatenate([w_gate, w_up, w_down], axis=1), "hid", axis=0, tiled=True
    )
    width = w_gate.shape[1]
    gate_rows = unit_rows[:, :width]
    up_rows = unit_rows[:, width : 2 * width]
    down_rows = unit_rows[:, 2 * width :]
    queries = rotate(rms_scale(q_raw, q_gain), positions).astype(jnp.bfloat16)
    key_heads = rotate(k_normed, positions).astype(jnp.bfloat16).reshape(shard_rows, KVH * HD)
    kv_cache = jnp.concatenate([key_heads, values], axis=1)
    hid_count = kv_rows.shape[0]
    pair = LANES // HD
    pairs = KVH // pair
    q5 = queries.reshape(shard_rows, pairs, pair, groups, HD).transpose(1, 2, 3, 0, 4)
    q5 = q5.reshape(pairs, pair, groups * shard_rows, 1, HD)
    slot = (jnp.arange(pair)[:, None] == jnp.arange(pair)[None, :]) * SCORE_SCALE
    slot = slot.astype(jnp.bfloat16)
    q_pad = (q5 * slot[None, :, None, :, None]).reshape(pairs, pair, groups * shard_rows, LANES)
    key_pos = group_pos.reshape(hid_count, shard_rows)
    cos_rows, sin_rows = rotation_tables(key_pos, HD)
    q_rows = jnp.tile(query_idx, groups).reshape(groups * shard_rows, 1)
    starts = jnp.tile(seg_start, groups).reshape(groups * shard_rows, 1)
    bounds = jnp.stack(
        [jnp.min(seg_start), row_base + shard_rows - 1, row_base, jnp.max(seg_start)]
    )
    attn_pairs = flash_attention(
        q_pad, kv_rows, shard_rows, cos_rows, sin_rows, swap_matrix(LANES), q_rows, starts, bounds
    )
    attended = (
        attn_pairs.reshape(pairs, groups, shard_rows, pair, HD)
        .transpose(2, 0, 3, 1, 4)
        .reshape(shard_rows, H * HD)
    )
    after_attn = (resid + jnp.dot(attended, w_out, preferred_element_type=jnp.float32)).astype(
        jnp.bfloat16
    )
    after_f32 = lax.optimization_barrier(after_attn).astype(jnp.float32)
    mlp_in = rms_scale(after_f32, ffn_gain).astype(jnp.bfloat16)
    gathered = lax.all_gather(mlp_in, "req", axis=0, tiled=True)
    unit_sum = unit_terms(
        (gate_rows, up_rows, down_rows),
        gathered,
    )
    own_share = lax.psum_scatter(
        unit_sum.astype(jnp.bfloat16), "req", scatter_dimension=0, tiled=True
    ).astype(jnp.float32)
    mixed = (after_f32 + own_share).astype(jnp.bfloat16)
    return (mixed, kv_cache)


def solution(mesh):
    placed = (
        P(("req", "hid"), None),
        P(("req", "hid")),
        P(),
        P(),
        P(),
        P(),
        P(),
        P(),
        P(),
        P(),
        P(("req", "hid"), None),
        P(("req", "hid"), None),
        P(("req", "hid"), None),
    )
    return jax.shard_map(
        per_device,
        mesh=mesh,
        in_specs=placed,
        out_specs=(P(("req", "hid"), None), P(("req", "hid"), None)),
        check_vma=False,
    )
```

```python
import jax
import jax.numpy as jnp
from jax import lax
from jax.experimental import pallas as pl
from jax.experimental.pallas import tpu as pltpu
from jax.sharding import PartitionSpec as P

H = 24
KVH = 8
HD = 64


EPSILON = 1e-05
ROPE_BASE = 1000000.0
NEG_FILL = -1e30
SCORE_SCALE = 0.125


def rms_scale(values, gain):
    mean_sq = jnp.mean(values * values, axis=-1, keepdims=True)
    return values * lax.rsqrt(mean_sq + EPSILON) * gain


def seg_positions(seg_ids):
    indices = jnp.arange(seg_ids.shape[0], dtype=jnp.int32)
    is_first = jnp.concatenate([jnp.ones((1,), bool), seg_ids[1:] != seg_ids[:-1]])
    seg_begin = lax.cummax(jnp.where(is_first, indices, jnp.zeros_like(indices)), axis=0)
    return indices - seg_begin


def rotate(heads, positions):
    half_dim = heads.shape[-1] // 2
    inv_freq = ROPE_BASE ** (-(jnp.arange(half_dim, dtype=jnp.float32) * 2.0) / (2.0 * half_dim))
    angles = positions.astype(jnp.float32)[:, None] * inv_freq[None, :]
    cos_val = jnp.cos(angles)[:, None, :]
    sin_val = jnp.sin(angles)[:, None, :]
    left = heads[..., :half_dim]
    right = heads[..., half_dim:]
    return jnp.concatenate(
        [left * cos_val - right * sin_val, right * cos_val + left * sin_val], axis=-1
    )


SHARDS_PER_TILE = 8
LANES = 128


def flash_kernel(
    bounds_ref, q_ref, k_ref, v_ref, cos_ref, sin_ref, swap_ref, qi_ref, ss_ref, o_ref,
    m_sc, l_sc, acc_sc,
):
    kb = pl.program_id(1)
    pair = q_ref.shape[1]
    tile = k_ref.shape[0] * k_ref.shape[1]
    k_start = kb * tile

    @pl.when(kb == 0)
    def _():
        m_sc[...] = jnp.full(m_sc.shape, 0.5 * NEG_FILL, jnp.float32)
        l_sc[...] = jnp.zeros(l_sc.shape, jnp.float32)
        acc_sc[...] = jnp.zeros(acc_sc.shape, jnp.float32)

    needed = (k_start <= bounds_ref[1]) & (k_start + tile > bounds_ref[0])
    open_tile = (k_start + tile - 1 <= bounds_ref[2]) & (k_start >= bounds_ref[3])

    def rotated_keys():
        k_raw = k_ref[...].reshape(tile, LANES)
        swapped = jnp.dot(k_raw, swap_ref[...], preferred_element_type=jnp.float32)
        return (
            k_raw.astype(jnp.float32) * cos_ref[...].reshape(tile, LANES)
            + swapped * sin_ref[...].reshape(tile, LANES)
        ).astype(jnp.bfloat16)

    def update(a, k_rot, v_blk, allowed):
        scores = lax.dot_general(
            q_ref[0, a], k_rot, (((1,), (1,)), ((), ())), preferred_element_type=jnp.float32
        )
        if allowed is not None:
            scores = jnp.where(allowed, scores, NEG_FILL)
        m_prev = m_sc[a]
        m_new = jnp.maximum(m_prev, jnp.max(scores, axis=1, keepdims=True))
        weights = jnp.exp(scores - m_new)
        factor = jnp.exp(m_prev - m_new)
        width = LANES // pair
        lane = lax.broadcasted_iota(jnp.int32, v_blk.shape, 1)
        v_ext = jnp.where(lane // width == a, v_blk, jnp.ones_like(v_blk))
        prod = jnp.dot(weights.astype(jnp.bfloat16), v_ext, preferred_element_type=jnp.float32)
        other = (1 - a) * width
        l_sc[a] = l_sc[a] * factor + prod[:, other : other + 1]
        acc_sc[a] = acc_sc[a] * factor + prod
        m_sc[a] = m_new

    @pl.when(needed & open_tile)
    def _():
        k_rot = rotated_keys()
        v_blk = v_ref[...].reshape(tile, LANES)
        for a in range(pair):
            update(a, k_rot, v_blk, None)

    @pl.when(needed & jnp.logical_not(open_tile))
    def _():
        k_rot = rotated_keys()
        v_blk = v_ref[...].reshape(tile, LANES)
        key_idx = k_start + lax.broadcasted_iota(jnp.int32, (q_ref.shape[2], tile), 1)
        allowed = (key_idx <= qi_ref[...]) & (key_idx >= ss_ref[...])
        for a in range(pair):
            update(a, k_rot, v_blk, allowed)

    @pl.when(kb == pl.num_programs(1) - 1)
    def _():
        width = LANES // pair
        lane = lax.broadcasted_iota(jnp.int32, acc_sc.shape[1:], 1)
        out = jnp.zeros(acc_sc.shape[1:], jnp.float32)
        for a in range(pair):
            out = jnp.where(lane // width == a, acc_sc[a] / l_sc[a], out)
        o_ref[0] = out.astype(o_ref.dtype)


def flash_attention(q_pad, kv_rows, shard_len, cos_rows, sin_rows, swap, q_rows, starts, bounds):
    pairs, pair, rows, _ = q_pad.shape
    shards, _, width = kv_rows.shape
    tile = SHARDS_PER_TILE * shard_len
    blocks = shards // SHARDS_PER_TILE
    v_col = width // (2 * LANES)

    def clamp(kb, b_ref):
        first = b_ref[0] // tile
        last = b_ref[1] // tile
        return jnp.minimum(jnp.maximum(kb, first), last)

    grid_spec = pltpu.PrefetchScalarGridSpec(
        num_scalar_prefetch=1,
        grid=(pairs, blocks),
        in_specs=[
            pl.BlockSpec((1, pair, rows, LANES), lambda p, kb, b_ref: (p, 0, 0, 0)),
            pl.BlockSpec(
                (SHARDS_PER_TILE, shard_len, LANES),
                lambda p, kb, b_ref: (clamp(kb, b_ref), 0, p),
            ),
            pl.BlockSpec(
                (SHARDS_PER_TILE, shard_len, LANES),
                lambda p, kb, b_ref: (clamp(kb, b_ref), 0, v_col + p),
            ),
            pl.BlockSpec(
                (SHARDS_PER_TILE, shard_len, LANES),
                lambda p, kb, b_ref: (clamp(kb, b_ref), 0, 0),
            ),
            pl.BlockSpec(
                (SHARDS_PER_TILE, shard_len, LANES),
                lambda p, kb, b_ref: (clamp(kb, b_ref), 0, 0),
            ),
            pl.BlockSpec((LANES, LANES), lambda p, kb, b_ref: (0, 0)),
            pl.BlockSpec((rows, 1), lambda p, kb, b_ref: (0, 0)),
            pl.BlockSpec((rows, 1), lambda p, kb, b_ref: (0, 0)),
        ],
        out_specs=pl.BlockSpec((1, rows, LANES), lambda p, kb, b_ref: (p, 0, 0)),
        scratch_shapes=[
            pltpu.VMEM((pair, rows, 1), jnp.float32),
            pltpu.VMEM((pair, rows, 1), jnp.float32),
            pltpu.VMEM((pair, rows, LANES), jnp.float32),
        ],
    )
    return pl.pallas_call(
        flash_kernel,
        out_shape=jax.ShapeDtypeStruct((pairs, rows, LANES), jnp.bfloat16),
        grid_spec=grid_spec,
    )(bounds, q_pad, kv_rows, kv_rows, cos_rows, sin_rows, swap, q_rows, starts)


def rotation_tables(positions, width):
    half_dim = HD // 2
    inv_freq = ROPE_BASE ** (-(jnp.arange(half_dim, dtype=jnp.float32) * 2.0) / (2.0 * half_dim))
    angles = positions.astype(jnp.float32)[..., None] * jnp.tile(inv_freq, width // half_dim)
    return jnp.cos(angles), jnp.sin(angles)


def swap_matrix(width):
    src = jnp.arange(width)[:, None]
    dst = jnp.arange(width)[None, :]
    half_dim = HD // 2
    first = (dst % HD) < half_dim
    neg = first & (src == dst + half_dim)
    pos = (~first) & (src == dst - half_dim)
    return (pos.astype(jnp.float32) - neg.astype(jnp.float32)).astype(jnp.bfloat16)


def unit_terms(pieces, gathered):
    gate_part, up_part, down_part = pieces
    contract = (((1,), (1,)), ((), ()))
    gate_act = lax.dot_general(gathered, gate_part, contract, preferred_element_type=jnp.float32)
    up_act = lax.dot_general(gathered, up_part, contract, preferred_element_type=jnp.float32)
    hidden = lax.optimization_barrier((jax.nn.silu(gate_act) * up_act).astype(jnp.bfloat16))
    return jnp.dot(hidden, down_part, preferred_element_type=jnp.float32)


def per_device(
    tokens,
    segment,
    attn_gain,
    w_query,
    w_key,
    w_value,
    q_gain,
    k_gain,
    w_out,
    ffn_gain,
    w_gate,
    w_up,
    w_down,
):
    shard_rows = tokens.shape[0]
    groups = H // KVH
    row_base = lax.axis_index("hid") * shard_rows
    resid = tokens.astype(jnp.float32)
    normed = rms_scale(resid, attn_gain).astype(jnp.bfloat16)
    q_raw = jnp.dot(normed, w_query, preferred_element_type=jnp.float32).reshape(shard_rows, H, HD)
    k_raw = jnp.dot(normed, w_key, preferred_element_type=jnp.float32).reshape(shard_rows, KVH, HD)
    k_normed = rms_scale(k_raw, k_gain)
    values = jnp.dot(normed, w_value, preferred_element_type=jnp.float32).astype(jnp.bfloat16)
    send = jnp.concatenate(
        [k_normed.astype(jnp.bfloat16).reshape(shard_rows, KVH * HD), values], axis=1
    )
    seg_row = jnp.zeros((1, send.shape[1]), jnp.bfloat16)
    seg_row = lax.dynamic_update_slice(seg_row, segment.astype(jnp.bfloat16)[None], (0, 0))
    kv_rows = lax.all_gather(
        jnp.concatenate([send, seg_row], axis=0), "hid", axis=0, tiled=False
    )
    group_seg = kv_rows[:, shard_rows, :shard_rows].reshape(-1).astype(jnp.int32)
    group_pos = seg_positions(group_seg)
    positions = lax.dynamic_slice_in_dim(group_pos, row_base, shard_rows)
    query_idx = row_base + jnp.arange(shard_rows, dtype=jnp.int32)
    seg_start = query_idx - positions
    unit_rows = lax.all_gather(
        jnp.concatenate([w_gate, w_up, w_down], axis=1), "hid", axis=0, tiled=True
    )
    width = w_gate.shape[1]
    gate_rows = unit_rows[:, :width]
    up_rows = unit_rows[:, width : 2 * width]
    down_rows = unit_rows[:, 2 * width :]
    queries = rotate(rms_scale(q_raw, q_gain), positions).astype(jnp.bfloat16)
    hid_count = kv_rows.shape[0]
    pair = LANES // HD
    pairs = KVH // pair
    q5 = queries.reshape(shard_rows, pairs, pair, groups, HD).transpose(1, 2, 3, 0, 4)
    q5 = q5.reshape(pairs, pair, groups * shard_rows, 1, HD)
    slot = (jnp.arange(pair)[:, None] == jnp.arange(pair)[None, :]) * SCORE_SCALE
    slot = slot.astype(jnp.bfloat16)
    q_pad = (q5 * slot[None, :, None, :, None]).reshape(pairs, pair, groups * shard_rows, LANES)
    key_pos = group_pos.reshape(hid_count, shard_rows)
    cos_rows, sin_rows = rotation_tables(key_pos, LANES)
    q_rows = jnp.tile(query_idx, groups).reshape(groups * shard_rows, 1)
    starts = jnp.tile(seg_start, groups).reshape(groups * shard_rows, 1)
    bounds = jnp.stack(
        [jnp.min(seg_start), row_base + shard_rows - 1, row_base, jnp.max(seg_start)]
    )
    attn_pairs = flash_attention(
        q_pad, kv_rows, shard_rows, cos_rows, sin_rows, swap_matrix(LANES), q_rows, starts, bounds
    )
    attn_pairs, k_late, pos_late = lax.optimization_barrier((attn_pairs, k_normed, positions))
    key_heads = rotate(k_late, pos_late).astype(jnp.bfloat16).reshape(shard_rows, KVH * HD)
    kv_cache = jnp.concatenate([key_heads, values], axis=1)
    attended = (
        attn_pairs.reshape(pairs, groups, shard_rows, pair, HD)
        .transpose(2, 0, 3, 1, 4)
        .reshape(shard_rows, H * HD)
    )
    after_attn = (resid + jnp.dot(attended, w_out, preferred_element_type=jnp.float32)).astype(
        jnp.bfloat16
    )
    after_f32 = lax.optimization_barrier(after_attn).astype(jnp.float32)
    mlp_in = rms_scale(after_f32, ffn_gain).astype(jnp.bfloat16)
    gathered = lax.all_gather(mlp_in, "req", axis=0, tiled=True)
    unit_sum = unit_terms(
        (gate_rows, up_rows, down_rows),
        gathered,
    )
    own_share = lax.psum_scatter(
        unit_sum.astype(jnp.bfloat16), "req", scatter_dimension=0, tiled=True
    ).astype(jnp.float32)
    mixed = (after_f32 + own_share).astype(jnp.bfloat16)
    return (mixed, kv_cache)


def solution(mesh):
    placed = (
        P(("req", "hid"), None),
        P(("req", "hid")),
        P(),
        P(),
        P(),
        P(),
        P(),
        P(),
        P(),
        P(),
        P(("req", "hid"), None),
        P(("req", "hid"), None),
        P(("req", "hid"), None),
    )
    return jax.shard_map(
        per_device,
        mesh=mesh,
        in_specs=placed,
        out_specs=(P(("req", "hid"), None), P(("req", "hid"), None)),
        check_vma=False,
    )
```

```python
import jax
import jax.numpy as jnp
from jax import lax
from jax.experimental import pallas as pl
from jax.experimental.pallas import tpu as pltpu
from jax.sharding import PartitionSpec as P

H = 24
KVH = 8
HD = 64


EPSILON = 1e-05
ROPE_BASE = 1000000.0
NEG_FILL = -1e30
SCORE_SCALE = 0.125


def rms_scale(values, gain):
    mean_sq = jnp.mean(values * values, axis=-1, keepdims=True)
    return values * lax.rsqrt(mean_sq + EPSILON) * gain


def seg_positions(seg_ids):
    indices = jnp.arange(seg_ids.shape[0], dtype=jnp.int32)
    is_first = jnp.concatenate([jnp.ones((1,), bool), seg_ids[1:] != seg_ids[:-1]])
    seg_begin = lax.cummax(jnp.where(is_first, indices, jnp.zeros_like(indices)), axis=0)
    return indices - seg_begin


def rotate(heads, positions):
    half_dim = heads.shape[-1] // 2
    inv_freq = ROPE_BASE ** (-(jnp.arange(half_dim, dtype=jnp.float32) * 2.0) / (2.0 * half_dim))
    angles = positions.astype(jnp.float32)[:, None] * inv_freq[None, :]
    cos_val = jnp.cos(angles)[:, None, :]
    sin_val = jnp.sin(angles)[:, None, :]
    left = heads[..., :half_dim]
    right = heads[..., half_dim:]
    return jnp.concatenate(
        [left * cos_val - right * sin_val, right * cos_val + left * sin_val], axis=-1
    )


SHARDS_PER_TILE = 8
LANES = 128


def flash_kernel(
    bounds_ref, q_ref, k_ref, v_ref, cos_ref, sin_ref, swap_ref, qi_ref, ss_ref, o_ref,
    m_sc, l_sc, acc_sc,
):
    kb = pl.program_id(1)
    pair = q_ref.shape[1]
    tile = k_ref.shape[0] * k_ref.shape[1]
    k_start = kb * tile

    @pl.when(kb == 0)
    def _():
        m_sc[...] = jnp.full(m_sc.shape, 0.5 * NEG_FILL, jnp.float32)
        l_sc[...] = jnp.zeros(l_sc.shape, jnp.float32)
        acc_sc[...] = jnp.zeros(acc_sc.shape, jnp.float32)

    needed = (k_start <= bounds_ref[1]) & (k_start + tile > bounds_ref[0])
    open_tile = (k_start + tile - 1 <= bounds_ref[2]) & (k_start >= bounds_ref[3])

    def rotated_keys():
        k_raw = k_ref[...].reshape(tile, LANES)
        swapped = jnp.dot(k_raw, swap_ref[...], preferred_element_type=jnp.float32)
        return (
            k_raw.astype(jnp.float32) * cos_ref[...].reshape(tile, LANES)
            + swapped * sin_ref[...].reshape(tile, LANES)
        ).astype(jnp.bfloat16)

    def update(a, k_rot, v_blk, allowed):
        scores = lax.dot_general(
            q_ref[0, a], k_rot, (((1,), (1,)), ((), ())), preferred_element_type=jnp.float32
        )
        if allowed is not None:
            scores = jnp.where(allowed, scores, NEG_FILL)
        m_prev = m_sc[a]
        m_new = jnp.maximum(m_prev, jnp.max(scores, axis=1, keepdims=True))
        weights = jnp.exp(scores - m_new)
        factor = jnp.exp(m_prev - m_new)
        width = LANES // pair
        lane = lax.broadcasted_iota(jnp.int32, v_blk.shape, 1)
        v_ext = jnp.where(lane // width == a, v_blk, jnp.ones_like(v_blk))
        prod = jnp.dot(weights.astype(jnp.bfloat16), v_ext, preferred_element_type=jnp.float32)
        other = (1 - a) * width
        l_sc[a] = l_sc[a] * factor + prod[:, other : other + 1]
        acc_sc[a] = acc_sc[a] * factor + prod
        m_sc[a] = m_new

    @pl.when(needed & open_tile)
    def _():
        k_rot = rotated_keys()
        v_blk = v_ref[...].reshape(tile, LANES)
        for a in range(pair):
            update(a, k_rot, v_blk, None)

    @pl.when(needed & jnp.logical_not(open_tile))
    def _():
        k_rot = rotated_keys()
        v_blk = v_ref[...].reshape(tile, LANES)
        key_idx = k_start + lax.broadcasted_iota(jnp.int32, (q_ref.shape[2], tile), 1)
        starts = ss_ref[...]
        span = (qi_ref[...] - starts).astype(jnp.uint32)
        allowed = (key_idx - starts).astype(jnp.uint32) <= span
        for a in range(pair):
            update(a, k_rot, v_blk, allowed)

    @pl.when(kb == pl.num_programs(1) - 1)
    def _():
        width = LANES // pair
        lane = lax.broadcasted_iota(jnp.int32, acc_sc.shape[1:], 1)
        out = jnp.zeros(acc_sc.shape[1:], jnp.float32)
        for a in range(pair):
            out = jnp.where(lane // width == a, acc_sc[a] / l_sc[a], out)
        o_ref[0] = out.astype(o_ref.dtype)


def flash_attention(q_pad, kv_rows, shard_len, cos_rows, sin_rows, swap, q_rows, starts, bounds):
    pairs, pair, rows, _ = q_pad.shape
    shards, _, width = kv_rows.shape
    tile = SHARDS_PER_TILE * shard_len
    blocks = shards // SHARDS_PER_TILE
    v_col = width // (2 * LANES)

    def clamp(kb, b_ref):
        first = b_ref[0] // tile
        last = b_ref[1] // tile
        return jnp.minimum(jnp.maximum(kb, first), last)

    grid_spec = pltpu.PrefetchScalarGridSpec(
        num_scalar_prefetch=1,
        grid=(pairs, blocks),
        in_specs=[
            pl.BlockSpec((1, pair, rows, LANES), lambda p, kb, b_ref: (p, 0, 0, 0)),
            pl.BlockSpec(
                (SHARDS_PER_TILE, shard_len, LANES),
                lambda p, kb, b_ref: (clamp(kb, b_ref), 0, p),
            ),
            pl.BlockSpec(
                (SHARDS_PER_TILE, shard_len, LANES),
                lambda p, kb, b_ref: (clamp(kb, b_ref), 0, v_col + p),
            ),
            pl.BlockSpec(
                (SHARDS_PER_TILE, shard_len, LANES),
                lambda p, kb, b_ref: (clamp(kb, b_ref), 0, 0),
            ),
            pl.BlockSpec(
                (SHARDS_PER_TILE, shard_len, LANES),
                lambda p, kb, b_ref: (clamp(kb, b_ref), 0, 0),
            ),
            pl.BlockSpec((LANES, LANES), lambda p, kb, b_ref: (0, 0)),
            pl.BlockSpec((rows, 1), lambda p, kb, b_ref: (0, 0)),
            pl.BlockSpec((rows, 1), lambda p, kb, b_ref: (0, 0)),
        ],
        out_specs=pl.BlockSpec((1, rows, LANES), lambda p, kb, b_ref: (p, 0, 0)),
        scratch_shapes=[
            pltpu.VMEM((pair, rows, 1), jnp.float32),
            pltpu.VMEM((pair, rows, 1), jnp.float32),
            pltpu.VMEM((pair, rows, LANES), jnp.float32),
        ],
    )
    return pl.pallas_call(
        flash_kernel,
        out_shape=jax.ShapeDtypeStruct((pairs, rows, LANES), jnp.bfloat16),
        grid_spec=grid_spec,
    )(bounds, q_pad, kv_rows, kv_rows, cos_rows, sin_rows, swap, q_rows, starts)


def rotation_tables(positions, width):
    half_dim = HD // 2
    inv_freq = ROPE_BASE ** (-(jnp.arange(half_dim, dtype=jnp.float32) * 2.0) / (2.0 * half_dim))
    angles = positions.astype(jnp.float32)[..., None] * jnp.tile(inv_freq, width // half_dim)
    return jnp.cos(angles), jnp.sin(angles)


def swap_matrix(width):
    src = jnp.arange(width)[:, None]
    dst = jnp.arange(width)[None, :]
    half_dim = HD // 2
    first = (dst % HD) < half_dim
    neg = first & (src == dst + half_dim)
    pos = (~first) & (src == dst - half_dim)
    return (pos.astype(jnp.float32) - neg.astype(jnp.float32)).astype(jnp.bfloat16)


def unit_terms(pieces, gathered):
    gate_part, up_part, down_part = pieces
    contract = (((1,), (1,)), ((), ()))
    gate_act = lax.dot_general(gathered, gate_part, contract, preferred_element_type=jnp.float32)
    up_act = lax.dot_general(gathered, up_part, contract, preferred_element_type=jnp.float32)
    hidden = lax.optimization_barrier((jax.nn.silu(gate_act) * up_act).astype(jnp.bfloat16))
    return jnp.dot(hidden, down_part, preferred_element_type=jnp.float32)


def per_device(
    tokens,
    segment,
    attn_gain,
    w_query,
    w_key,
    w_value,
    q_gain,
    k_gain,
    w_out,
    ffn_gain,
    w_gate,
    w_up,
    w_down,
):
    shard_rows = tokens.shape[0]
    groups = H // KVH
    row_base = lax.axis_index("hid") * shard_rows
    resid = tokens.astype(jnp.float32)
    normed = rms_scale(resid, attn_gain).astype(jnp.bfloat16)
    q_raw = jnp.dot(normed, w_query, preferred_element_type=jnp.float32).reshape(shard_rows, H, HD)
    k_raw = jnp.dot(normed, w_key, preferred_element_type=jnp.float32).reshape(shard_rows, KVH, HD)
    k_normed = rms_scale(k_raw, k_gain)
    values = jnp.dot(normed, w_value, preferred_element_type=jnp.float32).astype(jnp.bfloat16)
    send = jnp.concatenate(
        [k_normed.astype(jnp.bfloat16).reshape(shard_rows, KVH * HD), values], axis=1
    )
    seg_row = jnp.zeros((1, send.shape[1]), jnp.bfloat16)
    seg_row = lax.dynamic_update_slice(seg_row, segment.astype(jnp.bfloat16)[None], (0, 0))
    kv_rows = lax.all_gather(
        jnp.concatenate([send, seg_row], axis=0), "hid", axis=0, tiled=False
    )
    group_seg = kv_rows[:, shard_rows, :shard_rows].reshape(-1).astype(jnp.int32)
    group_pos = seg_positions(group_seg)
    positions = lax.dynamic_slice_in_dim(group_pos, row_base, shard_rows)
    query_idx = row_base + jnp.arange(shard_rows, dtype=jnp.int32)
    seg_start = query_idx - positions
    unit_rows = lax.all_gather(
        jnp.concatenate([w_gate, w_up, w_down], axis=1), "hid", axis=0, tiled=True
    )
    width = w_gate.shape[1]
    gate_rows = unit_rows[:, :width]
    up_rows = unit_rows[:, width : 2 * width]
    down_rows = unit_rows[:, 2 * width :]
    queries = rotate(rms_scale(q_raw, q_gain), positions).astype(jnp.bfloat16)
    hid_count = kv_rows.shape[0]
    pair = LANES // HD
    pairs = KVH // pair
    q5 = queries.reshape(shard_rows, pairs, pair, groups, HD).transpose(1, 2, 3, 0, 4)
    q5 = q5.reshape(pairs, pair, groups * shard_rows, 1, HD)
    slot = (jnp.arange(pair)[:, None] == jnp.arange(pair)[None, :]) * SCORE_SCALE
    slot = slot.astype(jnp.bfloat16)
    q_pad = (q5 * slot[None, :, None, :, None]).reshape(pairs, pair, groups * shard_rows, LANES)
    key_pos = group_pos.reshape(hid_count, shard_rows)
    cos_rows, sin_rows = rotation_tables(key_pos, LANES)
    q_rows = jnp.tile(query_idx, groups).reshape(groups * shard_rows, 1)
    starts = jnp.tile(seg_start, groups).reshape(groups * shard_rows, 1)
    bounds = jnp.stack(
        [jnp.min(seg_start), row_base + shard_rows - 1, row_base, jnp.max(seg_start)]
    )
    attn_pairs = flash_attention(
        q_pad, kv_rows, shard_rows, cos_rows, sin_rows, swap_matrix(LANES), q_rows, starts, bounds
    )
    attn_pairs, k_late, pos_late = lax.optimization_barrier((attn_pairs, k_normed, positions))
    key_heads = rotate(k_late, pos_late).astype(jnp.bfloat16).reshape(shard_rows, KVH * HD)
    kv_cache = jnp.concatenate([key_heads, values], axis=1)
    attended = (
        attn_pairs.reshape(pairs, groups, shard_rows, pair, HD)
        .transpose(2, 0, 3, 1, 4)
        .reshape(shard_rows, H * HD)
    )
    after_attn = (resid + jnp.dot(attended, w_out, preferred_element_type=jnp.float32)).astype(
        jnp.bfloat16
    )
    after_f32 = lax.optimization_barrier(after_attn).astype(jnp.float32)
    mlp_in = rms_scale(after_f32, ffn_gain).astype(jnp.bfloat16)
    gathered = lax.all_gather(mlp_in, "req", axis=0, tiled=True)
    unit_sum = unit_terms(
        (gate_rows, up_rows, down_rows),
        gathered,
    )
    own_share = lax.psum_scatter(
        unit_sum.astype(jnp.bfloat16), "req", scatter_dimension=0, tiled=True
    ).astype(jnp.float32)
    mixed = (after_f32 + own_share).astype(jnp.bfloat16)
    return (mixed, kv_cache)


def solution(mesh):
    placed = (
        P(("req", "hid"), None),
        P(("req", "hid")),
        P(),
        P(),
        P(),
        P(),
        P(),
        P(),
        P(),
        P(),
        P(("req", "hid"), None),
        P(("req", "hid"), None),
        P(("req", "hid"), None),
    )
    return jax.shard_map(
        per_device,
        mesh=mesh,
        in_specs=placed,
        out_specs=(P(("req", "hid"), None), P(("req", "hid"), None)),
        check_vma=False,
    )
```

```python
import jax
import jax.numpy as jnp
from jax import lax
from jax.experimental import pallas as pl
from jax.experimental.pallas import tpu as pltpu
from jax.sharding import PartitionSpec as P

H = 24
KVH = 8
HD = 64


EPSILON = 1e-05
ROPE_BASE = 1000000.0
NEG_FILL = -1e30
SCORE_SCALE = 0.125


def rms_scale(values, gain):
    mean_sq = jnp.mean(values * values, axis=-1, keepdims=True)
    return values * lax.rsqrt(mean_sq + EPSILON) * gain


def seg_positions(seg_ids):
    indices = jnp.arange(seg_ids.shape[0], dtype=jnp.int32)
    is_first = jnp.concatenate([jnp.ones((1,), bool), seg_ids[1:] != seg_ids[:-1]])
    seg_begin = lax.cummax(jnp.where(is_first, indices, jnp.zeros_like(indices)), axis=0)
    return indices - seg_begin


def rotate(heads, positions):
    half_dim = heads.shape[-1] // 2
    inv_freq = ROPE_BASE ** (-(jnp.arange(half_dim, dtype=jnp.float32) * 2.0) / (2.0 * half_dim))
    angles = positions.astype(jnp.float32)[:, None] * inv_freq[None, :]
    cos_val = jnp.cos(angles)[:, None, :]
    sin_val = jnp.sin(angles)[:, None, :]
    left = heads[..., :half_dim]
    right = heads[..., half_dim:]
    return jnp.concatenate(
        [left * cos_val - right * sin_val, right * cos_val + left * sin_val], axis=-1
    )


SHARDS_PER_TILE = 8
LANES = 128


def flash_kernel(
    bounds_ref, q_ref, k_ref, v_ref, cos_ref, sin_ref, swap_ref, qi_ref, ss_ref, o_ref,
    m_sc, l_sc, acc_sc,
):
    kb = pl.program_id(1)
    pair = q_ref.shape[1]
    tile = k_ref.shape[0] * k_ref.shape[1]
    k_start = kb * tile

    @pl.when(kb == 0)
    def _():
        m_sc[...] = jnp.full(m_sc.shape, 0.5 * NEG_FILL, jnp.float32)
        l_sc[...] = jnp.zeros(l_sc.shape, jnp.float32)
        acc_sc[...] = jnp.zeros(acc_sc.shape, jnp.float32)

    needed = (k_start <= bounds_ref[1]) & (k_start + tile > bounds_ref[0])
    open_tile = (k_start + tile - 1 <= bounds_ref[2]) & (k_start >= bounds_ref[3])

    def rotated_keys():
        k_raw = k_ref[...].reshape(tile, LANES)
        swapped = jnp.dot(k_raw, swap_ref[...], preferred_element_type=jnp.float32)
        return (
            k_raw.astype(jnp.float32) * cos_ref[...].reshape(tile, LANES)
            + swapped * sin_ref[...].reshape(tile, LANES)
        ).astype(jnp.bfloat16)

    def update(a, k_rot, v_blk, allowed):
        scores = lax.dot_general(
            q_ref[0, a], k_rot, (((1,), (1,)), ((), ())), preferred_element_type=jnp.float32
        )
        if allowed is not None:
            scores = jnp.where(allowed, scores, NEG_FILL)
        m_prev = m_sc[a]
        m_new = jnp.maximum(m_prev, jnp.max(scores, axis=1, keepdims=True))
        weights = jnp.exp(scores - m_new)
        factor = jnp.exp(m_prev - m_new)
        width = LANES // pair
        lane = lax.broadcasted_iota(jnp.int32, v_blk.shape, 1)
        v_ext = jnp.where(lane // width == a, v_blk, jnp.ones_like(v_blk))
        prod = jnp.dot(weights.astype(jnp.bfloat16), v_ext, preferred_element_type=jnp.float32)
        other = (1 - a) * width
        l_sc[a] = l_sc[a] * factor + prod[:, other : other + 1]
        acc_sc[a] = acc_sc[a] * factor + prod
        m_sc[a] = m_new

    @pl.when(needed & open_tile)
    def _():
        k_rot = rotated_keys()
        v_blk = v_ref[...].reshape(tile, LANES)
        for a in range(pair):
            update(a, k_rot, v_blk, None)

    @pl.when(needed & jnp.logical_not(open_tile))
    def _():
        k_rot = rotated_keys()
        v_blk = v_ref[...].reshape(tile, LANES)
        key_idx = k_start + lax.broadcasted_iota(jnp.int32, (q_ref.shape[2], tile), 1)
        allowed = (key_idx <= qi_ref[...]) & (key_idx >= ss_ref[...])
        for a in range(pair):
            update(a, k_rot, v_blk, allowed)

    @pl.when(kb == pl.num_programs(1) - 1)
    def _():
        width = LANES // pair
        lane = lax.broadcasted_iota(jnp.int32, acc_sc.shape[1:], 1)
        out = jnp.zeros(acc_sc.shape[1:], jnp.float32)
        for a in range(pair):
            out = jnp.where(lane // width == a, acc_sc[a] / l_sc[a], out)
        o_ref[0] = out.astype(o_ref.dtype)


def flash_attention(q_pad, kv_rows, shard_len, cos_rows, sin_rows, swap, q_rows, starts, bounds):
    pairs, pair, rows, _ = q_pad.shape
    shards, _, width = kv_rows.shape
    tile = SHARDS_PER_TILE * shard_len
    blocks = shards // SHARDS_PER_TILE
    v_col = width // (2 * LANES)

    def clamp(kb, b_ref):
        first = b_ref[0] // tile
        last = b_ref[1] // tile
        return jnp.minimum(jnp.maximum(kb, first), last)

    grid_spec = pltpu.PrefetchScalarGridSpec(
        num_scalar_prefetch=1,
        grid=(pairs, blocks),
        in_specs=[
            pl.BlockSpec((1, pair, rows, LANES), lambda p, kb, b_ref: (p, 0, 0, 0)),
            pl.BlockSpec(
                (SHARDS_PER_TILE, shard_len, LANES),
                lambda p, kb, b_ref: (clamp(kb, b_ref), 0, p),
            ),
            pl.BlockSpec(
                (SHARDS_PER_TILE, shard_len, LANES),
                lambda p, kb, b_ref: (clamp(kb, b_ref), 0, v_col + p),
            ),
            pl.BlockSpec(
                (SHARDS_PER_TILE, shard_len, LANES),
                lambda p, kb, b_ref: (clamp(kb, b_ref), 0, 0),
            ),
            pl.BlockSpec(
                (SHARDS_PER_TILE, shard_len, LANES),
                lambda p, kb, b_ref: (clamp(kb, b_ref), 0, 0),
            ),
            pl.BlockSpec((LANES, LANES), lambda p, kb, b_ref: (0, 0)),
            pl.BlockSpec((rows, 1), lambda p, kb, b_ref: (0, 0)),
            pl.BlockSpec((rows, 1), lambda p, kb, b_ref: (0, 0)),
        ],
        out_specs=pl.BlockSpec((1, rows, LANES), lambda p, kb, b_ref: (p, 0, 0)),
        scratch_shapes=[
            pltpu.VMEM((pair, rows, 1), jnp.float32),
            pltpu.VMEM((pair, rows, 1), jnp.float32),
            pltpu.VMEM((pair, rows, LANES), jnp.float32),
        ],
    )
    return pl.pallas_call(
        flash_kernel,
        out_shape=jax.ShapeDtypeStruct((pairs, rows, LANES), jnp.bfloat16),
        grid_spec=grid_spec,
    )(bounds, q_pad, kv_rows, kv_rows, cos_rows, sin_rows, swap, q_rows, starts)


def rotation_tables(positions, width):
    half_dim = HD // 2
    inv_freq = ROPE_BASE ** (-(jnp.arange(half_dim, dtype=jnp.float32) * 2.0) / (2.0 * half_dim))
    angles = positions.astype(jnp.float32)[..., None] * jnp.tile(inv_freq, width // half_dim)
    return jnp.cos(angles), jnp.sin(angles)


def swap_matrix(width):
    src = jnp.arange(width)[:, None]
    dst = jnp.arange(width)[None, :]
    half_dim = HD // 2
    first = (dst % HD) < half_dim
    neg = first & (src == dst + half_dim)
    pos = (~first) & (src == dst - half_dim)
    return (pos.astype(jnp.float32) - neg.astype(jnp.float32)).astype(jnp.bfloat16)


def unit_terms(pieces, gathered):
    gate_part, up_part, down_part = pieces
    gate_act = jnp.einsum("tc,hnc->thn", gathered, gate_part, preferred_element_type=jnp.float32)
    up_act = jnp.einsum("tc,hnc->thn", gathered, up_part, preferred_element_type=jnp.float32)
    hidden = lax.optimization_barrier((jax.nn.silu(gate_act) * up_act).astype(jnp.bfloat16))
    return jnp.einsum("thn,hnc->tc", hidden, down_part, preferred_element_type=jnp.float32)


def per_device(
    tokens,
    segment,
    attn_gain,
    w_query,
    w_key,
    w_value,
    q_gain,
    k_gain,
    w_out,
    ffn_gain,
    w_gate,
    w_up,
    w_down,
):
    shard_rows = tokens.shape[0]
    groups = H // KVH
    row_base = lax.axis_index("hid") * shard_rows
    resid = tokens.astype(jnp.float32)
    normed = rms_scale(resid, attn_gain).astype(jnp.bfloat16)
    q_raw = jnp.dot(normed, w_query, preferred_element_type=jnp.float32).reshape(shard_rows, H, HD)
    k_raw = jnp.dot(normed, w_key, preferred_element_type=jnp.float32).reshape(shard_rows, KVH, HD)
    k_normed = rms_scale(k_raw, k_gain)
    values = jnp.dot(normed, w_value, preferred_element_type=jnp.float32).astype(jnp.bfloat16)
    send = jnp.concatenate(
        [k_normed.astype(jnp.bfloat16).reshape(shard_rows, KVH * HD), values], axis=1
    )
    seg_row = jnp.zeros((1, send.shape[1]), jnp.bfloat16)
    seg_row = lax.dynamic_update_slice(seg_row, segment.astype(jnp.bfloat16)[None], (0, 0))
    kv_rows = lax.all_gather(
        jnp.concatenate([send, seg_row], axis=0), "hid", axis=0, tiled=False
    )
    group_seg = kv_rows[:, shard_rows, :shard_rows].reshape(-1).astype(jnp.int32)
    group_pos = seg_positions(group_seg)
    positions = lax.dynamic_slice_in_dim(group_pos, row_base, shard_rows)
    query_idx = row_base + jnp.arange(shard_rows, dtype=jnp.int32)
    seg_start = query_idx - positions
    unit_rows = lax.all_gather(
        jnp.concatenate([w_gate, w_up, w_down], axis=0), "hid", axis=0, tiled=False
    )
    count = w_gate.shape[0]
    gate_rows = unit_rows[:, :count]
    up_rows = unit_rows[:, count : 2 * count]
    down_rows = unit_rows[:, 2 * count :]
    queries = rotate(rms_scale(q_raw, q_gain), positions).astype(jnp.bfloat16)
    hid_count = kv_rows.shape[0]
    pair = LANES // HD
    pairs = KVH // pair
    q5 = queries.reshape(shard_rows, pairs, pair, groups, HD).transpose(1, 2, 3, 0, 4)
    q5 = q5.reshape(pairs, pair, groups * shard_rows, 1, HD)
    slot = (jnp.arange(pair)[:, None] == jnp.arange(pair)[None, :]) * SCORE_SCALE
    slot = slot.astype(jnp.bfloat16)
    q_pad = (q5 * slot[None, :, None, :, None]).reshape(pairs, pair, groups * shard_rows, LANES)
    key_pos = group_pos.reshape(hid_count, shard_rows)
    cos_rows, sin_rows = rotation_tables(key_pos, LANES)
    q_rows = jnp.tile(query_idx, groups).reshape(groups * shard_rows, 1)
    starts = jnp.tile(seg_start, groups).reshape(groups * shard_rows, 1)
    bounds = jnp.stack(
        [jnp.min(seg_start), row_base + shard_rows - 1, row_base, jnp.max(seg_start)]
    )
    attn_pairs = flash_attention(
        q_pad, kv_rows, shard_rows, cos_rows, sin_rows, swap_matrix(LANES), q_rows, starts, bounds
    )
    attn_pairs, k_late, pos_late = lax.optimization_barrier((attn_pairs, k_normed, positions))
    key_heads = rotate(k_late, pos_late).astype(jnp.bfloat16).reshape(shard_rows, KVH * HD)
    kv_cache = jnp.concatenate([key_heads, values], axis=1)
    attended = (
        attn_pairs.reshape(pairs, groups, shard_rows, pair, HD)
        .transpose(2, 0, 3, 1, 4)
        .reshape(shard_rows, H * HD)
    )
    after_attn = (resid + jnp.dot(attended, w_out, preferred_element_type=jnp.float32)).astype(
        jnp.bfloat16
    )
    after_f32 = lax.optimization_barrier(after_attn).astype(jnp.float32)
    mlp_in = rms_scale(after_f32, ffn_gain).astype(jnp.bfloat16)
    gathered = lax.all_gather(mlp_in, "req", axis=0, tiled=True)
    unit_sum = unit_terms(
        (gate_rows, up_rows, down_rows),
        gathered,
    )
    own_share = lax.psum_scatter(
        unit_sum.astype(jnp.bfloat16), "req", scatter_dimension=0, tiled=True
    ).astype(jnp.float32)
    mixed = (after_f32 + own_share).astype(jnp.bfloat16)
    return (mixed, kv_cache)


def solution(mesh):
    placed = (
        P(("req", "hid"), None),
        P(("req", "hid")),
        P(),
        P(),
        P(),
        P(),
        P(),
        P(),
        P(),
        P(),
        P(("req", "hid"), None),
        P(("req", "hid"), None),
        P(("req", "hid"), None),
    )
    return jax.shard_map(
        per_device,
        mesh=mesh,
        in_specs=placed,
        out_specs=(P(("req", "hid"), None), P(("req", "hid"), None)),
        check_vma=False,
    )
```
